32 devices in a mesh: grid: 8 (over z, x), mem: 4 (over y, core).
Axes of the slice: x: 2, y: 2, z: 4, core: 2. Of those that a mesh axis runs over, the one named last changes fastest.
Arguments:
- members: bfloat16 [80, 4, 16, 512], P('mem', None, 'grid'), may hold values from -0.8984375 to 0.8984375
- innovation: float32 [4, 16, 512], P(None, 'grid'), may hold values from -6 to 6
- observed_count: int32 [16, 512], P('grid'), may hold values from 0 to 3
- obs_precision: float32 [4], replicated, may hold values from 0.5 to 4
Outputs:
- recentred: bfloat16 [80, 4, 16, 512], P('mem', None, 'grid')
- increment: float32 [4, 16, 512], P('mem', 'grid')
The draws below stay inside these ranges and needn't reach their ends.
All inputs are finite; a program needn't handle non-finite values.
Results may differ from the reference program's by a relative error of at most 0.0004.
Values may be sent and summed in bfloat16 or wider, within the bound.
No kernel may reach another device: no remote copies, remote signals or barrier semaphores. Data moves between devices by JAX's collectives and lax.ppermute only.
A program may use at most 64 MiB of HBM per device.

```python
import math
import jax
import jax.numpy as jnp
from jax import lax

MEMBERS = 80
NLON = 512
PASSES = 2
ITERS = 2
LEV = 4
NLAT = 16


def plant(values, own_key, least, high):
    spot = [jax.random.randint(jax.random.fold_in(own_key, axis), (), 0, length) for axis, length in enumerate(values.shape)]
    widest = values.shape.index(max(values.shape))
    beside = spot[:widest] + [(spot[widest] + 1) % values.shape[widest]] + spot[widest + 1:]
    return values.at[tuple(spot)].set(least).at[tuple(beside)].set(high)


def levels(own_key, shape, split, low, largest):
    gain = 1.0
    for position, parts in split:
        heights = jax.random.uniform(jax.random.fold_in(jax.random.fold_in(own_key, 6), position), (parts,), jnp.float32, low / len(split), largest / len(split))
        gain = gain * jnp.repeat(jnp.exp(heights), shape[position] // parts).reshape((-1,) + (1,) * (len(shape) - 1 - position))
    return gain


def scatter_about(stream_key, shape, spread, most, cuts=(), held_as=jnp.bfloat16):
    result = spread * jax.random.normal(stream_key, shape, jnp.float32)
    if cuts:
        result = result * levels(stream_key, shape, cuts, -0.22, 0.18)
    return jnp.clip(result, -most, most).astype(held_as)


def setup_inputs(seed: int = 0) -> dict:
    arg_keys = jax.random.split(jax.random.key(seed), 5)
    members = scatter_about(arg_keys[0], (MEMBERS, LEV, NLAT, NLON), 0.15, 0.8984375, ((0, 4), (2, 8)))
    innovation = scatter_about(arg_keys[1], (LEV, NLAT, NLON), 1.0, 6.0, ((1, 8),), jnp.float32)
    observed_count = plant(jax.random.randint(arg_keys[2], (NLAT, NLON), 0, 4), jax.random.fold_in(arg_keys[2], 1), 0, 3).astype(jnp.int32)
    obs_precision = jnp.clip(jnp.exp(jax.random.uniform(arg_keys[3], (LEV,), jnp.float32, math.log(0.5), math.log(4.0))), 0.5, 4.0)
    return dict(members=members, innovation=innovation, observed_count=observed_count, obs_precision=obs_precision)


diffusion = 0.25


def smooth(field):
    for sweep_index in range(PASSES):
        edge = jnp.zeros_like(field[..., :1, :])
        north = jnp.concatenate([edge, field[..., :-1, :]], axis=-2)
        south = jnp.concatenate([field[..., 1:, :], edge], axis=-2)
        field = field + diffusion * (north + south - 2.0 * field)
    for sweep_index in range(PASSES):
        field = field + diffusion * (jnp.roll(field, 1, -1) + jnp.roll(field, -1, -1) - 2.0 * field)
    return field


def level_hessian(inputs):
    level_members, level_weight, direction = inputs
    widened = level_members.astype(jnp.float32)
    smoothed = smooth(direction)
    total = jnp.sum(widened * smoothed, axis=0)
    back = smooth(widened * (level_weight * total)[None])
    return direction + back, smoothed


def level_gradient(inputs):
    level_members, level_weight, level_innovation = inputs
    return smooth(level_members.astype(jnp.float32) * (level_weight * level_innovation)[None])


def level_increment(inputs):
    level_members, carried = inputs
    return jnp.sum(level_members.astype(jnp.float32) * carried, axis=0)


def reference(members, innovation, observed_count, obs_precision):
    by_level = jnp.transpose(members, (1, 0, 2, 3))
    weight = observed_count.astype(jnp.float32)[None] * obs_precision[:, None, None]
    gradient = lax.map(level_gradient, (by_level, weight, innovation))
    residual = gradient
    direction = gradient
    carried = jnp.zeros_like(gradient)
    norm_now = jnp.sum(residual * residual)
    for iteration in range(ITERS):
        image, smoothed = lax.map(level_hessian, (by_level, weight, direction))
        step_size = norm_now / jnp.sum(direction * image)
        carried = carried + step_size * smoothed
        residual = residual - step_size * image
        if iteration + 1 < ITERS:
            norm_next = jnp.sum(residual * residual)
            direction = residual + (norm_next / norm_now) * direction
            norm_now = norm_next
    increment = lax.map(level_increment, (by_level, carried))
    recentred = (members.astype(jnp.float32) + increment[None]).astype(jnp.bfloat16)
    return (recentred, increment)
```

```python
import jax
import jax.numpy as jnp
from jax import lax
from jax.sharding import PartitionSpec as P

PASSES = 2
ITERS = 2


diffusion = 0.25


def padded(value, sides, width):
    for axis, dim in sides:
        devices, length = (lax.axis_size(axis), value.shape[dim])
        up = [(i, (i + 1) % devices) for i in range(devices - 1)]
        down = [(j, i) for i, j in up]
        last = lax.slice_in_dim(value, length - width, length, axis=dim)
        leading = lax.slice_in_dim(value, 0, width, axis=dim)
        before = lax.ppermute(last, axis, up)
        after = lax.ppermute(leading, axis, down)
        value = jnp.concatenate([before, value, after], axis=dim)
    return value


def smooth(field):
    for sweep_index in range(PASSES):
        extended = padded(field, (("grid", 2),), 1)
        centre = extended[:, :, 1:-1]
        field = centre + diffusion * (extended[:, :, :-2] + extended[:, :, 2:] - 2.0 * centre)
    for sweep_index in range(PASSES):
        field = field + diffusion * (jnp.roll(field, 1, 3) + jnp.roll(field, -1, 3) - 2.0 * field)
    return field


def member_total(product):
    summed = jnp.sum(product, axis=0)
    return summed


def norm_of(residual):
    return lax.psum(jnp.sum(residual * residual), ("grid", "mem"))


def local(members, innovation, observed_count, obs_precision):
    mem_index = lax.axis_index("mem")
    level_share = members.shape[1] // lax.axis_size("mem")
    perturbed = lax.all_to_all(members, "mem", split_axis=1, concat_axis=0, tiled=True)
    precision = lax.dynamic_slice_in_dim(obs_precision, mem_index * level_share, level_share, 0)
    local_innovation = lax.dynamic_slice_in_dim(innovation, mem_index * level_share, level_share, 0)
    weight = observed_count.astype(jnp.float32)[None] * precision[:, None, None]
    gradient = smooth(perturbed * (weight * local_innovation)[None])
    carried = jnp.zeros_like(gradient)
    residual = gradient
    direction = residual
    norm_now = norm_of(residual)
    for iteration in range(ITERS):
        smoothed = smooth(direction)
        total = member_total(perturbed * smoothed)
        back = smooth(perturbed * (weight * total)[None])
        image, smoothed = (direction + back, smoothed)
        step_size = norm_now / lax.psum(jnp.sum(direction * image), ("grid", "mem"))
        carried = carried + step_size * smoothed
        residual = residual - step_size * image
        if iteration + 1 < ITERS:
            norm_next = norm_of(residual)
            direction = residual + norm_next / norm_now * direction
            norm_now = norm_next
    increment = member_total(perturbed * carried)
    whole = lax.all_gather(increment, "mem", axis=0, tiled=True)
    recentred = (members.astype(jnp.float32) + whole[None]).astype(jnp.bfloat16)
    return (recentred, increment)


def smooth_rows(field):
    for sweep_index in range(PASSES):
        edge = jnp.zeros_like(field[..., :1, :])
        north = jnp.concatenate([edge, field[..., :-1, :]], axis=-2)
        south = jnp.concatenate([field[..., 1:, :], edge], axis=-2)
        field = field + diffusion * (north + south - 2.0 * field)
    for sweep_index in range(PASSES):
        field = field + diffusion * (jnp.roll(field, 1, -1) + jnp.roll(field, -1, -1) - 2.0 * field)
    return field


def all_sum(values):
    devices = lax.axis_size("grid") * lax.axis_size("mem")
    row = jnp.zeros((128,), jnp.float32).at[: values.shape[0]].set(values)
    gathered = lax.all_to_all(jnp.broadcast_to(row, (devices, 128)), ("grid", "mem"), 0, 0, tiled=True)
    return jnp.sum(gathered, axis=0)


def local_by_level(members, innovation, observed_count, obs_precision):
    grid_size = lax.axis_size("grid")
    mem_size = lax.axis_size("mem")
    count, levels, rows, nlon = members.shape
    copies = grid_size // levels
    nlat = rows * grid_size
    grid_index = lax.axis_index("grid")
    mem_index = lax.axis_index("mem")
    level = grid_index // copies
    chunk_level = [j // copies for j in range(grid_size)]

    sent = jnp.stack([members[:, l] for l in chunk_level], axis=0)
    got = lax.all_to_all(sent, "grid", 0, 0, tiled=True)
    mine = jnp.transpose(got, (1, 0, 2, 3)).reshape(count, nlat, nlon)
    extra = jnp.stack(
        [jnp.stack([innovation[l], observed_count.astype(jnp.float32)]) for l in chunk_level], axis=0
    )
    extra = lax.all_to_all(extra, "grid", 0, 0, tiled=True)
    extra = jnp.transpose(extra, (1, 0, 2, 3)).reshape(2, nlat, nlon)
    precision = lax.dynamic_index_in_dim(obs_precision, level, 0, keepdims=False)
    weight = extra[1] * precision
    widened = mine.astype(jnp.float32)

    span = nlat // copies
    own = (lax.broadcasted_iota(jnp.int32, (nlat, nlon), 0) // span) == grid_index % copies
    first = mem_index == 0

    def squares(field):
        return jnp.sum(jnp.where(own[None], field * field, 0.0))

    def weighted(total):
        return jnp.where(first, jnp.sum(jnp.where(own, weight * total * total, 0.0)), 0.0)

    def project(field):
        return lax.psum(jnp.sum(widened * field, axis=0), "mem")

    residual = smooth_rows(widened * (weight * extra[0])[None])
    total1 = project(smooth_rows(residual))
    image = residual + smooth_rows(widened * (weight * total1)[None])
    projected_image = project(smooth_rows(image))
    first_sums = all_sum(jnp.stack([squares(residual), weighted(total1)]))
    norm_now = first_sums[0]
    step1 = norm_now / (norm_now + first_sums[1])
    residual_next = residual - step1 * image
    norm_next = all_sum(jnp.stack([squares(residual_next)]))[0]
    beta = norm_next / norm_now
    direction = residual_next + beta * residual
    total2 = (total1 - step1 * projected_image) + beta * total1
    second_sums = all_sum(jnp.stack([squares(direction), weighted(total2)]))
    step2 = norm_next / (second_sums[0] + second_sums[1])
    increment = step1 * total1 + step2 * total2

    spread = lax.all_to_all(increment.reshape(grid_size, rows, nlon), "grid", 0, 0, tiled=True)
    whole = spread.reshape(levels, copies, rows, nlon)[:, 0]
    share = levels // mem_size
    mine_out = lax.dynamic_slice_in_dim(whole, mem_index * share, share, 0)
    recentred = (members.astype(jnp.float32) + whole[None]).astype(jnp.bfloat16)
    return (recentred, mine_out)


def solution(mesh):
    placed = (P("mem", None, "grid", None), P(None, "grid", None), P("grid", None), P())
    grid_size, mem_size = mesh.shape["grid"], mesh.shape["mem"]
    body = local

    def chosen(members, innovation, observed_count, obs_precision):
        levels = members.shape[1]
        fits = grid_size % levels == 0 and grid_size // levels <= 2 and levels % mem_size == 0 and ITERS == 2
        pick = local_by_level if fits else body
        return jax.shard_map(
            pick,
            mesh=mesh,
            in_specs=placed,
            out_specs=(P("mem", None, "grid", None), P("mem", "grid", None)),
            check_vma=False,
        )(members, innovation, observed_count, obs_precision)

    return chosen
```

```python
import jax
import jax.numpy as jnp
from jax import lax
from jax.sharding import PartitionSpec as P

PASSES = 2
ITERS = 2


diffusion = 0.25


def padded(value, sides, width):
    for axis, dim in sides:
        devices, length = (lax.axis_size(axis), value.shape[dim])
        up = [(i, (i + 1) % devices) for i in range(devices - 1)]
        down = [(j, i) for i, j in up]
        last = lax.slice_in_dim(value, length - width, length, axis=dim)
        leading = lax.slice_in_dim(value, 0, width, axis=dim)
        before = lax.ppermute(last, axis, up)
        after = lax.ppermute(leading, axis, down)
        value = jnp.concatenate([before, value, after], axis=dim)
    return value


def smooth(field):
    for sweep_index in range(PASSES):
        extended = padded(field, (("grid", 2),), 1)
        centre = extended[:, :, 1:-1]
        field = centre + diffusion * (extended[:, :, :-2] + extended[:, :, 2:] - 2.0 * centre)
    for sweep_index in range(PASSES):
        field = field + diffusion * (jnp.roll(field, 1, 3) + jnp.roll(field, -1, 3) - 2.0 * field)
    return field


def member_total(product):
    summed = jnp.sum(product, axis=0)
    return summed


def norm_of(residual):
    return lax.psum(jnp.sum(residual * residual), ("grid", "mem"))


def local(members, innovation, observed_count, obs_precision):
    mem_index = lax.axis_index("mem")
    level_share = members.shape[1] // lax.axis_size("mem")
    perturbed = lax.all_to_all(members, "mem", split_axis=1, concat_axis=0, tiled=True)
    precision = lax.dynamic_slice_in_dim(obs_precision, mem_index * level_share, level_share, 0)
    local_innovation = lax.dynamic_slice_in_dim(innovation, mem_index * level_share, level_share, 0)
    weight = observed_count.astype(jnp.float32)[None] * precision[:, None, None]
    gradient = smooth(perturbed * (weight * local_innovation)[None])
    carried = jnp.zeros_like(gradient)
    residual = gradient
    direction = residual
    norm_now = norm_of(residual)
    for iteration in range(ITERS):
        smoothed = smooth(direction)
        total = member_total(perturbed * smoothed)
        back = smooth(perturbed * (weight * total)[None])
        image, smoothed = (direction + back, smoothed)
        step_size = norm_now / lax.psum(jnp.sum(direction * image), ("grid", "mem"))
        carried = carried + step_size * smoothed
        residual = residual - step_size * image
        if iteration + 1 < ITERS:
            norm_next = norm_of(residual)
            direction = residual + norm_next / norm_now * direction
            norm_now = norm_next
    increment = member_total(perturbed * carried)
    whole = lax.all_gather(increment, "mem", axis=0, tiled=True)
    recentred = (members.astype(jnp.float32) + whole[None]).astype(jnp.bfloat16)
    return (recentred, increment)


def smooth_rows(field):
    for sweep_index in range(PASSES):
        edge = jnp.zeros_like(field[..., :1, :])
        north = jnp.concatenate([edge, field[..., :-1, :]], axis=-2)
        south = jnp.concatenate([field[..., 1:, :], edge], axis=-2)
        field = field + diffusion * (north + south - 2.0 * field)
    for sweep_index in range(PASSES):
        field = field + diffusion * (jnp.roll(field, 1, -1) + jnp.roll(field, -1, -1) - 2.0 * field)
    return field


def exchange(values, rows_for):
    devices = lax.axis_size("grid") * lax.axis_size("mem")
    nlon = rows_for.shape[-1]
    head = jnp.zeros((nlon,), jnp.float32).at[: values.shape[0]].set(values)
    head = jnp.broadcast_to(head, (devices, 1, nlon))
    parcel = jnp.concatenate([head, rows_for], axis=1)
    return lax.all_to_all(parcel, ("grid", "mem"), 0, 0, tiled=True)


def local_by_level(members, innovation, observed_count, obs_precision):
    grid_size = lax.axis_size("grid")
    mem_size = lax.axis_size("mem")
    count, levels, rows, nlon = members.shape
    copies = grid_size // levels
    nlat = rows * grid_size
    grid_index = lax.axis_index("grid")
    mem_index = lax.axis_index("mem")
    level = grid_index // copies

    counts = jnp.broadcast_to(observed_count.astype(jnp.bfloat16), (1, levels, rows, nlon))
    packed = jnp.repeat(jnp.concatenate([members, counts], axis=0), copies, axis=1)
    got = lax.all_to_all(packed, "grid", 1, 2, tiled=True)[:, 0]
    innov = lax.all_to_all(jnp.repeat(innovation, copies, axis=0), "grid", 0, 1, tiled=True)[0]
    precision = lax.dynamic_index_in_dim(obs_precision, level, 0, keepdims=False)
    weight = got[count].astype(jnp.float32) * precision
    widened = got[:count].astype(jnp.float32)

    span = nlat // copies
    own = (lax.broadcasted_iota(jnp.int32, (nlat, nlon), 0) // span) == grid_index % copies
    first = mem_index == 0

    def squares(field):
        return jnp.sum(jnp.where(own[None], field * field, 0.0))

    def weighted(total):
        return jnp.where(first, jnp.sum(jnp.where(own, weight * total * total, 0.0)), 0.0)

    def by_target(field):
        return jnp.repeat(field.reshape(grid_size, rows, nlon), mem_size, axis=0)

    residual = smooth_rows(widened * (weight * innov)[None])
    total1 = lax.psum(jnp.sum(widened * smooth_rows(residual), axis=0), "mem")
    image = residual + smooth_rows(widened * (weight * total1)[None])
    image_part = jnp.sum(widened * smooth_rows(image), axis=0)

    got1 = exchange(jnp.stack([squares(residual), weighted(total1)]), by_target(total1))
    norm_now = jnp.sum(got1[:, 0, 0])
    step1 = norm_now / (norm_now + jnp.sum(got1[:, 0, 1]))
    total1_rows = got1.reshape(levels, copies * mem_size, 1 + rows, nlon)[:, 0, 1:]

    residual_next = residual - step1 * image
    got2 = exchange(jnp.stack([squares(residual_next)]), by_target(image_part))
    norm_next = jnp.sum(got2[:, 0, 0])
    beta = norm_next / norm_now
    image_rows = jnp.sum(got2.reshape(levels, copies, mem_size, 1 + rows, nlon)[:, 0, :, 1:], axis=1)

    direction = residual_next + beta * residual
    weight_rows = observed_count.astype(jnp.float32)[None] * obs_precision[:, None, None]
    total2_rows = (total1_rows - step1 * image_rows) + beta * total1_rows
    q2 = jnp.where(first, jnp.sum(weight_rows * total2_rows * total2_rows), 0.0)
    got3 = exchange(jnp.stack([squares(direction), q2]), jnp.zeros((grid_size * mem_size, 0, nlon), jnp.float32))
    step2 = norm_next / (jnp.sum(got3[:, 0, 0]) + jnp.sum(got3[:, 0, 1]))
    whole = step1 * total1_rows + step2 * total2_rows

    share = levels // mem_size
    mine_out = lax.dynamic_slice_in_dim(whole, mem_index * share, share, 0)
    recentred = (members.astype(jnp.float32) + whole[None]).astype(jnp.bfloat16)
    return (recentred, mine_out)


def solution(mesh):
    placed = (P("mem", None, "grid", None), P(None, "grid", None), P("grid", None), P())
    grid_size, mem_size = mesh.shape["grid"], mesh.shape["mem"]
    body = local

    def chosen(members, innovation, observed_count, obs_precision):
        levels = members.shape[1]
        fits = grid_size % levels == 0 and grid_size // levels <= 2 and levels % mem_size == 0 and ITERS == 2
        pick = local_by_level if fits else body
        return jax.shard_map(
            pick,
            mesh=mesh,
            in_specs=placed,
            out_specs=(P("mem", None, "grid", None), P("mem", "grid", None)),
            check_vma=False,
        )(members, innovation, observed_count, obs_precision)

    return chosen
```

```python
import jax
import jax.numpy as jnp
from jax import lax
from jax.sharding import PartitionSpec as P

PASSES = 2
ITERS = 2


diffusion = 0.25


def padded(value, sides, width):
    for axis, dim in sides:
        devices, length = (lax.axis_size(axis), value.shape[dim])
        up = [(i, (i + 1) % devices) for i in range(devices - 1)]
        down = [(j, i) for i, j in up]
        last = lax.slice_in_dim(value, length - width, length, axis=dim)
        leading = lax.slice_in_dim(value, 0, width, axis=dim)
        before = lax.ppermute(last, axis, up)
        after = lax.ppermute(leading, axis, down)
        value = jnp.concatenate([before, value, after], axis=dim)
    return value


def smooth(field):
    for sweep_index in range(PASSES):
        extended = padded(field, (("grid", 2),), 1)
        centre = extended[:, :, 1:-1]
        field = centre + diffusion * (extended[:, :, :-2] + extended[:, :, 2:] - 2.0 * centre)
    for sweep_index in range(PASSES):
        field = field + diffusion * (jnp.roll(field, 1, 3) + jnp.roll(field, -1, 3) - 2.0 * field)
    return field


def member_total(product):
    summed = jnp.sum(product, axis=0)
    return summed


def norm_of(residual):
    return lax.psum(jnp.sum(residual * residual), ("grid", "mem"))


def local(members, innovation, observed_count, obs_precision):
    mem_index = lax.axis_index("mem")
    level_share = members.shape[1] // lax.axis_size("mem")
    perturbed = lax.all_to_all(members, "mem", split_axis=1, concat_axis=0, tiled=True)
    precision = lax.dynamic_slice_in_dim(obs_precision, mem_index * level_share, level_share, 0)
    local_innovation = lax.dynamic_slice_in_dim(innovation, mem_index * level_share, level_share, 0)
    weight = observed_count.astype(jnp.float32)[None] * precision[:, None, None]
    gradient = smooth(perturbed * (weight * local_innovation)[None])
    carried = jnp.zeros_like(gradient)
    residual = gradient
    direction = residual
    norm_now = norm_of(residual)
    for iteration in range(ITERS):
        smoothed = smooth(direction)
        total = member_total(perturbed * smoothed)
        back = smooth(perturbed * (weight * total)[None])
        image, smoothed = (direction + back, smoothed)
        step_size = norm_now / lax.psum(jnp.sum(direction * image), ("grid", "mem"))
        carried = carried + step_size * smoothed
        residual = residual - step_size * image
        if iteration + 1 < ITERS:
            norm_next = norm_of(residual)
            direction = residual + norm_next / norm_now * direction
            norm_now = norm_next
    increment = member_total(perturbed * carried)
    whole = lax.all_gather(increment, "mem", axis=0, tiled=True)
    recentred = (members.astype(jnp.float32) + whole[None]).astype(jnp.bfloat16)
    return (recentred, increment)


def smooth_rows(field):
    for sweep_index in range(PASSES):
        edge = jnp.zeros_like(field[..., :1, :])
        north = jnp.concatenate([edge, field[..., :-1, :]], axis=-2)
        south = jnp.concatenate([field[..., 1:, :], edge], axis=-2)
        field = field + diffusion * (north + south - 2.0 * field)
    for sweep_index in range(PASSES):
        field = field + diffusion * (jnp.roll(field, 1, -1) + jnp.roll(field, -1, -1) - 2.0 * field)
    return field


def exchange(values, rows_for):
    devices = lax.axis_size("grid") * lax.axis_size("mem")
    nlon = rows_for.shape[-1]
    head = jnp.zeros((nlon,), jnp.float32).at[: values.shape[0]].set(values)
    head = jnp.broadcast_to(head, (devices, 1, nlon))
    parcel = jnp.concatenate([head, rows_for], axis=1)
    return lax.all_to_all(parcel, ("grid", "mem"), 0, 0, tiled=True)


def local_by_level(members, innovation, observed_count, obs_precision):
    grid_size = lax.axis_size("grid")
    mem_size = lax.axis_size("mem")
    count, levels, rows, nlon = members.shape
    copies = grid_size // levels
    nlat = rows * grid_size
    grid_index = lax.axis_index("grid")
    mem_index = lax.axis_index("mem")
    level = grid_index // copies

    counts = jnp.broadcast_to(observed_count.astype(jnp.bfloat16), (1, levels, rows, nlon))
    high = lax.reduce_precision(innovation, exponent_bits=8, mantissa_bits=7)
    rest = innovation - high
    middle = lax.reduce_precision(rest, exponent_bits=8, mantissa_bits=7)
    low = rest - middle
    parts = jnp.stack([high, middle, low]).astype(jnp.bfloat16)
    packed = jnp.repeat(jnp.concatenate([members, counts, parts], axis=0), copies, axis=1)
    got = lax.all_to_all(packed, "grid", 1, 2, tiled=True)[:, 0]
    split = got[count + 1 :].astype(jnp.float32)
    innov = (split[0] + split[1]) + split[2]
    precision = lax.dynamic_index_in_dim(obs_precision, level, 0, keepdims=False)
    weight = got[count].astype(jnp.float32) * precision
    widened = got[:count].astype(jnp.float32)

    span = nlat // copies
    own = (lax.broadcasted_iota(jnp.int32, (nlat, nlon), 0) // span) == grid_index % copies
    first = mem_index == 0

    def squares(field):
        return jnp.sum(jnp.where(own[None], field * field, 0.0))

    def weighted(total):
        return jnp.where(first, jnp.sum(jnp.where(own, weight * total * total, 0.0)), 0.0)

    def by_target(field):
        return jnp.repeat(field.reshape(grid_size, rows, nlon), mem_size, axis=0)

    residual = smooth_rows(widened * (weight * innov)[None])
    total1 = lax.psum(jnp.sum(widened * smooth_rows(residual), axis=0), "mem")
    image = residual + smooth_rows(widened * (weight * total1)[None])
    image_part = jnp.sum(widened * smooth_rows(image), axis=0)

    got1 = exchange(jnp.stack([squares(residual), weighted(total1)]), by_target(total1))
    norm_now = jnp.sum(got1[:, 0, 0])
    step1 = norm_now / (norm_now + jnp.sum(got1[:, 0, 1]))
    total1_rows = got1.reshape(levels, copies * mem_size, 1 + rows, nlon)[:, 0, 1:]

    residual_next = residual - step1 * image
    got2 = exchange(jnp.stack([squares(residual_next)]), by_target(image_part))
    norm_next = jnp.sum(got2[:, 0, 0])
    beta = norm_next / norm_now
    image_rows = jnp.sum(got2.reshape(levels, copies, mem_size, 1 + rows, nlon)[:, 0, :, 1:], axis=1)

    direction = residual_next + beta * residual
    weight_rows = observed_count.astype(jnp.float32)[None] * obs_precision[:, None, None]
    total2_rows = (total1_rows - step1 * image_rows) + beta * total1_rows
    q2 = jnp.where(first, jnp.sum(weight_rows * total2_rows * total2_rows), 0.0)
    got3 = exchange(jnp.stack([squares(direction), q2]), jnp.zeros((grid_size * mem_size, 0, nlon), jnp.float32))
    step2 = norm_next / (jnp.sum(got3[:, 0, 0]) + jnp.sum(got3[:, 0, 1]))
    whole = step1 * total1_rows + step2 * total2_rows

    share = levels // mem_size
    mine_out = lax.dynamic_slice_in_dim(whole, mem_index * share, share, 0)
    recentred = (members.astype(jnp.float32) + whole[None]).astype(jnp.bfloat16)
    return (recentred, mine_out)


def solution(mesh):
    placed = (P("mem", None, "grid", None), P(None, "grid", None), P("grid", None), P())
    grid_size, mem_size = mesh.shape["grid"], mesh.shape["mem"]
    body = local

    def chosen(members, innovation, observed_count, obs_precision):
        levels = members.shape[1]
        fits = grid_size % levels == 0 and grid_size // levels <= 2 and levels % mem_size == 0 and ITERS == 2
        pick = local_by_level if fits else body
        return jax.shard_map(
            pick,
            mesh=mesh,
            in_specs=placed,
            out_specs=(P("mem", None, "grid", None), P("mem", "grid", None)),
            check_vma=False,
        )(members, innovation, observed_count, obs_precision)

    return chosen
```

```python
import jax
import jax.numpy as jnp
from jax import lax
from jax.sharding import PartitionSpec as P

PASSES = 2
ITERS = 2


diffusion = 0.25


def padded(value, sides, width):
    for axis, dim in sides:
        devices, length = (lax.axis_size(axis), value.shape[dim])
        up = [(i, (i + 1) % devices) for i in range(devices - 1)]
        down = [(j, i) for i, j in up]
        last = lax.slice_in_dim(value, length - width, length, axis=dim)
        leading = lax.slice_in_dim(value, 0, width, axis=dim)
        before = lax.ppermute(last, axis, up)
        after = lax.ppermute(leading, axis, down)
        value = jnp.concatenate([before, value, after], axis=dim)
    return value


def smooth(field):
    for sweep_index in range(PASSES):
        extended = padded(field, (("grid", 2),), 1)
        centre = extended[:, :, 1:-1]
        field = centre + diffusion * (extended[:, :, :-2] + extended[:, :, 2:] - 2.0 * centre)
    for sweep_index in range(PASSES):
        field = field + diffusion * (jnp.roll(field, 1, 3) + jnp.roll(field, -1, 3) - 2.0 * field)
    return field


def member_total(product):
    summed = jnp.sum(product, axis=0)
    return summed


def norm_of(residual):
    return lax.psum(jnp.sum(residual * residual), ("grid", "mem"))


def local(members, innovation, observed_count, obs_precision):
    mem_index = lax.axis_index("mem")
    level_share = members.shape[1] // lax.axis_size("mem")
    perturbed = lax.all_to_all(members, "mem", split_axis=1, concat_axis=0, tiled=True)
    precision = lax.dynamic_slice_in_dim(obs_precision, mem_index * level_share, level_share, 0)
    local_innovation = lax.dynamic_slice_in_dim(innovation, mem_index * level_share, level_share, 0)
    weight = observed_count.astype(jnp.float32)[None] * precision[:, None, None]
    gradient = smooth(perturbed * (weight * local_innovation)[None])
    carried = jnp.zeros_like(gradient)
    residual = gradient
    direction = residual
    norm_now = norm_of(residual)
    for iteration in range(ITERS):
        smoothed = smooth(direction)
        total = member_total(perturbed * smoothed)
        back = smooth(perturbed * (weight * total)[None])
        image, smoothed = (direction + back, smoothed)
        step_size = norm_now / lax.psum(jnp.sum(direction * image), ("grid", "mem"))
        carried = carried + step_size * smoothed
        residual = residual - step_size * image
        if iteration + 1 < ITERS:
            norm_next = norm_of(residual)
            direction = residual + norm_next / norm_now * direction
            norm_now = norm_next
    increment = member_total(perturbed * carried)
    whole = lax.all_gather(increment, "mem", axis=0, tiled=True)
    recentred = (members.astype(jnp.float32) + whole[None]).astype(jnp.bfloat16)
    return (recentred, increment)


def smooth_rows(field):
    for sweep_index in range(PASSES):
        edge = jnp.zeros_like(field[..., :1, :])
        north = jnp.concatenate([edge, field[..., :-1, :]], axis=-2)
        south = jnp.concatenate([field[..., 1:, :], edge], axis=-2)
        field = field + diffusion * (north + south - 2.0 * field)
    for sweep_index in range(PASSES):
        field = field + diffusion * (jnp.roll(field, 1, -1) + jnp.roll(field, -1, -1) - 2.0 * field)
    return field


def exchange(values, rows_for):
    devices = lax.axis_size("grid") * lax.axis_size("mem")
    nlon = rows_for.shape[-1]
    head = jnp.zeros((nlon,), jnp.float32).at[: values.shape[0]].set(values)
    head = jnp.broadcast_to(head, (devices, 1, nlon))
    parcel = jnp.concatenate([head, rows_for], axis=1)
    return lax.all_to_all(parcel, ("grid", "mem"), 0, 0, tiled=True)


def local_by_level(members, innovation, observed_count, obs_precision):
    grid_size = lax.axis_size("grid")
    mem_size = lax.axis_size("mem")
    count, levels, rows, nlon = members.shape
    copies = grid_size // levels
    nlat = rows * grid_size
    grid_index = lax.axis_index("grid")
    mem_index = lax.axis_index("mem")
    level = grid_index // copies

    counts = jnp.broadcast_to(observed_count.astype(jnp.bfloat16), (1, levels, rows, nlon))
    high = lax.reduce_precision(innovation, exponent_bits=8, mantissa_bits=7)
    rest = innovation - high
    middle = lax.reduce_precision(rest, exponent_bits=8, mantissa_bits=7)
    low = rest - middle
    parts = jnp.stack([high, middle, low]).astype(jnp.bfloat16)
    packed = jnp.repeat(jnp.concatenate([members, counts, parts], axis=0), copies, axis=1)
    got = lax.all_to_all(packed, "grid", 1, 2, tiled=True)[:, 0]
    split = got[count + 1 :].astype(jnp.float32)
    innov = (split[0] + split[1]) + split[2]
    precision = lax.dynamic_index_in_dim(obs_precision, level, 0, keepdims=False)
    weight = got[count].astype(jnp.float32) * precision
    widened = got[:count].astype(jnp.float32)

    span = nlat // copies
    own = (lax.broadcasted_iota(jnp.int32, (nlat, nlon), 0) // span) == grid_index % copies
    first = mem_index == 0

    def squares(field):
        return jnp.sum(jnp.where(own[None], field * field, 0.0))

    def weighted(total):
        return jnp.where(first, jnp.sum(jnp.where(own, weight * total * total, 0.0)), 0.0)

    def by_target(field):
        return jnp.repeat(field.reshape(grid_size, rows, nlon), mem_size, axis=0)

    residual = smooth_rows(widened * (weight * innov)[None])
    total1 = lax.psum(jnp.sum(widened * smooth_rows(residual), axis=0), "mem")
    image = residual + smooth_rows(widened * (weight * total1)[None])
    image_part = jnp.sum(widened * smooth_rows(image), axis=0)

    got1 = exchange(
        jnp.stack([squares(residual), weighted(total1)]),
        jnp.concatenate([by_target(total1), by_target(image_part)], axis=1),
    )
    norm_now = jnp.sum(got1[:, 0, 0])
    curvature1 = jnp.sum(got1[:, 0, 1])
    step1 = norm_now / (norm_now + curvature1)
    by_source = got1.reshape(levels, copies, mem_size, 1 + 2 * rows, nlon)[:, 0]
    total1_rows = by_source[:, 0, 1 : 1 + rows]
    image_rows = jnp.sum(by_source[:, :, 1 + rows :], axis=1)

    residual_next = residual - step1 * image
    weight_rows = observed_count.astype(jnp.float32)[None] * obs_precision[:, None, None]
    moved_rows = total1_rows - step1 * image_rows
    got2 = exchange(
        jnp.stack(
            [
                squares(residual_next),
                jnp.sum(jnp.where(own[None], residual_next * residual, 0.0)),
                jnp.where(first, jnp.sum(weight_rows * moved_rows * moved_rows), 0.0),
                jnp.where(first, jnp.sum(weight_rows * moved_rows * total1_rows), 0.0),
            ]
        ),
        jnp.zeros((grid_size * mem_size, 0, nlon), jnp.float32),
    )
    sums = jnp.sum(got2[:, 0, :4], axis=0)
    norm_next = sums[0]
    beta = norm_next / norm_now
    direction_sq = norm_next + 2.0 * beta * sums[1] + beta * beta * norm_now
    curvature2 = sums[2] + 2.0 * beta * sums[3] + beta * beta * curvature1
    step2 = norm_next / (direction_sq + curvature2)
    total2_rows = moved_rows + beta * total1_rows
    whole = step1 * total1_rows + step2 * total2_rows

    share = levels // mem_size
    mine_out = lax.dynamic_slice_in_dim(whole, mem_index * share, share, 0)
    recentred = (members.astype(jnp.float32) + whole[None]).astype(jnp.bfloat16)
    return (recentred, mine_out)


def solution(mesh):
    placed = (P("mem", None, "grid", None), P(None, "grid", None), P("grid", None), P())
    grid_size, mem_size = mesh.shape["grid"], mesh.shape["mem"]
    body = local

    def chosen(members, innovation, observed_count, obs_precision):
        levels = members.shape[1]
        fits = grid_size % levels == 0 and grid_size // levels <= 2 and levels % mem_size == 0 and ITERS == 2
        pick = local_by_level if fits else body
        return jax.shard_map(
            pick,
            mesh=mesh,
            in_specs=placed,
            out_specs=(P("mem", None, "grid", None), P("mem", "grid", None)),
            check_vma=False,
        )(members, innovation, observed_count, obs_precision)

    return chosen
```

```python
import jax
import jax.numpy as jnp
from jax import lax
from jax.sharding import PartitionSpec as P

PASSES = 2
ITERS = 2


diffusion = 0.25


def padded(value, sides, width):
    for axis, dim in sides:
        devices, length = (lax.axis_size(axis), value.shape[dim])
        up = [(i, (i + 1) % devices) for i in range(devices - 1)]
        down = [(j, i) for i, j in up]
        last = lax.slice_in_dim(value, length - width, length, axis=dim)
        leading = lax.slice_in_dim(value, 0, width, axis=dim)
        before = lax.ppermute(last, axis, up)
        after = lax.ppermute(leading, axis, down)
        value = jnp.concatenate([before, value, after], axis=dim)
    return value


def smooth(field):
    for sweep_index in range(PASSES):
        extended = padded(field, (("grid", 2),), 1)
        centre = extended[:, :, 1:-1]
        field = centre + diffusion * (extended[:, :, :-2] + extended[:, :, 2:] - 2.0 * centre)
    for sweep_index in range(PASSES):
        field = field + diffusion * (jnp.roll(field, 1, 3) + jnp.roll(field, -1, 3) - 2.0 * field)
    return field


def member_total(product):
    summed = jnp.sum(product, axis=0)
    return summed


def norm_of(residual):
    return lax.psum(jnp.sum(residual * residual), ("grid", "mem"))


def local(members, innovation, observed_count, obs_precision):
    mem_index = lax.axis_index("mem")
    level_share = members.shape[1] // lax.axis_size("mem")
    perturbed = lax.all_to_all(members, "mem", split_axis=1, concat_axis=0, tiled=True)
    precision = lax.dynamic_slice_in_dim(obs_precision, mem_index * level_share, level_share, 0)
    local_innovation = lax.dynamic_slice_in_dim(innovation, mem_index * level_share, level_share, 0)
    weight = observed_count.astype(jnp.float32)[None] * precision[:, None, None]
    gradient = smooth(perturbed * (weight * local_innovation)[None])
    carried = jnp.zeros_like(gradient)
    residual = gradient
    direction = residual
    norm_now = norm_of(residual)
    for iteration in range(ITERS):
        smoothed = smooth(direction)
        total = member_total(perturbed * smoothed)
        back = smooth(perturbed * (weight * total)[None])
        image, smoothed = (direction + back, smoothed)
        step_size = norm_now / lax.psum(jnp.sum(direction * image), ("grid", "mem"))
        carried = carried + step_size * smoothed
        residual = residual - step_size * image
        if iteration + 1 < ITERS:
            norm_next = norm_of(residual)
            direction = residual + norm_next / norm_now * direction
            norm_now = norm_next
    increment = member_total(perturbed * carried)
    whole = lax.all_gather(increment, "mem", axis=0, tiled=True)
    recentred = (members.astype(jnp.float32) + whole[None]).astype(jnp.bfloat16)
    return (recentred, increment)


def smooth_rows(field):
    for sweep_index in range(PASSES):
        edge = jnp.zeros_like(field[..., :1, :])
        north = jnp.concatenate([edge, field[..., :-1, :]], axis=-2)
        south = jnp.concatenate([field[..., 1:, :], edge], axis=-2)
        field = field + diffusion * (north + south - 2.0 * field)
    for sweep_index in range(PASSES):
        field = field + diffusion * (jnp.roll(field, 1, -1) + jnp.roll(field, -1, -1) - 2.0 * field)
    return field


def exchange(values, rows_for):
    devices = lax.axis_size("grid") * lax.axis_size("mem")
    nlon = rows_for.shape[-1]
    head = jnp.zeros((nlon,), jnp.float32).at[: values.shape[0]].set(values)
    head = jnp.broadcast_to(head, (devices, 1, nlon))
    parcel = jnp.concatenate([head, rows_for], axis=1)
    return lax.all_to_all(parcel, ("grid", "mem"), 0, 0, tiled=True)


def local_by_level(members, innovation, observed_count, obs_precision):
    grid_size = lax.axis_size("grid")
    mem_size = lax.axis_size("mem")
    count, levels, rows, nlon = members.shape
    copies = grid_size // levels
    nlat = rows * grid_size
    grid_index = lax.axis_index("grid")
    mem_index = lax.axis_index("mem")
    level = grid_index // copies

    counts = jnp.broadcast_to(observed_count.astype(jnp.bfloat16), (1, levels, rows, nlon))
    high = lax.reduce_precision(innovation, exponent_bits=8, mantissa_bits=7)
    rest = innovation - high
    middle = lax.reduce_precision(rest, exponent_bits=8, mantissa_bits=7)
    low = rest - middle
    parts = jnp.stack([high, middle, low]).astype(jnp.bfloat16)
    packed = jnp.repeat(jnp.concatenate([members, counts, parts], axis=0), copies, axis=1)
    got = lax.all_to_all(packed, "grid", 1, 2, tiled=True)[:, 0]
    split = got[count + 1 :].astype(jnp.float32)
    innov = (split[0] + split[1]) + split[2]
    precision = lax.dynamic_index_in_dim(obs_precision, level, 0, keepdims=False)
    weight = got[count].astype(jnp.float32) * precision
    widened = got[:count].astype(jnp.float32)

    span = nlat // copies
    own = (lax.broadcasted_iota(jnp.int32, (nlat, nlon), 0) // span) == grid_index % copies
    first = mem_index == 0

    def squares(field):
        return jnp.sum(jnp.where(own[None], field * field, 0.0))

    def weighted(total):
        return jnp.where(first, jnp.sum(jnp.where(own, weight * total * total, 0.0)), 0.0)

    def by_target(field):
        return jnp.repeat(field.reshape(grid_size, rows, nlon), mem_size, axis=0)

    residual = smooth_rows(widened * (weight * innov)[None])
    total1 = lax.psum(jnp.sum(widened * smooth_rows(residual), axis=0), "mem")
    image = residual + smooth_rows(widened * (weight * total1)[None])
    image_part = jnp.sum(widened * smooth_rows(image), axis=0)

    if copies > 1:
        rows_for = jnp.where(grid_index % copies == 0, by_target(total1), by_target(image_part))
    else:
        rows_for = jnp.concatenate([by_target(total1), by_target(image_part)], axis=1)
    got1 = exchange(jnp.stack([squares(residual), weighted(total1)]), rows_for)
    norm_now = jnp.sum(got1[:, 0, 0])
    curvature1 = jnp.sum(got1[:, 0, 1])
    step1 = norm_now / (norm_now + curvature1)
    if copies > 1:
        by_source = got1.reshape(levels, copies, mem_size, 1 + rows, nlon)
        total1_rows = by_source[:, 0, 0, 1:]
        image_rows = jnp.sum(by_source[:, 1, :, 1:], axis=1)
    else:
        by_source = got1.reshape(levels, mem_size, 1 + 2 * rows, nlon)
        total1_rows = by_source[:, 0, 1 : 1 + rows]
        image_rows = jnp.sum(by_source[:, :, 1 + rows :], axis=1)

    residual_next = residual - step1 * image
    weight_rows = observed_count.astype(jnp.float32)[None] * obs_precision[:, None, None]
    moved_rows = total1_rows - step1 * image_rows
    got2 = exchange(
        jnp.stack(
            [
                squares(residual_next),
                jnp.sum(jnp.where(own[None], residual_next * residual, 0.0)),
                jnp.where(first, jnp.sum(weight_rows * moved_rows * moved_rows), 0.0),
                jnp.where(first, jnp.sum(weight_rows * moved_rows * total1_rows), 0.0),
            ]
        ),
        jnp.zeros((grid_size * mem_size, 0, nlon), jnp.float32),
    )
    sums = jnp.sum(got2[:, 0, :4], axis=0)
    norm_next = sums[0]
    beta = norm_next / norm_now
    direction_sq = norm_next + 2.0 * beta * sums[1] + beta * beta * norm_now
    curvature2 = sums[2] + 2.0 * beta * sums[3] + beta * beta * curvature1
    step2 = norm_next / (direction_sq + curvature2)
    total2_rows = moved_rows + beta * total1_rows
    whole = step1 * total1_rows + step2 * total2_rows

    share = levels // mem_size
    mine_out = lax.dynamic_slice_in_dim(whole, mem_index * share, share, 0)
    recentred = (members.astype(jnp.float32) + whole[None]).astype(jnp.bfloat16)
    return (recentred, mine_out)


def solution(mesh):
    placed = (P("mem", None, "grid", None), P(None, "grid", None), P("grid", None), P())
    grid_size, mem_size = mesh.shape["grid"], mesh.shape["mem"]
    body = local

    def chosen(members, innovation, observed_count, obs_precision):
        levels = members.shape[1]
        fits = grid_size % levels == 0 and grid_size // levels <= 2 and levels % mem_size == 0 and ITERS == 2
        pick = local_by_level if fits else body
        return jax.shard_map(
            pick,
            mesh=mesh,
            in_specs=placed,
            out_specs=(P("mem", None, "grid", None), P("mem", "grid", None)),
            check_vma=False,
        )(members, innovation, observed_count, obs_precision)

    return chosen
```

```python
import jax
import jax.numpy as jnp
from jax import lax
from jax.sharding import PartitionSpec as P

PASSES = 2
ITERS = 2


diffusion = 0.25


def padded(value, sides, width):
    for axis, dim in sides:
        devices, length = (lax.axis_size(axis), value.shape[dim])
        up = [(i, (i + 1) % devices) for i in range(devices - 1)]
        down = [(j, i) for i, j in up]
        last = lax.slice_in_dim(value, length - width, length, axis=dim)
        leading = lax.slice_in_dim(value, 0, width, axis=dim)
        before = lax.ppermute(last, axis, up)
        after = lax.ppermute(leading, axis, down)
        value = jnp.concatenate([before, value, after], axis=dim)
    return value


def smooth(field):
    for sweep_index in range(PASSES):
        extended = padded(field, (("grid", 2),), 1)
        centre = extended[:, :, 1:-1]
        field = centre + diffusion * (extended[:, :, :-2] + extended[:, :, 2:] - 2.0 * centre)
    for sweep_index in range(PASSES):
        field = field + diffusion * (jnp.roll(field, 1, 3) + jnp.roll(field, -1, 3) - 2.0 * field)
    return field


def member_total(product):
    summed = jnp.sum(product, axis=0)
    return summed


def norm_of(residual):
    return lax.psum(jnp.sum(residual * residual), ("grid", "mem"))


def local(members, innovation, observed_count, obs_precision):
    mem_index = lax.axis_index("mem")
    level_share = members.shape[1] // lax.axis_size("mem")
    perturbed = lax.all_to_all(members, "mem", split_axis=1, concat_axis=0, tiled=True)
    precision = lax.dynamic_slice_in_dim(obs_precision, mem_index * level_share, level_share, 0)
    local_innovation = lax.dynamic_slice_in_dim(innovation, mem_index * level_share, level_share, 0)
    weight = observed_count.astype(jnp.float32)[None] * precision[:, None, None]
    gradient = smooth(perturbed * (weight * local_innovation)[None])
    carried = jnp.zeros_like(gradient)
    residual = gradient
    direction = residual
    norm_now = norm_of(residual)
    for iteration in range(ITERS):
        smoothed = smooth(direction)
        total = member_total(perturbed * smoothed)
        back = smooth(perturbed * (weight * total)[None])
        image, smoothed = (direction + back, smoothed)
        step_size = norm_now / lax.psum(jnp.sum(direction * image), ("grid", "mem"))
        carried = carried + step_size * smoothed
        residual = residual - step_size * image
        if iteration + 1 < ITERS:
            norm_next = norm_of(residual)
            direction = residual + norm_next / norm_now * direction
            norm_now = norm_next
    increment = member_total(perturbed * carried)
    whole = lax.all_gather(increment, "mem", axis=0, tiled=True)
    recentred = (members.astype(jnp.float32) + whole[None]).astype(jnp.bfloat16)
    return (recentred, increment)


def smooth_rows(field):
    for sweep_index in range(PASSES):
        edge = jnp.zeros_like(field[..., :1, :])
        north = jnp.concatenate([edge, field[..., :-1, :]], axis=-2)
        south = jnp.concatenate([field[..., 1:, :], edge], axis=-2)
        field = field + diffusion * (north + south - 2.0 * field)
    for sweep_index in range(PASSES):
        field = field + diffusion * (jnp.roll(field, 1, -1) + jnp.roll(field, -1, -1) - 2.0 * field)
    return field


def exchange(values, rows_for):
    devices = lax.axis_size("grid") * lax.axis_size("mem")
    nlon = rows_for.shape[-1]
    lanes = [jnp.sum(v.reshape(-1, 128), axis=0) for v in values]
    lanes.append(jnp.zeros((nlon - 128 * len(values),), jnp.float32))
    head = jnp.broadcast_to(jnp.concatenate(lanes), (devices, 1, nlon))
    parcel = jnp.concatenate([head, rows_for], axis=1)
    got = lax.all_to_all(parcel, ("grid", "mem"), 0, 0, tiled=True)
    sums = jnp.sum(got[:, 0].reshape(devices, nlon // 128, 128), axis=(0, 2))
    return sums, got[:, 1:]


def mem_total(part):
    mem_size = lax.axis_size("mem")
    got = lax.all_to_all(jnp.broadcast_to(part, (mem_size,) + part.shape), "mem", 0, 0, tiled=True)
    return jnp.sum(got, axis=0)


def local_by_level(members, innovation, observed_count, obs_precision):
    grid_size = lax.axis_size("grid")
    mem_size = lax.axis_size("mem")
    count, levels, rows, nlon = members.shape
    copies = grid_size // levels
    nlat = rows * grid_size
    grid_index = lax.axis_index("grid")
    mem_index = lax.axis_index("mem")
    level = grid_index // copies

    counts = jnp.broadcast_to(observed_count.astype(jnp.bfloat16), (1, levels, rows, nlon))
    high = lax.reduce_precision(innovation, exponent_bits=8, mantissa_bits=7)
    rest = innovation - high
    middle = lax.reduce_precision(rest, exponent_bits=8, mantissa_bits=7)
    low = rest - middle
    parts = jnp.stack([high, middle, low]).astype(jnp.bfloat16)
    packed = jnp.repeat(jnp.concatenate([members, counts, parts], axis=0), copies, axis=1)
    got = lax.all_to_all(packed, "grid", 1, 2, tiled=True)[:, 0]
    split = got[count + 1 :].astype(jnp.float32)
    innov = (split[0] + split[1]) + split[2]
    precision = lax.dynamic_index_in_dim(obs_precision, level, 0, keepdims=False)
    weight = got[count].astype(jnp.float32) * precision
    widened = got[:count].astype(jnp.float32)

    span = nlat // copies
    own = (lax.broadcasted_iota(jnp.int32, (nlat, nlon), 0) // span) == grid_index % copies
    first = mem_index == 0

    def squares(field):
        return jnp.sum(jnp.where(own[None], field * field, 0.0), axis=(0, 1))

    def weighted(total):
        return jnp.where(first, jnp.sum(jnp.where(own, weight * total * total, 0.0), axis=0), 0.0)

    def by_target(field):
        return jnp.repeat(field.reshape(grid_size, rows, nlon), mem_size, axis=0)

    residual = smooth_rows(widened * (weight * innov)[None])
    total1 = mem_total(jnp.sum(widened * smooth_rows(residual), axis=0))
    image = residual + smooth_rows(widened * (weight * total1)[None])
    image_part = jnp.sum(widened * smooth_rows(image), axis=0)

    if copies > 1:
        rows_for = jnp.where(grid_index % copies == 0, by_target(total1), by_target(image_part))
    else:
        rows_for = jnp.concatenate([by_target(total1), by_target(image_part)], axis=1)
    sums1, got1 = exchange([squares(residual), weighted(total1)], rows_for)
    norm_now = sums1[0]
    curvature1 = sums1[1]
    step1 = norm_now / (norm_now + curvature1)
    if copies > 1:
        by_source = got1.reshape(levels, copies, mem_size, rows, nlon)
        total1_rows = by_source[:, 0, 0]
        image_rows = jnp.sum(by_source[:, 1], axis=1)
    else:
        by_source = got1.reshape(levels, mem_size, 2 * rows, nlon)
        total1_rows = by_source[:, 0, :rows]
        image_rows = jnp.sum(by_source[:, :, rows:], axis=1)

    residual_next = residual - step1 * image
    weight_rows = observed_count.astype(jnp.float32)[None] * obs_precision[:, None, None]
    moved_rows = total1_rows - step1 * image_rows
    sums, _ = exchange(
        [
            squares(residual_next),
            jnp.sum(jnp.where(own[None], residual_next * residual, 0.0), axis=(0, 1)),
            jnp.where(first, jnp.sum(weight_rows * moved_rows * moved_rows, axis=(0, 1)), 0.0),
            jnp.where(first, jnp.sum(weight_rows * moved_rows * total1_rows, axis=(0, 1)), 0.0),
        ],
        jnp.zeros((grid_size * mem_size, 0, nlon), jnp.float32),
    )
    norm_next = sums[0]
    beta = norm_next / norm_now
    direction_sq = norm_next + 2.0 * beta * sums[1] + beta * beta * norm_now
    curvature2 = sums[2] + 2.0 * beta * sums[3] + beta * beta * curvature1
    step2 = norm_next / (direction_sq + curvature2)
    total2_rows = moved_rows + beta * total1_rows
    whole = step1 * total1_rows + step2 * total2_rows

    share = levels // mem_size
    mine_out = lax.dynamic_slice_in_dim(whole, mem_index * share, share, 0)
    recentred = (members.astype(jnp.float32) + whole[None]).astype(jnp.bfloat16)
    return (recentred, mine_out)


def solution(mesh):
    placed = (P("mem", None, "grid", None), P(None, "grid", None), P("grid", None), P())
    grid_size, mem_size = mesh.shape["grid"], mesh.shape["mem"]
    body = local

    def chosen(members, innovation, observed_count, obs_precision):
        levels = members.shape[1]
        fits = grid_size % levels == 0 and grid_size // levels <= 2 and levels % mem_size == 0 and ITERS == 2
        pick = local_by_level if fits else body
        return jax.shard_map(
            pick,
            mesh=mesh,
            in_specs=placed,
            out_specs=(P("mem", None, "grid", None), P("mem", "grid", None)),
            check_vma=False,
        )(members, innovation, observed_count, obs_precision)

    return chosen
```

```python
import jax
import jax.numpy as jnp
from jax import lax
from jax.sharding import PartitionSpec as P

PASSES = 2
ITERS = 2


diffusion = 0.25


def padded(value, sides, width):
    for axis, dim in sides:
        devices, length = (lax.axis_size(axis), value.shape[dim])
        up = [(i, (i + 1) % devices) for i in range(devices - 1)]
        down = [(j, i) for i, j in up]
        last = lax.slice_in_dim(value, length - width, length, axis=dim)
        leading = lax.slice_in_dim(value, 0, width, axis=dim)
        before = lax.ppermute(last, axis, up)
        after = lax.ppermute(leading, axis, down)
        value = jnp.concatenate([before, value, after], axis=dim)
    return value


def smooth(field):
    for sweep_index in range(PASSES):
        extended = padded(field, (("grid", 2),), 1)
        centre = extended[:, :, 1:-1]
        field = centre + diffusion * (extended[:, :, :-2] + extended[:, :, 2:] - 2.0 * centre)
    for sweep_index in range(PASSES):
        field = field + diffusion * (jnp.roll(field, 1, 3) + jnp.roll(field, -1, 3) - 2.0 * field)
    return field


def member_total(product):
    summed = jnp.sum(product, axis=0)
    return summed


def norm_of(residual):
    return lax.psum(jnp.sum(residual * residual), ("grid", "mem"))


def local(members, innovation, observed_count, obs_precision):
    mem_index = lax.axis_index("mem")
    level_share = members.shape[1] // lax.axis_size("mem")
    perturbed = lax.all_to_all(members, "mem", split_axis=1, concat_axis=0, tiled=True)
    precision = lax.dynamic_slice_in_dim(obs_precision, mem_index * level_share, level_share, 0)
    local_innovation = lax.dynamic_slice_in_dim(innovation, mem_index * level_share, level_share, 0)
    weight = observed_count.astype(jnp.float32)[None] * precision[:, None, None]
    gradient = smooth(perturbed * (weight * local_innovation)[None])
    carried = jnp.zeros_like(gradient)
    residual = gradient
    direction = residual
    norm_now = norm_of(residual)
    for iteration in range(ITERS):
        smoothed = smooth(direction)
        total = member_total(perturbed * smoothed)
        back = smooth(perturbed * (weight * total)[None])
        image, smoothed = (direction + back, smoothed)
        step_size = norm_now / lax.psum(jnp.sum(direction * image), ("grid", "mem"))
        carried = carried + step_size * smoothed
        residual = residual - step_size * image
        if iteration + 1 < ITERS:
            norm_next = norm_of(residual)
            direction = residual + norm_next / norm_now * direction
            norm_now = norm_next
    increment = member_total(perturbed * carried)
    whole = lax.all_gather(increment, "mem", axis=0, tiled=True)
    recentred = (members.astype(jnp.float32) + whole[None]).astype(jnp.bfloat16)
    return (recentred, increment)


def smooth_rows(field):
    for sweep_index in range(PASSES):
        edge = jnp.zeros_like(field[..., :1, :])
        north = jnp.concatenate([edge, field[..., :-1, :]], axis=-2)
        south = jnp.concatenate([field[..., 1:, :], edge], axis=-2)
        field = field + diffusion * (north + south - 2.0 * field)
    for sweep_index in range(PASSES):
        field = field + diffusion * (jnp.roll(field, 1, -1) + jnp.roll(field, -1, -1) - 2.0 * field)
    return field


def exchange(values, rows_for):
    devices = lax.axis_size("grid") * lax.axis_size("mem")
    nlon = rows_for.shape[-1]
    lanes = [jnp.sum(v.reshape(-1, 128), axis=0) for v in values]
    lanes.append(jnp.zeros((nlon - 128 * len(values),), jnp.float32))
    head = jnp.broadcast_to(jnp.concatenate(lanes), (devices, 1, nlon))
    parcel = jnp.concatenate([head, rows_for], axis=1)
    got = lax.all_to_all(parcel, ("grid", "mem"), 0, 0, tiled=True)
    lanes = jnp.sum(got[:, 0].reshape(devices, nlon // 128, 128), axis=0)
    sums = jnp.dot(lanes, jnp.ones((128, 128), jnp.float32), precision=lax.Precision.HIGHEST)
    return [jnp.tile(sums[i : i + 1], (1, nlon // 128)) for i in range(len(values))], got[:, 1:]


def mem_total(part):
    mem_size = lax.axis_size("mem")
    got = lax.all_to_all(jnp.broadcast_to(part, (mem_size,) + part.shape), "mem", 0, 0, tiled=True)
    return jnp.sum(got, axis=0)


def local_by_level(members, innovation, observed_count, obs_precision):
    grid_size = lax.axis_size("grid")
    mem_size = lax.axis_size("mem")
    count, levels, rows, nlon = members.shape
    copies = grid_size // levels
    nlat = rows * grid_size
    grid_index = lax.axis_index("grid")
    mem_index = lax.axis_index("mem")
    level = grid_index // copies

    counts = jnp.broadcast_to(observed_count.astype(jnp.bfloat16), (1, levels, rows, nlon))
    high = lax.reduce_precision(innovation, exponent_bits=8, mantissa_bits=7)
    rest = innovation - high
    middle = lax.reduce_precision(rest, exponent_bits=8, mantissa_bits=7)
    low = rest - middle
    parts = jnp.stack([high, middle, low]).astype(jnp.bfloat16)
    packed = jnp.repeat(jnp.concatenate([members, counts, parts], axis=0), copies, axis=1)
    got = lax.all_to_all(packed, "grid", 1, 2, tiled=True)[:, 0]
    split = got[count + 1 :].astype(jnp.float32)
    innov = (split[0] + split[1]) + split[2]
    precision = lax.dynamic_index_in_dim(obs_precision, level, 0, keepdims=False)
    weight = got[count].astype(jnp.float32) * precision
    widened = got[:count].astype(jnp.float32)

    span = nlat // copies
    own = (lax.broadcasted_iota(jnp.int32, (nlat, nlon), 0) // span) == grid_index % copies
    first = mem_index == 0

    def squares(field):
        return jnp.sum(jnp.where(own[None], field * field, 0.0), axis=(0, 1))

    def weighted(total):
        return jnp.where(first, jnp.sum(jnp.where(own, weight * total * total, 0.0), axis=0), 0.0)

    def by_target(field):
        return jnp.repeat(field.reshape(grid_size, rows, nlon), mem_size, axis=0)

    residual = smooth_rows(widened * (weight * innov)[None])
    total1 = mem_total(jnp.sum(widened * smooth_rows(residual), axis=0))
    image = residual + smooth_rows(widened * (weight * total1)[None])
    image_part = jnp.sum(widened * smooth_rows(image), axis=0)

    if copies > 1:
        rows_for = jnp.where(grid_index % copies == 0, by_target(total1), by_target(image_part))
    else:
        rows_for = jnp.concatenate([by_target(total1), by_target(image_part)], axis=1)
    sums1, got1 = exchange([squares(residual), weighted(total1)], rows_for)
    norm_now = sums1[0]
    curvature1 = sums1[1]
    step1 = norm_now / (norm_now + curvature1)
    if copies > 1:
        by_source = got1.reshape(levels, copies, mem_size, rows, nlon)
        total1_rows = by_source[:, 0, 0]
        image_rows = jnp.sum(by_source[:, 1], axis=1)
    else:
        by_source = got1.reshape(levels, mem_size, 2 * rows, nlon)
        total1_rows = by_source[:, 0, :rows]
        image_rows = jnp.sum(by_source[:, :, rows:], axis=1)

    residual_next = residual - step1 * image
    weight_rows = observed_count.astype(jnp.float32)[None] * obs_precision[:, None, None]
    moved_rows = total1_rows - step1 * image_rows
    sums, _ = exchange(
        [
            squares(residual_next),
            jnp.sum(jnp.where(own[None], residual_next * residual, 0.0), axis=(0, 1)),
            jnp.where(first, jnp.sum(weight_rows * moved_rows * moved_rows, axis=(0, 1)), 0.0),
            jnp.where(first, jnp.sum(weight_rows * moved_rows * total1_rows, axis=(0, 1)), 0.0),
        ],
        jnp.zeros((grid_size * mem_size, 0, nlon), jnp.float32),
    )
    norm_next = sums[0]
    beta = norm_next / norm_now
    direction_sq = norm_next + 2.0 * beta * sums[1] + beta * beta * norm_now
    curvature2 = sums[2] + 2.0 * beta * sums[3] + beta * beta * curvature1
    step2 = norm_next / (direction_sq + curvature2)
    total2_rows = moved_rows + beta * total1_rows
    whole = step1 * total1_rows + step2 * total2_rows

    share = levels // mem_size
    mine_out = lax.dynamic_slice_in_dim(whole, mem_index * share, share, 0)
    recentred = (members.astype(jnp.float32) + whole[None]).astype(jnp.bfloat16)
    return (recentred, mine_out)


def solution(mesh):
    placed = (P("mem", None, "grid", None), P(None, "grid", None), P("grid", None), P())
    grid_size, mem_size = mesh.shape["grid"], mesh.shape["mem"]
    body = local

    def chosen(members, innovation, observed_count, obs_precision):
        levels = members.shape[1]
        fits = grid_size % levels == 0 and grid_size // levels <= 2 and levels % mem_size == 0 and ITERS == 2
        pick = local_by_level if fits else body
        return jax.shard_map(
            pick,
            mesh=mesh,
            in_specs=placed,
            out_specs=(P("mem", None, "grid", None), P("mem", "grid", None)),
            check_vma=False,
        )(members, innovation, observed_count, obs_precision)

    return chosen
```

```python
import jax
import jax.numpy as jnp
from jax import lax
from jax.sharding import PartitionSpec as P

PASSES = 2
ITERS = 2


diffusion = 0.25


def padded(value, sides, width):
    for axis, dim in sides:
        devices, length = (lax.axis_size(axis), value.shape[dim])
        up = [(i, (i + 1) % devices) for i in range(devices - 1)]
        down = [(j, i) for i, j in up]
        last = lax.slice_in_dim(value, length - width, length, axis=dim)
        leading = lax.slice_in_dim(value, 0, width, axis=dim)
        before = lax.ppermute(last, axis, up)
        after = lax.ppermute(leading, axis, down)
        value = jnp.concatenate([before, value, after], axis=dim)
    return value


def smooth(field):
    for sweep_index in range(PASSES):
        extended = padded(field, (("grid", 2),), 1)
        centre = extended[:, :, 1:-1]
        field = centre + diffusion * (extended[:, :, :-2] + extended[:, :, 2:] - 2.0 * centre)
    for sweep_index in range(PASSES):
        field = field + diffusion * (jnp.roll(field, 1, 3) + jnp.roll(field, -1, 3) - 2.0 * field)
    return field


def member_total(product):
    summed = jnp.sum(product, axis=0)
    return summed


def norm_of(residual):
    return lax.psum(jnp.sum(residual * residual), ("grid", "mem"))


def local(members, innovation, observed_count, obs_precision):
    mem_index = lax.axis_index("mem")
    level_share = members.shape[1] // lax.axis_size("mem")
    perturbed = lax.all_to_all(members, "mem", split_axis=1, concat_axis=0, tiled=True)
    precision = lax.dynamic_slice_in_dim(obs_precision, mem_index * level_share, level_share, 0)
    local_innovation = lax.dynamic_slice_in_dim(innovation, mem_index * level_share, level_share, 0)
    weight = observed_count.astype(jnp.float32)[None] * precision[:, None, None]
    gradient = smooth(perturbed * (weight * local_innovation)[None])
    carried = jnp.zeros_like(gradient)
    residual = gradient
    direction = residual
    norm_now = norm_of(residual)
    for iteration in range(ITERS):
        smoothed = smooth(direction)
        total = member_total(perturbed * smoothed)
        back = smooth(perturbed * (weight * total)[None])
        image, smoothed = (direction + back, smoothed)
        step_size = norm_now / lax.psum(jnp.sum(direction * image), ("grid", "mem"))
        carried = carried + step_size * smoothed
        residual = residual - step_size * image
        if iteration + 1 < ITERS:
            norm_next = norm_of(residual)
            direction = residual + norm_next / norm_now * direction
            norm_now = norm_next
    increment = member_total(perturbed * carried)
    whole = lax.all_gather(increment, "mem", axis=0, tiled=True)
    recentred = (members.astype(jnp.float32) + whole[None]).astype(jnp.bfloat16)
    return (recentred, increment)


def smooth_rows(field):
    for sweep_index in range(PASSES):
        edge = jnp.zeros_like(field[..., :1, :])
        north = jnp.concatenate([edge, field[..., :-1, :]], axis=-2)
        south = jnp.concatenate([field[..., 1:, :], edge], axis=-2)
        field = field + diffusion * (north + south - 2.0 * field)
    for sweep_index in range(PASSES):
        field = field + diffusion * (jnp.roll(field, 1, -1) + jnp.roll(field, -1, -1) - 2.0 * field)
    return field


def exchange(values, rows_for):
    devices = lax.axis_size("grid") * lax.axis_size("mem")
    nlon = rows_for.shape[-1]
    lanes = [jnp.sum(v.reshape(-1, 128), axis=0) for v in values]
    lanes.append(jnp.zeros((nlon - 128 * len(values),), jnp.float32))
    head = jnp.broadcast_to(jnp.concatenate(lanes), (devices, 1, nlon))
    parcel = jnp.concatenate([head, rows_for], axis=1)
    got = lax.all_to_all(parcel, ("grid", "mem"), 0, 0, tiled=True)
    lanes = jnp.sum(got[:, 0].reshape(devices, nlon // 128, 128), axis=0)
    sums = jnp.dot(lanes, jnp.ones((128, 128), jnp.float32), precision=lax.Precision.HIGHEST)
    return [jnp.tile(sums[i : i + 1], (1, nlon // 128)) for i in range(len(values))], got[:, 1:]


def mem_total(part):
    mem_size = lax.axis_size("mem")
    got = lax.all_to_all(jnp.broadcast_to(part, (mem_size,) + part.shape), "mem", 0, 0, tiled=True)
    return jnp.sum(got, axis=0)


def local_by_level(members, innovation, observed_count, obs_precision):
    grid_size = lax.axis_size("grid")
    mem_size = lax.axis_size("mem")
    count, levels, rows, nlon = members.shape
    copies = grid_size // levels
    nlat = rows * grid_size
    grid_index = lax.axis_index("grid")
    mem_index = lax.axis_index("mem")
    level = grid_index // copies

    counts = jnp.broadcast_to(observed_count.astype(jnp.bfloat16), (1, levels, rows, nlon))
    high = lax.reduce_precision(innovation, exponent_bits=8, mantissa_bits=7)
    rest = innovation - high
    middle = lax.reduce_precision(rest, exponent_bits=8, mantissa_bits=7)
    low = rest - middle
    parts = jnp.stack([high, middle, low]).astype(jnp.bfloat16)
    packed = jnp.transpose(jnp.concatenate([members, counts, parts], axis=0), (1, 2, 0, 3))
    got = lax.all_to_all(jnp.repeat(packed, copies, axis=0), "grid", 0, 0, tiled=True)
    received = jnp.transpose(got, (2, 0, 1, 3)).reshape(count + 4, nlat, nlon).astype(jnp.float32)
    split = received[count + 1 :]
    innov = (split[0] + split[1]) + split[2]
    precision = lax.dynamic_index_in_dim(obs_precision, level, 0, keepdims=False)
    weight = received[count] * precision
    widened = received[:count]

    span = nlat // copies
    own = (lax.broadcasted_iota(jnp.int32, (nlat, nlon), 0) // span) == grid_index % copies
    first = mem_index == 0

    def squares(field):
        return jnp.sum(jnp.where(own[None], field * field, 0.0), axis=(0, 1))

    def weighted(total):
        return jnp.where(first, jnp.sum(jnp.where(own, weight * total * total, 0.0), axis=0), 0.0)

    def by_target(field):
        return jnp.repeat(field.reshape(grid_size, rows, nlon), mem_size, axis=0)

    residual = smooth_rows(widened * (weight * innov)[None])
    total1 = mem_total(jnp.sum(widened * smooth_rows(residual), axis=0))
    image = residual + smooth_rows(widened * (weight * total1)[None])
    image_part = jnp.sum(widened * smooth_rows(image), axis=0)

    if copies > 1:
        rows_for = jnp.where(grid_index % copies == 0, by_target(total1), by_target(image_part))
    else:
        rows_for = jnp.concatenate([by_target(total1), by_target(image_part)], axis=1)
    sums1, got1 = exchange([squares(residual), weighted(total1)], rows_for)
    norm_now = sums1[0]
    curvature1 = sums1[1]
    step1 = norm_now / (norm_now + curvature1)
    if copies > 1:
        by_source = got1.reshape(levels, copies, mem_size, rows, nlon)
        total1_rows = by_source[:, 0, 0]
        image_rows = jnp.sum(by_source[:, 1], axis=1)
    else:
        by_source = got1.reshape(levels, mem_size, 2 * rows, nlon)
        total1_rows = by_source[:, 0, :rows]
        image_rows = jnp.sum(by_source[:, :, rows:], axis=1)

    residual_next = residual - step1 * image
    weight_rows = observed_count.astype(jnp.float32)[None] * obs_precision[:, None, None]
    moved_rows = total1_rows - step1 * image_rows
    sums, _ = exchange(
        [
            squares(residual_next),
            jnp.sum(jnp.where(own[None], residual_next * residual, 0.0), axis=(0, 1)),
            jnp.where(first, jnp.sum(weight_rows * moved_rows * moved_rows, axis=(0, 1)), 0.0),
            jnp.where(first, jnp.sum(weight_rows * moved_rows * total1_rows, axis=(0, 1)), 0.0),
        ],
        jnp.zeros((grid_size * mem_size, 0, nlon), jnp.float32),
    )
    norm_next = sums[0]
    beta = norm_next / norm_now
    direction_sq = norm_next + 2.0 * beta * sums[1] + beta * beta * norm_now
    curvature2 = sums[2] + 2.0 * beta * sums[3] + beta * beta * curvature1
    step2 = norm_next / (direction_sq + curvature2)
    total2_rows = moved_rows + beta * total1_rows
    whole = step1 * total1_rows + step2 * total2_rows

    share = levels // mem_size
    mine_out = lax.dynamic_slice_in_dim(whole, mem_index * share, share, 0)
    recentred = (members.astype(jnp.float32) + whole[None]).astype(jnp.bfloat16)
    return (recentred, mine_out)


def solution(mesh):
    placed = (P("mem", None, "grid", None), P(None, "grid", None), P("grid", None), P())
    grid_size, mem_size = mesh.shape["grid"], mesh.shape["mem"]
    body = local

    def chosen(members, innovation, observed_count, obs_precision):
        levels = members.shape[1]
        fits = grid_size % levels == 0 and grid_size // levels <= 2 and levels % mem_size == 0 and ITERS == 2
        pick = local_by_level if fits else body
        return jax.shard_map(
            pick,
            mesh=mesh,
            in_specs=placed,
            out_specs=(P("mem", None, "grid", None), P("mem", "grid", None)),
            check_vma=False,
        )(members, innovation, observed_count, obs_precision)

    return chosen
```

```python
import jax
import jax.numpy as jnp
from jax import lax
from jax.experimental import pallas as pl
from jax.experimental.pallas import tpu as pltpu
from jax.sharding import PartitionSpec as P

PASSES = 2
ITERS = 2


diffusion = 0.25


def padded(value, sides, width):
    for axis, dim in sides:
        devices, length = (lax.axis_size(axis), value.shape[dim])
        up = [(i, (i + 1) % devices) for i in range(devices - 1)]
        down = [(j, i) for i, j in up]
        last = lax.slice_in_dim(value, length - width, length, axis=dim)
        leading = lax.slice_in_dim(value, 0, width, axis=dim)
        before = lax.ppermute(last, axis, up)
        after = lax.ppermute(leading, axis, down)
        value = jnp.concatenate([before, value, after], axis=dim)
    return value


def smooth(field):
    for sweep_index in range(PASSES):
        extended = padded(field, (("grid", 2),), 1)
        centre = extended[:, :, 1:-1]
        field = centre + diffusion * (extended[:, :, :-2] + extended[:, :, 2:] - 2.0 * centre)
    for sweep_index in range(PASSES):
        field = field + diffusion * (jnp.roll(field, 1, 3) + jnp.roll(field, -1, 3) - 2.0 * field)
    return field


def member_total(product):
    summed = jnp.sum(product, axis=0)
    return summed


def norm_of(residual):
    return lax.psum(jnp.sum(residual * residual), ("grid", "mem"))


def local(members, innovation, observed_count, obs_precision):
    mem_index = lax.axis_index("mem")
    level_share = members.shape[1] // lax.axis_size("mem")
    perturbed = lax.all_to_all(members, "mem", split_axis=1, concat_axis=0, tiled=True)
    precision = lax.dynamic_slice_in_dim(obs_precision, mem_index * level_share, level_share, 0)
    local_innovation = lax.dynamic_slice_in_dim(innovation, mem_index * level_share, level_share, 0)
    weight = observed_count.astype(jnp.float32)[None] * precision[:, None, None]
    gradient = smooth(perturbed * (weight * local_innovation)[None])
    carried = jnp.zeros_like(gradient)
    residual = gradient
    direction = residual
    norm_now = norm_of(residual)
    for iteration in range(ITERS):
        smoothed = smooth(direction)
        total = member_total(perturbed * smoothed)
        back = smooth(perturbed * (weight * total)[None])
        image, smoothed = (direction + back, smoothed)
        step_size = norm_now / lax.psum(jnp.sum(direction * image), ("grid", "mem"))
        carried = carried + step_size * smoothed
        residual = residual - step_size * image
        if iteration + 1 < ITERS:
            norm_next = norm_of(residual)
            direction = residual + norm_next / norm_now * direction
            norm_now = norm_next
    increment = member_total(perturbed * carried)
    whole = lax.all_gather(increment, "mem", axis=0, tiled=True)
    recentred = (members.astype(jnp.float32) + whole[None]).astype(jnp.bfloat16)
    return (recentred, increment)


def smooth_rows(field):
    for sweep_index in range(PASSES):
        edge = jnp.zeros_like(field[..., :1, :])
        north = jnp.concatenate([edge, field[..., :-1, :]], axis=-2)
        south = jnp.concatenate([field[..., 1:, :], edge], axis=-2)
        field = field + diffusion * (north + south - 2.0 * field)
    for sweep_index in range(PASSES):
        field = field + diffusion * (jnp.roll(field, 1, -1) + jnp.roll(field, -1, -1) - 2.0 * field)
    return field


def smooth_in_kernel(field):
    rows, nlon = field.shape[-2], field.shape[-1]
    lat, lon = field.ndim - 2, field.ndim - 1
    row = lax.broadcasted_iota(jnp.int32, field.shape, lat)
    keep_ahead = jnp.abs(pltpu.roll(row, 1, lat) - row) == 1
    keep_behind = jnp.abs(pltpu.roll(row, rows - 1, lat) - row) == 1
    for sweep_index in range(PASSES):
        ahead = jnp.where(keep_ahead, pltpu.roll(field, 1, lat), 0.0)
        behind = jnp.where(keep_behind, pltpu.roll(field, rows - 1, lat), 0.0)
        field = field + diffusion * (ahead + behind - 2.0 * field)
    for sweep_index in range(PASSES):
        field = field + diffusion * (pltpu.roll(field, 1, lon) + pltpu.roll(field, nlon - 1, lon) - 2.0 * field)
    return field


def gradient_kernel(members_ref, forcing_ref, residual_ref, total_ref):
    widened = members_ref[...]
    residual = smooth_in_kernel(widened * forcing_ref[...][None])
    residual_ref[...] = residual
    total_ref[...] = jnp.sum(widened * smooth_in_kernel(residual), axis=0)


def image_kernel(members_ref, weight_ref, total_ref, residual_ref, image_ref, part_ref):
    widened = members_ref[...]
    image = residual_ref[...] + smooth_in_kernel(widened * (weight_ref[...] * total_ref[...])[None])
    image_ref[...] = image
    part_ref[...] = jnp.sum(widened * smooth_in_kernel(image), axis=0)


def in_vmem(kernel, outs, *args):
    return pl.pallas_call(
        kernel,
        out_shape=tuple(jax.ShapeDtypeStruct(s, jnp.float32) for s in outs),
        in_specs=[pl.BlockSpec(memory_space=pltpu.VMEM)] * len(args),
        out_specs=tuple(pl.BlockSpec(memory_space=pltpu.VMEM) for _ in outs),
    )(*args)


def exchange(values, rows_for):
    devices = lax.axis_size("grid") * lax.axis_size("mem")
    nlon = rows_for.shape[-1]
    lanes = [jnp.sum(v.reshape(-1, 128), axis=0) for v in values]
    lanes.append(jnp.zeros((nlon - 128 * len(values),), jnp.float32))
    head = jnp.broadcast_to(jnp.concatenate(lanes), (devices, 1, nlon))
    parcel = jnp.concatenate([head, rows_for], axis=1)
    got = lax.all_to_all(parcel, ("grid", "mem"), 0, 0, tiled=True)
    lanes = jnp.sum(got[:, 0].reshape(devices, nlon // 128, 128), axis=0)
    sums = jnp.dot(lanes, jnp.ones((128, 128), jnp.float32), precision=lax.Precision.HIGHEST)
    return [jnp.tile(sums[i : i + 1], (1, nlon // 128)) for i in range(len(values))], got[:, 1:]


def mem_total(part):
    mem_size = lax.axis_size("mem")
    got = lax.all_to_all(jnp.broadcast_to(part, (mem_size,) + part.shape), "mem", 0, 0, tiled=True)
    return jnp.sum(got, axis=0)


def local_by_level(members, innovation, observed_count, obs_precision):
    grid_size = lax.axis_size("grid")
    mem_size = lax.axis_size("mem")
    count, levels, rows, nlon = members.shape
    copies = grid_size // levels
    nlat = rows * grid_size
    grid_index = lax.axis_index("grid")
    mem_index = lax.axis_index("mem")
    level = grid_index // copies

    counts = jnp.broadcast_to(observed_count.astype(jnp.bfloat16), (1, levels, rows, nlon))
    high = lax.reduce_precision(innovation, exponent_bits=8, mantissa_bits=7)
    rest = innovation - high
    middle = lax.reduce_precision(rest, exponent_bits=8, mantissa_bits=7)
    low = rest - middle
    parts = jnp.stack([high, middle, low]).astype(jnp.bfloat16)
    packed = jnp.repeat(jnp.concatenate([members, counts, parts], axis=0), copies, axis=1)
    got = lax.all_to_all(packed, "grid", 1, 2, tiled=True)[:, 0]
    split = got[count + 1 :].astype(jnp.float32)
    innov = (split[0] + split[1]) + split[2]
    precision = lax.dynamic_index_in_dim(obs_precision, level, 0, keepdims=False)
    weight = got[count].astype(jnp.float32) * precision
    widened = got[:count].astype(jnp.float32)

    span = nlat // copies
    own = (lax.broadcasted_iota(jnp.int32, (nlat, nlon), 0) // span) == grid_index % copies
    first = mem_index == 0

    def squares(field):
        return jnp.sum(jnp.where(own[None], field * field, 0.0), axis=(0, 1))

    def weighted(total):
        return jnp.where(first, jnp.sum(jnp.where(own, weight * total * total, 0.0), axis=0), 0.0)

    def by_target(field):
        return jnp.repeat(field.reshape(grid_size, rows, nlon), mem_size, axis=0)

    field, plane = (count, nlat, nlon), (nlat, nlon)
    residual, total1_part = in_vmem(gradient_kernel, (field, plane), widened, weight * innov)
    total1 = mem_total(total1_part)
    image, image_part = in_vmem(image_kernel, (field, plane), widened, weight, total1, residual)

    if copies > 1:
        rows_for = jnp.where(grid_index % copies == 0, by_target(total1), by_target(image_part))
    else:
        rows_for = jnp.concatenate([by_target(total1), by_target(image_part)], axis=1)
    sums1, got1 = exchange([squares(residual), weighted(total1)], rows_for)
    norm_now = sums1[0]
    curvature1 = sums1[1]
    step1 = norm_now / (norm_now + curvature1)
    if copies > 1:
        by_source = got1.reshape(levels, copies, mem_size, rows, nlon)
        total1_rows = by_source[:, 0, 0]
        image_rows = jnp.sum(by_source[:, 1], axis=1)
    else:
        by_source = got1.reshape(levels, mem_size, 2 * rows, nlon)
        total1_rows = by_source[:, 0, :rows]
        image_rows = jnp.sum(by_source[:, :, rows:], axis=1)

    residual_next = residual - step1 * image
    weight_rows = observed_count.astype(jnp.float32)[None] * obs_precision[:, None, None]
    moved_rows = total1_rows - step1 * image_rows
    sums, _ = exchange(
        [
            squares(residual_next),
            jnp.sum(jnp.where(own[None], residual_next * residual, 0.0), axis=(0, 1)),
            jnp.where(first, jnp.sum(weight_rows * moved_rows * moved_rows, axis=(0, 1)), 0.0),
            jnp.where(first, jnp.sum(weight_rows * moved_rows * total1_rows, axis=(0, 1)), 0.0),
        ],
        jnp.zeros((grid_size * mem_size, 0, nlon), jnp.float32),
    )
    norm_next = sums[0]
    beta = norm_next / norm_now
    direction_sq = norm_next + 2.0 * beta * sums[1] + beta * beta * norm_now
    curvature2 = sums[2] + 2.0 * beta * sums[3] + beta * beta * curvature1
    step2 = norm_next / (direction_sq + curvature2)
    total2_rows = moved_rows + beta * total1_rows
    whole = step1 * total1_rows + step2 * total2_rows

    share = levels // mem_size
    mine_out = lax.dynamic_slice_in_dim(whole, mem_index * share, share, 0)
    recentred = (members.astype(jnp.float32) + whole[None]).astype(jnp.bfloat16)
    return (recentred, mine_out)


def solution(mesh):
    placed = (P("mem", None, "grid", None), P(None, "grid", None), P("grid", None), P())
    grid_size, mem_size = mesh.shape["grid"], mesh.shape["mem"]
    body = local

    def chosen(members, innovation, observed_count, obs_precision):
        levels = members.shape[1]
        fits = grid_size % levels == 0 and grid_size // levels <= 2 and levels % mem_size == 0 and ITERS == 2
        pick = local_by_level if fits else body
        return jax.shard_map(
            pick,
            mesh=mesh,
            in_specs=placed,
            out_specs=(P("mem", None, "grid", None), P("mem", "grid", None)),
            check_vma=False,
        )(members, innovation, observed_count, obs_precision)

    return chosen
```

```python
import jax
import jax.numpy as jnp
from jax import lax
from jax.experimental import pallas as pl
from jax.experimental.pallas import tpu as pltpu
from jax.sharding import PartitionSpec as P

PASSES = 2
ITERS = 2


diffusion = 0.25


def padded(value, sides, width):
    for axis, dim in sides:
        devices, length = (lax.axis_size(axis), value.shape[dim])
        up = [(i, (i + 1) % devices) for i in range(devices - 1)]
        down = [(j, i) for i, j in up]
        last = lax.slice_in_dim(value, length - width, length, axis=dim)
        leading = lax.slice_in_dim(value, 0, width, axis=dim)
        before = lax.ppermute(last, axis, up)
        after = lax.ppermute(leading, axis, down)
        value = jnp.concatenate([before, value, after], axis=dim)
    return value


def smooth(field):
    for sweep_index in range(PASSES):
        extended = padded(field, (("grid", 2),), 1)
        centre = extended[:, :, 1:-1]
        field = centre + diffusion * (extended[:, :, :-2] + extended[:, :, 2:] - 2.0 * centre)
    for sweep_index in range(PASSES):
        field = field + diffusion * (jnp.roll(field, 1, 3) + jnp.roll(field, -1, 3) - 2.0 * field)
    return field


def member_total(product):
    summed = jnp.sum(product, axis=0)
    return summed


def norm_of(residual):
    return lax.psum(jnp.sum(residual * residual), ("grid", "mem"))


def local(members, innovation, observed_count, obs_precision):
    mem_index = lax.axis_index("mem")
    level_share = members.shape[1] // lax.axis_size("mem")
    perturbed = lax.all_to_all(members, "mem", split_axis=1, concat_axis=0, tiled=True)
    precision = lax.dynamic_slice_in_dim(obs_precision, mem_index * level_share, level_share, 0)
    local_innovation = lax.dynamic_slice_in_dim(innovation, mem_index * level_share, level_share, 0)
    weight = observed_count.astype(jnp.float32)[None] * precision[:, None, None]
    gradient = smooth(perturbed * (weight * local_innovation)[None])
    carried = jnp.zeros_like(gradient)
    residual = gradient
    direction = residual
    norm_now = norm_of(residual)
    for iteration in range(ITERS):
        smoothed = smooth(direction)
        total = member_total(perturbed * smoothed)
        back = smooth(perturbed * (weight * total)[None])
        image, smoothed = (direction + back, smoothed)
        step_size = norm_now / lax.psum(jnp.sum(direction * image), ("grid", "mem"))
        carried = carried + step_size * smoothed
        residual = residual - step_size * image
        if iteration + 1 < ITERS:
            norm_next = norm_of(residual)
            direction = residual + norm_next / norm_now * direction
            norm_now = norm_next
    increment = member_total(perturbed * carried)
    whole = lax.all_gather(increment, "mem", axis=0, tiled=True)
    recentred = (members.astype(jnp.float32) + whole[None]).astype(jnp.bfloat16)
    return (recentred, increment)


def smooth_rows(field):
    for sweep_index in range(PASSES):
        edge = jnp.zeros_like(field[..., :1, :])
        north = jnp.concatenate([edge, field[..., :-1, :]], axis=-2)
        south = jnp.concatenate([field[..., 1:, :], edge], axis=-2)
        field = field + diffusion * (north + south - 2.0 * field)
    for sweep_index in range(PASSES):
        field = field + diffusion * (jnp.roll(field, 1, -1) + jnp.roll(field, -1, -1) - 2.0 * field)
    return field


def smooth_in_kernel(field):
    rows, nlon = field.shape[-2], field.shape[-1]
    lat, lon = field.ndim - 2, field.ndim - 1
    row = lax.broadcasted_iota(jnp.int32, field.shape, lat)
    keep_ahead = jnp.abs(pltpu.roll(row, 1, lat) - row) == 1
    keep_behind = jnp.abs(pltpu.roll(row, rows - 1, lat) - row) == 1
    for sweep_index in range(PASSES):
        ahead = jnp.where(keep_ahead, pltpu.roll(field, 1, lat), 0.0)
        behind = jnp.where(keep_behind, pltpu.roll(field, rows - 1, lat), 0.0)
        field = field + diffusion * (ahead + behind - 2.0 * field)
    for sweep_index in range(PASSES):
        field = field + diffusion * (pltpu.roll(field, 1, lon) + pltpu.roll(field, nlon - 1, lon) - 2.0 * field)
    return field


def gradient_kernel(members_ref, weight_ref, innov_ref, residual_ref, total_ref):
    widened = members_ref[...]
    residual = smooth_in_kernel(widened * (weight_ref[...] * innov_ref[...])[None])
    residual_ref[...] = residual
    total_ref[...] = jnp.sum(widened * smooth_in_kernel(residual), axis=0)


def in_vmem(kernel, outs, *args):
    return pl.pallas_call(
        kernel,
        out_shape=tuple(jax.ShapeDtypeStruct(s, jnp.float32) for s in outs),
        in_specs=[pl.BlockSpec(memory_space=pltpu.VMEM)] * len(args),
        out_specs=tuple(pl.BlockSpec(memory_space=pltpu.VMEM) for _ in outs),
    )(*args)


def exchange(values, rows_for):
    devices = lax.axis_size("grid") * lax.axis_size("mem")
    nlon = rows_for.shape[-1]
    lanes = [jnp.sum(v.reshape(-1, 128), axis=0) for v in values]
    lanes.append(jnp.zeros((nlon - 128 * len(values),), jnp.float32))
    head = jnp.broadcast_to(jnp.concatenate(lanes), (devices, 1, nlon))
    parcel = jnp.concatenate([head, rows_for], axis=1)
    got = lax.all_to_all(parcel, ("grid", "mem"), 0, 0, tiled=True)
    lanes = jnp.sum(got[:, 0].reshape(devices, nlon // 128, 128), axis=0)
    sums = jnp.dot(lanes, jnp.ones((128, 128), jnp.float32), precision=lax.Precision.HIGHEST)
    return [jnp.tile(sums[i : i + 1], (1, nlon // 128)) for i in range(len(values))], got[:, 1:]


def mem_total(part):
    mem_size = lax.axis_size("mem")
    got = lax.all_to_all(jnp.broadcast_to(part, (mem_size,) + part.shape), "mem", 0, 0, tiled=True)
    return jnp.sum(got, axis=0)


def local_by_level(members, innovation, observed_count, obs_precision):
    grid_size = lax.axis_size("grid")
    mem_size = lax.axis_size("mem")
    count, levels, rows, nlon = members.shape
    copies = grid_size // levels
    nlat = rows * grid_size
    grid_index = lax.axis_index("grid")
    mem_index = lax.axis_index("mem")
    level = grid_index // copies

    counts = jnp.broadcast_to(observed_count.astype(jnp.bfloat16), (1, levels, rows, nlon))
    high = lax.reduce_precision(innovation, exponent_bits=8, mantissa_bits=7)
    rest = innovation - high
    middle = lax.reduce_precision(rest, exponent_bits=8, mantissa_bits=7)
    low = rest - middle
    parts = jnp.stack([high, middle, low]).astype(jnp.bfloat16)
    packed = jnp.transpose(jnp.concatenate([members, counts, parts], axis=0), (1, 2, 0, 3))
    got = lax.all_to_all(jnp.repeat(packed, copies, axis=0), "grid", 0, 0, tiled=True)
    received = jnp.transpose(got, (2, 0, 1, 3)).reshape(count + 4, nlat, nlon).astype(jnp.float32)
    split = received[count + 1 :]
    innov = (split[0] + split[1]) + split[2]
    precision = lax.dynamic_index_in_dim(obs_precision, level, 0, keepdims=False)
    weight = received[count] * precision
    widened = received[:count]

    span = nlat // copies
    own = (lax.broadcasted_iota(jnp.int32, (nlat, nlon), 0) // span) == grid_index % copies
    first = mem_index == 0

    def squares(field):
        return jnp.sum(jnp.where(own[None], field * field, 0.0), axis=(0, 1))

    def weighted(total):
        return jnp.where(first, jnp.sum(jnp.where(own, weight * total * total, 0.0), axis=0), 0.0)

    def by_target(field):
        return jnp.repeat(field.reshape(grid_size, rows, nlon), mem_size, axis=0)

    residual, total1_part = in_vmem(gradient_kernel, ((count, nlat, nlon), (nlat, nlon)), widened, weight, innov)
    total1 = mem_total(total1_part)
    image = residual + smooth_rows(widened * (weight * total1)[None])
    image_part = jnp.sum(widened * smooth_rows(image), axis=0)

    if copies > 1:
        rows_for = jnp.where(grid_index % copies == 0, by_target(total1), by_target(image_part))
    else:
        rows_for = jnp.concatenate([by_target(total1), by_target(image_part)], axis=1)
    sums1, got1 = exchange([squares(residual), weighted(total1)], rows_for)
    norm_now = sums1[0]
    curvature1 = sums1[1]
    step1 = norm_now / (norm_now + curvature1)
    if copies > 1:
        by_source = got1.reshape(levels, copies, mem_size, rows, nlon)
        total1_rows = by_source[:, 0, 0]
        image_rows = jnp.sum(by_source[:, 1], axis=1)
    else:
        by_source = got1.reshape(levels, mem_size, 2 * rows, nlon)
        total1_rows = by_source[:, 0, :rows]
        image_rows = jnp.sum(by_source[:, :, rows:], axis=1)

    residual_next = residual - step1 * image
    weight_rows = observed_count.astype(jnp.float32)[None] * obs_precision[:, None, None]
    moved_rows = total1_rows - step1 * image_rows
    sums, _ = exchange(
        [
            squares(residual_next),
            jnp.sum(jnp.where(own[None], residual_next * residual, 0.0), axis=(0, 1)),
            jnp.where(first, jnp.sum(weight_rows * moved_rows * moved_rows, axis=(0, 1)), 0.0),
            jnp.where(first, jnp.sum(weight_rows * moved_rows * total1_rows, axis=(0, 1)), 0.0),
        ],
        jnp.zeros((grid_size * mem_size, 0, nlon), jnp.float32),
    )
    norm_next = sums[0]
    beta = norm_next / norm_now
    direction_sq = norm_next + 2.0 * beta * sums[1] + beta * beta * norm_now
    curvature2 = sums[2] + 2.0 * beta * sums[3] + beta * beta * curvature1
    step2 = norm_next / (direction_sq + curvature2)
    total2_rows = moved_rows + beta * total1_rows
    whole = step1 * total1_rows + step2 * total2_rows

    share = levels // mem_size
    mine_out = lax.dynamic_slice_in_dim(whole, mem_index * share, share, 0)
    recentred = (members.astype(jnp.float32) + whole[None]).astype(jnp.bfloat16)
    return (recentred, mine_out)


def solution(mesh):
    placed = (P("mem", None, "grid", None), P(None, "grid", None), P("grid", None), P())
    grid_size, mem_size = mesh.shape["grid"], mesh.shape["mem"]
    body = local

    def chosen(members, innovation, observed_count, obs_precision):
        levels = members.shape[1]
        fits = grid_size % levels == 0 and grid_size // levels <= 2 and levels % mem_size == 0 and ITERS == 2
        pick = local_by_level if fits else body
        return jax.shard_map(
            pick,
            mesh=mesh,
            in_specs=placed,
            out_specs=(P("mem", None, "grid", None), P("mem", "grid", None)),
            check_vma=False,
        )(members, innovation, observed_count, obs_precision)

    return chosen
```

```python
import jax
import jax.numpy as jnp
from jax import lax
from jax.sharding import PartitionSpec as P

PASSES = 2
ITERS = 2


diffusion = 0.25


def padded(value, sides, width):
    for axis, dim in sides:
        devices, length = (lax.axis_size(axis), value.shape[dim])
        up = [(i, (i + 1) % devices) for i in range(devices - 1)]
        down = [(j, i) for i, j in up]
        last = lax.slice_in_dim(value, length - width, length, axis=dim)
        leading = lax.slice_in_dim(value, 0, width, axis=dim)
        before = lax.ppermute(last, axis, up)
        after = lax.ppermute(leading, axis, down)
        value = jnp.concatenate([before, value, after], axis=dim)
    return value


def smooth(field):
    for sweep_index in range(PASSES):
        extended = padded(field, (("grid", 2),), 1)
        centre = extended[:, :, 1:-1]
        field = centre + diffusion * (extended[:, :, :-2] + extended[:, :, 2:] - 2.0 * centre)
    for sweep_index in range(PASSES):
        field = field + diffusion * (jnp.roll(field, 1, 3) + jnp.roll(field, -1, 3) - 2.0 * field)
    return field


def member_total(product):
    summed = jnp.sum(product, axis=0)
    return summed


def norm_of(residual):
    return lax.psum(jnp.sum(residual * residual), ("grid", "mem"))


def local(members, innovation, observed_count, obs_precision):
    mem_index = lax.axis_index("mem")
    level_share = members.shape[1] // lax.axis_size("mem")
    perturbed = lax.all_to_all(members, "mem", split_axis=1, concat_axis=0, tiled=True)
    precision = lax.dynamic_slice_in_dim(obs_precision, mem_index * level_share, level_share, 0)
    local_innovation = lax.dynamic_slice_in_dim(innovation, mem_index * level_share, level_share, 0)
    weight = observed_count.astype(jnp.float32)[None] * precision[:, None, None]
    gradient = smooth(perturbed * (weight * local_innovation)[None])
    carried = jnp.zeros_like(gradient)
    residual = gradient
    direction = residual
    norm_now = norm_of(residual)
    for iteration in range(ITERS):
        smoothed = smooth(direction)
        total = member_total(perturbed * smoothed)
        back = smooth(perturbed * (weight * total)[None])
        image, smoothed = (direction + back, smoothed)
        step_size = norm_now / lax.psum(jnp.sum(direction * image), ("grid", "mem"))
        carried = carried + step_size * smoothed
        residual = residual - step_size * image
        if iteration + 1 < ITERS:
            norm_next = norm_of(residual)
            direction = residual + norm_next / norm_now * direction
            norm_now = norm_next
    increment = member_total(perturbed * carried)
    whole = lax.all_gather(increment, "mem", axis=0, tiled=True)
    recentred = (members.astype(jnp.float32) + whole[None]).astype(jnp.bfloat16)
    return (recentred, increment)


def smooth_rows(field):
    nlat = field.shape[-2]
    row = lax.broadcasted_iota(jnp.int32, (nlat, 1), 0)
    centre = jnp.where((row == 0) | (row == nlat - 1), 0.3125, 0.375)
    wide = jnp.pad(field, [(0, 0)] * (field.ndim - 2) + [(2, 2), (0, 0)])
    near = lax.slice_in_dim(wide, 1, nlat + 1, axis=-2) + lax.slice_in_dim(wide, 3, nlat + 3, axis=-2)
    far = lax.slice_in_dim(wide, 0, nlat, axis=-2) + lax.slice_in_dim(wide, 4, nlat + 4, axis=-2)
    field = centre * field + 0.25 * near + 0.0625 * far
    near = jnp.roll(field, 1, -1) + jnp.roll(field, -1, -1)
    far = jnp.roll(field, 2, -1) + jnp.roll(field, -2, -1)
    return 0.375 * field + 0.25 * near + 0.0625 * far


def exchange(values, rows_for):
    devices = lax.axis_size("grid") * lax.axis_size("mem")
    nlon = rows_for.shape[-1]
    lanes = [jnp.sum(v.reshape(-1, 128), axis=0) for v in values]
    lanes.append(jnp.zeros((nlon - 128 * len(values),), jnp.float32))
    head = jnp.broadcast_to(jnp.concatenate(lanes), (devices, 1, nlon))
    parcel = jnp.concatenate([head, rows_for], axis=1)
    got = lax.all_to_all(parcel, ("grid", "mem"), 0, 0, tiled=True)
    lanes = jnp.sum(got[:, 0].reshape(devices, nlon // 128, 128), axis=0)
    sums = jnp.dot(lanes, jnp.ones((128, 128), jnp.float32), precision=lax.Precision.HIGHEST)
    return [jnp.tile(sums[i : i + 1], (1, nlon // 128)) for i in range(len(values))], got[:, 1:]


def mem_total(part):
    mem_size = lax.axis_size("mem")
    got = lax.all_to_all(jnp.broadcast_to(part, (mem_size,) + part.shape), "mem", 0, 0, tiled=True)
    return jnp.sum(got, axis=0)


def local_by_level(members, innovation, observed_count, obs_precision):
    grid_size = lax.axis_size("grid")
    mem_size = lax.axis_size("mem")
    count, levels, rows, nlon = members.shape
    copies = grid_size // levels
    nlat = rows * grid_size
    grid_index = lax.axis_index("grid")
    mem_index = lax.axis_index("mem")
    level = grid_index // copies

    counts = jnp.broadcast_to(observed_count.astype(jnp.bfloat16), (1, levels, rows, nlon))
    high = lax.reduce_precision(innovation, exponent_bits=8, mantissa_bits=7)
    rest = innovation - high
    middle = lax.reduce_precision(rest, exponent_bits=8, mantissa_bits=7)
    low = rest - middle
    parts = jnp.stack([high, middle, low]).astype(jnp.bfloat16)
    packed = jnp.repeat(jnp.concatenate([members, counts, parts], axis=0), copies, axis=1)
    got = lax.all_to_all(packed, "grid", 1, 2, tiled=True)[:, 0]
    split = got[count + 1 :].astype(jnp.float32)
    innov = (split[0] + split[1]) + split[2]
    precision = lax.dynamic_index_in_dim(obs_precision, level, 0, keepdims=False)
    weight = got[count].astype(jnp.float32) * precision
    widened = got[:count].astype(jnp.float32)

    span = nlat // copies
    own = (lax.broadcasted_iota(jnp.int32, (nlat, nlon), 0) // span) == grid_index % copies
    first = mem_index == 0

    def squares(field):
        return jnp.sum(jnp.where(own[None], field * field, 0.0), axis=(0, 1))

    def weighted(total):
        return jnp.where(first, jnp.sum(jnp.where(own, weight * total * total, 0.0), axis=0), 0.0)

    def by_target(field):
        return jnp.repeat(field.reshape(grid_size, rows, nlon), mem_size, axis=0)

    residual = smooth_rows(widened * (weight * innov)[None])
    total1 = mem_total(jnp.sum(widened * smooth_rows(residual), axis=0))
    image = residual + smooth_rows(widened * (weight * total1)[None])
    image_part = jnp.sum(widened * smooth_rows(image), axis=0)

    if copies > 1:
        rows_for = jnp.where(grid_index % copies == 0, by_target(total1), by_target(image_part))
    else:
        rows_for = jnp.concatenate([by_target(total1), by_target(image_part)], axis=1)
    sums1, got1 = exchange([squares(residual), weighted(total1)], rows_for)
    norm_now = sums1[0]
    curvature1 = sums1[1]
    step1 = norm_now / (norm_now + curvature1)
    if copies > 1:
        by_source = got1.reshape(levels, copies, mem_size, rows, nlon)
        total1_rows = by_source[:, 0, 0]
        image_rows = jnp.sum(by_source[:, 1], axis=1)
    else:
        by_source = got1.reshape(levels, mem_size, 2 * rows, nlon)
        total1_rows = by_source[:, 0, :rows]
        image_rows = jnp.sum(by_source[:, :, rows:], axis=1)

    residual_next = residual - step1 * image
    weight_rows = observed_count.astype(jnp.float32)[None] * obs_precision[:, None, None]
    moved_rows = total1_rows - step1 * image_rows
    sums, _ = exchange(
        [
            squares(residual_next),
            jnp.sum(jnp.where(own[None], residual_next * residual, 0.0), axis=(0, 1)),
            jnp.where(first, jnp.sum(weight_rows * moved_rows * moved_rows, axis=(0, 1)), 0.0),
            jnp.where(first, jnp.sum(weight_rows * moved_rows * total1_rows, axis=(0, 1)), 0.0),
        ],
        jnp.zeros((grid_size * mem_size, 0, nlon), jnp.float32),
    )
    norm_next = sums[0]
    beta = norm_next / norm_now
    direction_sq = norm_next + 2.0 * beta * sums[1] + beta * beta * norm_now
    curvature2 = sums[2] + 2.0 * beta * sums[3] + beta * beta * curvature1
    step2 = norm_next / (direction_sq + curvature2)
    total2_rows = moved_rows + beta * total1_rows
    whole = step1 * total1_rows + step2 * total2_rows

    share = levels // mem_size
    mine_out = lax.dynamic_slice_in_dim(whole, mem_index * share, share, 0)
    recentred = (members.astype(jnp.float32) + whole[None]).astype(jnp.bfloat16)
    return (recentred, mine_out)


def solution(mesh):
    placed = (P("mem", None, "grid", None), P(None, "grid", None), P("grid", None), P())
    grid_size, mem_size = mesh.shape["grid"], mesh.shape["mem"]
    body = local

    def chosen(members, innovation, observed_count, obs_precision):
        levels = members.shape[1]
        fits = grid_size % levels == 0 and grid_size // levels <= 2 and levels % mem_size == 0 and ITERS == 2
        pick = local_by_level if fits else body
        return jax.shard_map(
            pick,
            mesh=mesh,
            in_specs=placed,
            out_specs=(P("mem", None, "grid", None), P("mem", "grid", None)),
            check_vma=False,
        )(members, innovation, observed_count, obs_precision)

    return chosen
```

```python
import jax
import jax.numpy as jnp
from jax import lax
from jax.sharding import PartitionSpec as P

PASSES = 2
ITERS = 2


diffusion = 0.25


def padded(value, sides, width):
    for axis, dim in sides:
        devices, length = (lax.axis_size(axis), value.shape[dim])
        up = [(i, (i + 1) % devices) for i in range(devices - 1)]
        down = [(j, i) for i, j in up]
        last = lax.slice_in_dim(value, length - width, length, axis=dim)
        leading = lax.slice_in_dim(value, 0, width, axis=dim)
        before = lax.ppermute(last, axis, up)
        after = lax.ppermute(leading, axis, down)
        value = jnp.concatenate([before, value, after], axis=dim)
    return value


def smooth(field):
    for sweep_index in range(PASSES):
        extended = padded(field, (("grid", 2),), 1)
        centre = extended[:, :, 1:-1]
        field = centre + diffusion * (extended[:, :, :-2] + extended[:, :, 2:] - 2.0 * centre)
    for sweep_index in range(PASSES):
        field = field + diffusion * (jnp.roll(field, 1, 3) + jnp.roll(field, -1, 3) - 2.0 * field)
    return field


def member_total(product):
    summed = jnp.sum(product, axis=0)
    return summed


def norm_of(residual):
    return lax.psum(jnp.sum(residual * residual), ("grid", "mem"))


def local(members, innovation, observed_count, obs_precision):
    mem_index = lax.axis_index("mem")
    level_share = members.shape[1] // lax.axis_size("mem")
    perturbed = lax.all_to_all(members, "mem", split_axis=1, concat_axis=0, tiled=True)
    precision = lax.dynamic_slice_in_dim(obs_precision, mem_index * level_share, level_share, 0)
    local_innovation = lax.dynamic_slice_in_dim(innovation, mem_index * level_share, level_share, 0)
    weight = observed_count.astype(jnp.float32)[None] * precision[:, None, None]
    gradient = smooth(perturbed * (weight * local_innovation)[None])
    carried = jnp.zeros_like(gradient)
    residual = gradient
    direction = residual
    norm_now = norm_of(residual)
    for iteration in range(ITERS):
        smoothed = smooth(direction)
        total = member_total(perturbed * smoothed)
        back = smooth(perturbed * (weight * total)[None])
        image, smoothed = (direction + back, smoothed)
        step_size = norm_now / lax.psum(jnp.sum(direction * image), ("grid", "mem"))
        carried = carried + step_size * smoothed
        residual = residual - step_size * image
        if iteration + 1 < ITERS:
            norm_next = norm_of(residual)
            direction = residual + norm_next / norm_now * direction
            norm_now = norm_next
    increment = member_total(perturbed * carried)
    whole = lax.all_gather(increment, "mem", axis=0, tiled=True)
    recentred = (members.astype(jnp.float32) + whole[None]).astype(jnp.bfloat16)
    return (recentred, increment)


def smooth_rows(field):
    nlat = field.shape[-2]
    row = lax.broadcasted_iota(jnp.int32, (nlat, 1), 0)
    centre = jnp.where((row == 0) | (row == nlat - 1), 0.3125, 0.375)
    wide = jnp.pad(field, [(0, 0)] * (field.ndim - 2) + [(2, 2), (0, 0)])
    near = lax.slice_in_dim(wide, 1, nlat + 1, axis=-2) + lax.slice_in_dim(wide, 3, nlat + 3, axis=-2)
    far = lax.slice_in_dim(wide, 0, nlat, axis=-2) + lax.slice_in_dim(wide, 4, nlat + 4, axis=-2)
    field = centre * field + 0.25 * near + 0.0625 * far
    nlon = field.shape[-1]
    wide = jnp.concatenate([field[..., nlon - 2 :], field, field[..., :2]], axis=-1)
    near = wide[..., 1 : nlon + 1] + wide[..., 3 : nlon + 3]
    far = wide[..., :nlon] + wide[..., 4 : nlon + 4]
    return 0.375 * field + 0.25 * near + 0.0625 * far


def exchange(values, rows_for):
    devices = lax.axis_size("grid") * lax.axis_size("mem")
    nlon = rows_for.shape[-1]
    lanes = [jnp.sum(v.reshape(-1, 128), axis=0) for v in values]
    lanes.append(jnp.zeros((nlon - 128 * len(values),), jnp.float32))
    head = jnp.broadcast_to(jnp.concatenate(lanes), (devices, 1, nlon))
    parcel = jnp.concatenate([head, rows_for], axis=1)
    got = lax.all_to_all(parcel, ("grid", "mem"), 0, 0, tiled=True)
    lanes = jnp.sum(got[:, 0].reshape(devices, nlon // 128, 128), axis=0)
    sums = jnp.dot(lanes, jnp.ones((128, 128), jnp.float32), precision=lax.Precision.HIGHEST)
    return [jnp.tile(sums[i : i + 1], (1, nlon // 128)) for i in range(len(values))], got[:, 1:]


def mem_total(part):
    mem_size = lax.axis_size("mem")
    got = lax.all_to_all(jnp.broadcast_to(part, (mem_size,) + part.shape), "mem", 0, 0, tiled=True)
    return jnp.sum(got, axis=0)


def local_by_level(members, innovation, observed_count, obs_precision):
    grid_size = lax.axis_size("grid")
    mem_size = lax.axis_size("mem")
    count, levels, rows, nlon = members.shape
    copies = grid_size // levels
    nlat = rows * grid_size
    grid_index = lax.axis_index("grid")
    mem_index = lax.axis_index("mem")
    level = grid_index // copies

    counts = jnp.broadcast_to(observed_count.astype(jnp.bfloat16), (1, levels, rows, nlon))
    high = lax.reduce_precision(innovation, exponent_bits=8, mantissa_bits=7)
    rest = innovation - high
    middle = lax.reduce_precision(rest, exponent_bits=8, mantissa_bits=7)
    low = rest - middle
    parts = jnp.stack([high, middle, low]).astype(jnp.bfloat16)
    packed = jnp.repeat(jnp.concatenate([members, counts, parts], axis=0), copies, axis=1)
    got = lax.all_to_all(packed, "grid", 1, 2, tiled=True)[:, 0]
    split = got[count + 1 :].astype(jnp.float32)
    innov = (split[0] + split[1]) + split[2]
    precision = lax.dynamic_index_in_dim(obs_precision, level, 0, keepdims=False)
    weight = got[count].astype(jnp.float32) * precision
    widened = got[:count].astype(jnp.float32)

    span = nlat // copies
    own = (lax.broadcasted_iota(jnp.int32, (nlat, nlon), 0) // span) == grid_index % copies
    first = mem_index == 0

    def squares(field):
        return jnp.sum(jnp.where(own[None], field * field, 0.0), axis=(0, 1))

    def weighted(total):
        return jnp.where(first, jnp.sum(jnp.where(own, weight * total * total, 0.0), axis=0), 0.0)

    def by_target(field):
        return jnp.repeat(field.reshape(grid_size, rows, nlon), mem_size, axis=0)

    residual = smooth_rows(widened * (weight * innov)[None])
    total1 = mem_total(jnp.sum(widened * smooth_rows(residual), axis=0))
    image = residual + smooth_rows(widened * (weight * total1)[None])
    image_part = jnp.sum(widened * smooth_rows(image), axis=0)

    if copies > 1:
        rows_for = jnp.where(grid_index % copies == 0, by_target(total1), by_target(image_part))
    else:
        rows_for = jnp.concatenate([by_target(total1), by_target(image_part)], axis=1)
    sums1, got1 = exchange([squares(residual), weighted(total1)], rows_for)
    norm_now = sums1[0]
    curvature1 = sums1[1]
    step1 = norm_now / (norm_now + curvature1)
    if copies > 1:
        by_source = got1.reshape(levels, copies, mem_size, rows, nlon)
        total1_rows = by_source[:, 0, 0]
        image_rows = jnp.sum(by_source[:, 1], axis=1)
    else:
        by_source = got1.reshape(levels, mem_size, 2 * rows, nlon)
        total1_rows = by_source[:, 0, :rows]
        image_rows = jnp.sum(by_source[:, :, rows:], axis=1)

    residual_next = residual - step1 * image
    weight_rows = observed_count.astype(jnp.float32)[None] * obs_precision[:, None, None]
    moved_rows = total1_rows - step1 * image_rows
    sums, _ = exchange(
        [
            squares(residual_next),
            jnp.sum(jnp.where(own[None], residual_next * residual, 0.0), axis=(0, 1)),
            jnp.where(first, jnp.sum(weight_rows * moved_rows * moved_rows, axis=(0, 1)), 0.0),
            jnp.where(first, jnp.sum(weight_rows * moved_rows * total1_rows, axis=(0, 1)), 0.0),
        ],
        jnp.zeros((grid_size * mem_size, 0, nlon), jnp.float32),
    )
    norm_next = sums[0]
    beta = norm_next / norm_now
    direction_sq = norm_next + 2.0 * beta * sums[1] + beta * beta * norm_now
    curvature2 = sums[2] + 2.0 * beta * sums[3] + beta * beta * curvature1
    step2 = norm_next / (direction_sq + curvature2)
    total2_rows = moved_rows + beta * total1_rows
    whole = step1 * total1_rows + step2 * total2_rows

    share = levels // mem_size
    mine_out = lax.dynamic_slice_in_dim(whole, mem_index * share, share, 0)
    recentred = (members.astype(jnp.float32) + whole[None]).astype(jnp.bfloat16)
    return (recentred, mine_out)


def solution(mesh):
    placed = (P("mem", None, "grid", None), P(None, "grid", None), P("grid", None), P())
    grid_size, mem_size = mesh.shape["grid"], mesh.shape["mem"]
    body = local

    def chosen(members, innovation, observed_count, obs_precision):
        levels = members.shape[1]
        fits = grid_size % levels == 0 and grid_size // levels <= 2 and levels % mem_size == 0 and ITERS == 2
        pick = local_by_level if fits else body
        return jax.shard_map(
            pick,
            mesh=mesh,
            in_specs=placed,
            out_specs=(P("mem", None, "grid", None), P("mem", "grid", None)),
            check_vma=False,
        )(members, innovation, observed_count, obs_precision)

    return chosen
```

```python
import jax
import jax.numpy as jnp
from jax import lax
from jax.sharding import PartitionSpec as P


PASSES = 2
ITERS = 2


diffusion = 0.25


def padded(value, sides, width):
    for axis, dim in sides:
        devices, length = (lax.axis_size(axis), value.shape[dim])
        up = [(i, (i + 1) % devices) for i in range(devices - 1)]
        down = [(j, i) for i, j in up]
        last = lax.slice_in_dim(value, length - width, length, axis=dim)
        leading = lax.slice_in_dim(value, 0, width, axis=dim)
        before = lax.ppermute(last, axis, up)
        after = lax.ppermute(leading, axis, down)
        value = jnp.concatenate([before, value, after], axis=dim)
    return value


def smooth(field):
    for _ in range(PASSES):
        extended = padded(field, (("grid", 2),), 1)
        centre = extended[:, :, 1:-1]
        field = centre + diffusion * (extended[:, :, :-2] + extended[:, :, 2:] - 2.0 * centre)
    for _ in range(PASSES):
        field = field + diffusion * (jnp.roll(field, 1, 3) + jnp.roll(field, -1, 3) - 2.0 * field)
    return field


def member_total(product):
    summed = jnp.sum(product, axis=0)
    return summed


def norm_of(residual):
    return lax.psum(jnp.sum(residual * residual), ("grid", "mem"))


def local(members, innovation, observed_count, obs_precision):
    mem_index = lax.axis_index("mem")
    level_share = members.shape[1] // lax.axis_size("mem")
    perturbed = lax.all_to_all(members, "mem", split_axis=1, concat_axis=0, tiled=True)
    precision = lax.dynamic_slice_in_dim(obs_precision, mem_index * level_share, level_share, 0)
    local_innovation = lax.dynamic_slice_in_dim(innovation, mem_index * level_share, level_share, 0)
    weight = observed_count.astype(jnp.float32)[None] * precision[:, None, None]
    gradient = smooth(perturbed * (weight * local_innovation)[None])
    carried = jnp.zeros_like(gradient)
    residual = gradient
    direction = residual
    norm_now = norm_of(residual)
    for iteration in range(ITERS):
        smoothed = smooth(direction)
        total = member_total(perturbed * smoothed)
        back = smooth(perturbed * (weight * total)[None])
        image, smoothed = (direction + back, smoothed)
        step_size = norm_now / lax.psum(jnp.sum(direction * image), ("grid", "mem"))
        carried = carried + step_size * smoothed
        residual = residual - step_size * image
        if iteration + 1 < ITERS:
            norm_next = norm_of(residual)
            direction = residual + norm_next / norm_now * direction
            norm_now = norm_next
    increment = member_total(perturbed * carried)
    whole = lax.all_gather(increment, "mem", axis=0, tiled=True)
    recentred = (members.astype(jnp.float32) + whole[None]).astype(jnp.bfloat16)
    return (recentred, increment)


def smooth_rows(field):
    nlat = field.shape[-2]
    row = lax.broadcasted_iota(jnp.int32, (nlat, 1), 0)
    centre = jnp.where((row == 0) | (row == nlat - 1), 0.3125, 0.375)
    wide = jnp.pad(field, [(0, 0)] * (field.ndim - 2) + [(2, 2), (0, 0)])
    near = lax.slice_in_dim(wide, 1, nlat + 1, axis=-2) + lax.slice_in_dim(wide, 3, nlat + 3, axis=-2)
    far = lax.slice_in_dim(wide, 0, nlat, axis=-2) + lax.slice_in_dim(wide, 4, nlat + 4, axis=-2)
    field = centre * field + 0.25 * near + 0.0625 * far
    nlon = field.shape[-1]
    wide = jnp.concatenate([field[..., nlon - 2 :], field, field[..., :2]], axis=-1)
    near = wide[..., 1 : nlon + 1] + wide[..., 3 : nlon + 3]
    far = wide[..., :nlon] + wide[..., 4 : nlon + 4]
    return 0.375 * field + 0.25 * near + 0.0625 * far


def exchange(values, rows_for):
    devices = lax.axis_size("grid") * lax.axis_size("mem")
    nlon = rows_for.shape[-1]
    lanes = [jnp.sum(v.reshape(-1, 128), axis=0) for v in values]
    lanes.append(jnp.zeros((nlon - 128 * len(values),), jnp.float32))
    head = jnp.broadcast_to(jnp.concatenate(lanes), (devices, 1, nlon))
    parcel = jnp.concatenate([head, rows_for], axis=1)
    got = lax.all_to_all(parcel, ("grid", "mem"), 0, 0, tiled=True)
    lanes = jnp.sum(got[:, 0].reshape(devices, nlon // 128, 128), axis=0)
    sums = jnp.dot(lanes, jnp.ones((128, 128), jnp.float32), precision=lax.Precision.HIGHEST)
    return [jnp.tile(sums[i : i + 1], (1, nlon // 128)) for i in range(len(values))], got[:, 1:]


def mem_total(part):
    mem_size = lax.axis_size("mem")
    got = lax.all_to_all(jnp.broadcast_to(part, (mem_size,) + part.shape), "mem", 0, 0, tiled=True)
    return jnp.sum(got, axis=0)


def local_by_level(*args):
    return level_body(*args)


def level_body(members, innovation, observed_count, obs_precision):
    grid_size = lax.axis_size("grid")
    mem_size = lax.axis_size("mem")
    count, levels, rows, nlon = members.shape
    copies = grid_size // levels
    nlat = rows * grid_size
    grid_index = lax.axis_index("grid")
    mem_index = lax.axis_index("mem")
    level = grid_index // copies

    counts = jnp.broadcast_to(observed_count.astype(jnp.bfloat16), (1, levels, rows, nlon))
    high = lax.reduce_precision(innovation, exponent_bits=8, mantissa_bits=7)
    rest = innovation - high
    middle = lax.reduce_precision(rest, exponent_bits=8, mantissa_bits=7)
    low = rest - middle
    parts = jnp.stack([high, middle, low]).astype(jnp.bfloat16)
    packed = jnp.repeat(jnp.concatenate([members, counts, parts], axis=0), copies, axis=1)
    got = lax.all_to_all(packed, "grid", 1, 2, tiled=True)[:, 0]
    split = got[count + 1 :].astype(jnp.float32)
    innov = (split[0] + split[1]) + split[2]
    precision = lax.dynamic_index_in_dim(obs_precision, level, 0, keepdims=False)
    weight = got[count].astype(jnp.float32) * precision
    widened = got[:count].astype(jnp.float32)

    span = nlat // copies
    own = (lax.broadcasted_iota(jnp.int32, (nlat, nlon), 0) // span) == grid_index % copies
    first = mem_index == 0

    def squares(field):
        return jnp.sum(jnp.where(own[None], field * field, 0.0), axis=(0, 1))

    def weighted(total):
        return jnp.where(first, jnp.sum(jnp.where(own, weight * total * total, 0.0), axis=0), 0.0)

    def by_target(field):
        return jnp.repeat(field.reshape(grid_size, rows, nlon), mem_size, axis=0)

    residual = smooth_rows(widened * (weight * innov)[None])
    total1 = mem_total(jnp.sum(widened * smooth_rows(residual), axis=0))
    image = residual + smooth_rows(widened * (weight * total1)[None])
    image_part = jnp.sum(widened * smooth_rows(image), axis=0)

    if copies > 1:
        rows_for = jnp.where(grid_index % copies == 0, by_target(total1), by_target(image_part))
    else:
        rows_for = jnp.concatenate([by_target(total1), by_target(image_part)], axis=1)
    norm_part = squares(lax.optimization_barrier(residual))
    sums1, got1 = exchange([norm_part, weighted(total1)], rows_for)
    norm_now = sums1[0]
    curvature1 = sums1[1]
    step1 = norm_now / (norm_now + curvature1)
    if copies > 1:
        by_source = got1.reshape(levels, copies, mem_size, rows, nlon)
        total1_rows = by_source[:, 0, 0]
        image_rows = jnp.sum(by_source[:, 1], axis=1)
    else:
        by_source = got1.reshape(levels, mem_size, 2 * rows, nlon)
        total1_rows = by_source[:, 0, :rows]
        image_rows = jnp.sum(by_source[:, :, rows:], axis=1)

    residual_next = residual - step1 * image
    weight_rows = observed_count.astype(jnp.float32)[None] * obs_precision[:, None, None]
    moved_rows = total1_rows - step1 * image_rows
    sums, _ = exchange(
        [
            squares(residual_next),
            jnp.sum(jnp.where(own[None], residual_next * residual, 0.0), axis=(0, 1)),
            jnp.where(first, jnp.sum(weight_rows * moved_rows * moved_rows, axis=(0, 1)), 0.0),
            jnp.where(first, jnp.sum(weight_rows * moved_rows * total1_rows, axis=(0, 1)), 0.0),
        ],
        jnp.zeros((grid_size * mem_size, 0, nlon), jnp.float32),
    )
    norm_next = sums[0]
    beta = norm_next / norm_now
    direction_sq = norm_next + 2.0 * beta * sums[1] + beta * beta * norm_now
    curvature2 = sums[2] + 2.0 * beta * sums[3] + beta * beta * curvature1
    step2 = norm_next / (direction_sq + curvature2)
    total2_rows = moved_rows + beta * total1_rows
    whole = step1 * total1_rows + step2 * total2_rows

    share = levels // mem_size
    mine_out = lax.dynamic_slice_in_dim(whole, mem_index * share, share, 0)
    recentred = (members.astype(jnp.float32) + whole[None]).astype(jnp.bfloat16)
    return (recentred, mine_out)


def solution(mesh):
    placed = (P("mem", None, "grid", None), P(None, "grid", None), P("grid", None), P())
    grid_size, mem_size = mesh.shape["grid"], mesh.shape["mem"]
    body = local

    def chosen(members, innovation, observed_count, obs_precision):
        levels = members.shape[1]
        fits = grid_size % levels == 0 and grid_size // levels <= 2 and levels % mem_size == 0 and ITERS == 2
        pick = local_by_level if fits else body
        return jax.shard_map(
            pick,
            mesh=mesh,
            in_specs=placed,
            out_specs=(P("mem", None, "grid", None), P("mem", "grid", None)),
            check_vma=False,
        )(members, innovation, observed_count, obs_precision)

    return chosen
```

```python
import jax
import jax.numpy as jnp
from jax import lax
from jax.sharding import PartitionSpec as P

PASSES = 2
ITERS = 2


diffusion = 0.25


def padded(value, sides, width):
    for axis, dim in sides:
        devices, length = (lax.axis_size(axis), value.shape[dim])
        up = [(i, (i + 1) % devices) for i in range(devices - 1)]
        down = [(j, i) for i, j in up]
        last = lax.slice_in_dim(value, length - width, length, axis=dim)
        leading = lax.slice_in_dim(value, 0, width, axis=dim)
        before = lax.ppermute(last, axis, up)
        after = lax.ppermute(leading, axis, down)
        value = jnp.concatenate([before, value, after], axis=dim)
    return value


def smooth(field):
    for sweep_index in range(PASSES):
        extended = padded(field, (("grid", 2),), 1)
        centre = extended[:, :, 1:-1]
        field = centre + diffusion * (extended[:, :, :-2] + extended[:, :, 2:] - 2.0 * centre)
    for sweep_index in range(PASSES):
        field = field + diffusion * (jnp.roll(field, 1, 3) + jnp.roll(field, -1, 3) - 2.0 * field)
    return field


def member_total(product):
    summed = jnp.sum(product, axis=0)
    return summed


def norm_of(residual):
    return lax.psum(jnp.sum(residual * residual), ("grid", "mem"))


def local(members, innovation, observed_count, obs_precision):
    mem_index = lax.axis_index("mem")
    level_share = members.shape[1] // lax.axis_size("mem")
    perturbed = lax.all_to_all(members, "mem", split_axis=1, concat_axis=0, tiled=True)
    precision = lax.dynamic_slice_in_dim(obs_precision, mem_index * level_share, level_share, 0)
    local_innovation = lax.dynamic_slice_in_dim(innovation, mem_index * level_share, level_share, 0)
    weight = observed_count.astype(jnp.float32)[None] * precision[:, None, None]
    gradient = smooth(perturbed * (weight * local_innovation)[None])
    carried = jnp.zeros_like(gradient)
    residual = gradient
    direction = residual
    norm_now = norm_of(residual)
    for iteration in range(ITERS):
        smoothed = smooth(direction)
        total = member_total(perturbed * smoothed)
        back = smooth(perturbed * (weight * total)[None])
        image, smoothed = (direction + back, smoothed)
        step_size = norm_now / lax.psum(jnp.sum(direction * image), ("grid", "mem"))
        carried = carried + step_size * smoothed
        residual = residual - step_size * image
        if iteration + 1 < ITERS:
            norm_next = norm_of(residual)
            direction = residual + norm_next / norm_now * direction
            norm_now = norm_next
    increment = member_total(perturbed * carried)
    whole = lax.all_gather(increment, "mem", axis=0, tiled=True)
    recentred = (members.astype(jnp.float32) + whole[None]).astype(jnp.bfloat16)
    return (recentred, increment)


def smooth_rows(field):
    nlat = field.shape[-2]
    row = lax.broadcasted_iota(jnp.int32, (nlat, 1), 0)
    centre = jnp.where((row == 0) | (row == nlat - 1), 0.3125, 0.375)
    wide = jnp.pad(field, [(0, 0)] * (field.ndim - 2) + [(2, 2), (0, 0)])
    near = lax.slice_in_dim(wide, 1, nlat + 1, axis=-2) + lax.slice_in_dim(wide, 3, nlat + 3, axis=-2)
    far = lax.slice_in_dim(wide, 0, nlat, axis=-2) + lax.slice_in_dim(wide, 4, nlat + 4, axis=-2)
    field = centre * field + 0.25 * near + 0.0625 * far
    nlon = field.shape[-1]
    wide = jnp.concatenate([field[..., nlon - 2 :], field, field[..., :2]], axis=-1)
    near = wide[..., 1 : nlon + 1] + wide[..., 3 : nlon + 3]
    far = wide[..., :nlon] + wide[..., 4 : nlon + 4]
    return 0.375 * field + 0.25 * near + 0.0625 * far


def exchange(values, rows_for):
    devices = lax.axis_size("grid") * lax.axis_size("mem")
    nlon = rows_for.shape[-1]
    lanes = [jnp.sum(v.reshape(-1, 128), axis=0) for v in values]
    lanes.append(jnp.zeros((nlon - 128 * len(values),), jnp.float32))
    head = jnp.broadcast_to(jnp.concatenate(lanes), (devices, 1, nlon))
    parcel = jnp.concatenate([head, rows_for], axis=1)
    got = lax.all_to_all(parcel, ("grid", "mem"), 0, 0, tiled=True)
    lanes = jnp.sum(got[:, 0].reshape(devices, nlon // 128, 128), axis=0)
    sums = jnp.dot(lanes, jnp.ones((128, 128), jnp.float32), precision=lax.Precision.HIGHEST)
    return [jnp.tile(sums[i : i + 1], (1, nlon // 128)) for i in range(len(values))], got[:, 1:]


def mem_total(part):
    mem_size = lax.axis_size("mem")
    got = lax.all_to_all(jnp.broadcast_to(part, (mem_size,) + part.shape), "mem", 0, 0, tiled=True)
    return jnp.sum(got, axis=0)


def local_by_level(members, innovation, observed_count, obs_precision):
    grid_size = lax.axis_size("grid")
    mem_size = lax.axis_size("mem")
    count, levels, rows, nlon = members.shape
    copies = grid_size // levels
    nlat = rows * grid_size
    grid_index = lax.axis_index("grid")
    mem_index = lax.axis_index("mem")
    level = grid_index // copies

    counts = jnp.broadcast_to(observed_count.astype(jnp.bfloat16), (1, levels, rows, nlon))
    high = lax.reduce_precision(innovation, exponent_bits=8, mantissa_bits=7)
    rest = innovation - high
    middle = lax.reduce_precision(rest, exponent_bits=8, mantissa_bits=7)
    low = rest - middle
    parts = jnp.stack([high, middle, low]).astype(jnp.bfloat16)
    packed = jnp.repeat(jnp.concatenate([members, counts, parts], axis=0), copies, axis=1)
    got = lax.all_to_all(packed, "grid", 1, 2, tiled=True)[:, 0]
    split = got[count + 1 :].astype(jnp.float32)
    innov = (split[0] + split[1]) + split[2]
    precision = lax.dynamic_index_in_dim(obs_precision, level, 0, keepdims=False)
    weight = got[count].astype(jnp.float32) * precision
    widened = got[:count].astype(jnp.float32)

    span = nlat // copies
    own = (lax.broadcasted_iota(jnp.int32, (nlat, nlon), 0) // span) == grid_index % copies
    first = mem_index == 0

    def squares(field):
        return jnp.sum(jnp.where(own[None], field * field, 0.0), axis=(0, 1))

    def weighted(total):
        return jnp.where(first, jnp.sum(jnp.where(own, weight * total * total, 0.0), axis=0), 0.0)

    def by_target(field):
        return jnp.repeat(field.reshape(grid_size, rows, nlon), mem_size, axis=0)

    residual = smooth_rows(widened * (weight * innov)[None])
    total1 = mem_total(jnp.sum(widened * smooth_rows(residual), axis=0))
    image = residual + smooth_rows(widened * (weight * total1)[None])
    image_part = jnp.sum(widened * smooth_rows(image), axis=0)

    if copies > 1:
        rows_for = jnp.where(grid_index % copies == 0, by_target(total1), by_target(image_part))
    else:
        rows_for = jnp.concatenate([by_target(total1), by_target(image_part)], axis=1)
    sums1, got1 = exchange([squares(residual), weighted(total1)], rows_for)
    norm_now = sums1[0]
    curvature1 = sums1[1]
    step1 = norm_now / (norm_now + curvature1)
    if copies > 1:
        by_source = got1.reshape(levels, copies, mem_size, rows, nlon)
        total1_rows = by_source[:, 0, 0]
        image_rows = jnp.sum(by_source[:, 1], axis=1)
    else:
        by_source = got1.reshape(levels, mem_size, 2 * rows, nlon)
        total1_rows = by_source[:, 0, :rows]
        image_rows = jnp.sum(by_source[:, :, rows:], axis=1)

    residual_next = residual - step1 * image
    weight_rows = observed_count.astype(jnp.float32)[None] * obs_precision[:, None, None]
    moved_rows = total1_rows - step1 * image_rows
    sums, _ = exchange(
        [
            squares(residual_next),
            jnp.sum(jnp.where(own[None], residual_next * residual, 0.0), axis=(0, 1)),
            jnp.where(first, jnp.sum(weight_rows * moved_rows * moved_rows, axis=(0, 1)), 0.0),
            jnp.where(first, jnp.sum(weight_rows * moved_rows * total1_rows, axis=(0, 1)), 0.0),
        ],
        jnp.zeros((grid_size * mem_size, 0, nlon), jnp.float32),
    )
    norm_next = sums[0]
    beta = norm_next / norm_now
    direction_sq = norm_next + 2.0 * beta * sums[1] + beta * beta * norm_now
    curvature2 = sums[2] + 2.0 * beta * sums[3] + beta * beta * curvature1
    step2 = norm_next / (direction_sq + curvature2)
    total2_rows = moved_rows + beta * total1_rows
    whole = step1 * total1_rows + step2 * total2_rows

    share = levels // mem_size
    if share == 1:
        pick = lax.broadcasted_iota(jnp.int32, (levels, 1, 1), 0) == mem_index
        mine_out = jnp.sum(jnp.where(pick, whole, 0.0), axis=0, keepdims=True)
    else:
        mine_out = lax.dynamic_slice_in_dim(whole, mem_index * share, share, 0)
    recentred = (members.astype(jnp.float32) + whole[None]).astype(jnp.bfloat16)
    return (recentred, mine_out)


def solution(mesh):
    placed = (P("mem", None, "grid", None), P(None, "grid", None), P("grid", None), P())
    grid_size, mem_size = mesh.shape["grid"], mesh.shape["mem"]
    body = local

    def chosen(members, innovation, observed_count, obs_precision):
        levels = members.shape[1]
        fits = grid_size % levels == 0 and grid_size // levels <= 2 and levels % mem_size == 0 and ITERS == 2
        pick = local_by_level if fits else body
        return jax.shard_map(
            pick,
            mesh=mesh,
            in_specs=placed,
            out_specs=(P("mem", None, "grid", None), P("mem", "grid", None)),
            check_vma=False,
        )(members, innovation, observed_count, obs_precision)

    return chosen
```

```python
import jax
import jax.numpy as jnp
from jax import lax
from jax.sharding import PartitionSpec as P

PASSES = 2
ITERS = 2


diffusion = 0.25


def padded(value, sides, width):
    for axis, dim in sides:
        devices, length = (lax.axis_size(axis), value.shape[dim])
        up = [(i, (i + 1) % devices) for i in range(devices - 1)]
        down = [(j, i) for i, j in up]
        last = lax.slice_in_dim(value, length - width, length, axis=dim)
        leading = lax.slice_in_dim(value, 0, width, axis=dim)
        before = lax.ppermute(last, axis, up)
        after = lax.ppermute(leading, axis, down)
        value = jnp.concatenate([before, value, after], axis=dim)
    return value


def smooth(field):
    for sweep_index in range(PASSES):
        extended = padded(field, (("grid", 2),), 1)
        centre = extended[:, :, 1:-1]
        field = centre + diffusion * (extended[:, :, :-2] + extended[:, :, 2:] - 2.0 * centre)
    for sweep_index in range(PASSES):
        field = field + diffusion * (jnp.roll(field, 1, 3) + jnp.roll(field, -1, 3) - 2.0 * field)
    return field


def member_total(product):
    summed = jnp.sum(product, axis=0)
    return summed


def norm_of(residual):
    return lax.psum(jnp.sum(residual * residual), ("grid", "mem"))


def local(members, innovation, observed_count, obs_precision):
    mem_index = lax.axis_index("mem")
    level_share = members.shape[1] // lax.axis_size("mem")
    perturbed = lax.all_to_all(members, "mem", split_axis=1, concat_axis=0, tiled=True)
    precision = lax.dynamic_slice_in_dim(obs_precision, mem_index * level_share, level_share, 0)
    local_innovation = lax.dynamic_slice_in_dim(innovation, mem_index * level_share, level_share, 0)
    weight = observed_count.astype(jnp.float32)[None] * precision[:, None, None]
    gradient = smooth(perturbed * (weight * local_innovation)[None])
    carried = jnp.zeros_like(gradient)
    residual = gradient
    direction = residual
    norm_now = norm_of(residual)
    for iteration in range(ITERS):
        smoothed = smooth(direction)
        total = member_total(perturbed * smoothed)
        back = smooth(perturbed * (weight * total)[None])
        image, smoothed = (direction + back, smoothed)
        step_size = norm_now / lax.psum(jnp.sum(direction * image), ("grid", "mem"))
        carried = carried + step_size * smoothed
        residual = residual - step_size * image
        if iteration + 1 < ITERS:
            norm_next = norm_of(residual)
            direction = residual + norm_next / norm_now * direction
            norm_now = norm_next
    increment = member_total(perturbed * carried)
    whole = lax.all_gather(increment, "mem", axis=0, tiled=True)
    recentred = (members.astype(jnp.float32) + whole[None]).astype(jnp.bfloat16)
    return (recentred, increment)


def smooth_rows(field):
    nlat = field.shape[-2]
    row = lax.broadcasted_iota(jnp.int32, (nlat, 1), 0)
    centre = jnp.where((row == 0) | (row == nlat - 1), 0.3125, 0.375)
    wide = jnp.pad(field, [(0, 0)] * (field.ndim - 2) + [(2, 2), (0, 0)])
    near = lax.slice_in_dim(wide, 1, nlat + 1, axis=-2) + lax.slice_in_dim(wide, 3, nlat + 3, axis=-2)
    far = lax.slice_in_dim(wide, 0, nlat, axis=-2) + lax.slice_in_dim(wide, 4, nlat + 4, axis=-2)
    field = centre * field + 0.25 * near + 0.0625 * far
    nlon = field.shape[-1]
    wide = jnp.concatenate([field[..., nlon - 2 :], field, field[..., :2]], axis=-1)
    near = wide[..., 1 : nlon + 1] + wide[..., 3 : nlon + 3]
    far = wide[..., :nlon] + wide[..., 4 : nlon + 4]
    return 0.375 * field + 0.25 * near + 0.0625 * far


def exchange(values, rows_for, width=128):
    devices = lax.axis_size("grid") * lax.axis_size("mem")
    nlon = rows_for.shape[-1]
    rows = rows_for.shape[1]
    lanes = [jnp.sum(v.reshape(-1, width), axis=0) for v in values]
    head = jnp.broadcast_to(jnp.concatenate(lanes), (devices, width * len(values)))
    parcel = jnp.concatenate([head, rows_for.reshape(devices, rows * nlon)], axis=1)
    got = lax.all_to_all(parcel, ("grid", "mem"), 0, 0, tiled=True)
    parts = jnp.sum(got[:, : width * len(values)].reshape(devices, len(values), width), axis=0)
    sums = jnp.dot(parts, jnp.ones((width, 128), jnp.float32), precision=lax.Precision.HIGHEST)
    received = got[:, width * len(values) :].reshape(devices, rows, nlon)
    return [jnp.tile(sums[i : i + 1], (1, nlon // 128)) for i in range(len(values))], received


def mem_total(part):
    mem_size = lax.axis_size("mem")
    got = lax.all_to_all(jnp.broadcast_to(part, (mem_size,) + part.shape), "mem", 0, 0, tiled=True)
    return jnp.sum(got, axis=0)


def local_by_level(members, innovation, observed_count, obs_precision):
    grid_size = lax.axis_size("grid")
    mem_size = lax.axis_size("mem")
    count, levels, rows, nlon = members.shape
    copies = grid_size // levels
    nlat = rows * grid_size
    grid_index = lax.axis_index("grid")
    mem_index = lax.axis_index("mem")
    level = grid_index // copies

    counts = jnp.broadcast_to(observed_count.astype(jnp.bfloat16), (1, levels, rows, nlon))
    high = lax.reduce_precision(innovation, exponent_bits=8, mantissa_bits=7)
    rest = innovation - high
    middle = lax.reduce_precision(rest, exponent_bits=8, mantissa_bits=7)
    low = rest - middle
    parts = jnp.stack([high, middle, low]).astype(jnp.bfloat16)
    packed = jnp.repeat(jnp.concatenate([members, counts, parts], axis=0), copies, axis=1)
    got = lax.all_to_all(packed, "grid", 1, 2, tiled=True)[:, 0]
    split = got[count + 1 :].astype(jnp.float32)
    innov = (split[0] + split[1]) + split[2]
    precision = lax.dynamic_index_in_dim(obs_precision, level, 0, keepdims=False)
    weight = got[count].astype(jnp.float32) * precision
    widened = got[:count].astype(jnp.float32)

    span = nlat // copies
    own = (lax.broadcasted_iota(jnp.int32, (nlat, nlon), 0) // span) == grid_index % copies
    first = mem_index == 0

    def squares(field):
        return jnp.sum(jnp.where(own[None], field * field, 0.0), axis=(0, 1))

    def weighted(total):
        return jnp.where(first, jnp.sum(jnp.where(own, weight * total * total, 0.0), axis=0), 0.0)

    def by_target(field):
        return jnp.repeat(field.reshape(grid_size, rows, nlon), mem_size, axis=0)

    residual = smooth_rows(widened * (weight * innov)[None])
    total1 = mem_total(jnp.sum(widened * smooth_rows(residual), axis=0))
    image = residual + smooth_rows(widened * (weight * total1)[None])
    image_part = jnp.sum(widened * smooth_rows(image), axis=0)

    if copies > 1:
        rows_for = jnp.where(grid_index % copies == 0, by_target(total1), by_target(image_part))
    else:
        rows_for = jnp.concatenate([by_target(total1), by_target(image_part)], axis=1)
    sums1, got1 = exchange([squares(residual), weighted(total1)], rows_for)
    norm_now = sums1[0]
    curvature1 = sums1[1]
    step1 = norm_now / (norm_now + curvature1)
    if copies > 1:
        by_source = got1.reshape(levels, copies, mem_size, rows, nlon)
        total1_rows = by_source[:, 0, 0]
        image_rows = jnp.sum(by_source[:, 1], axis=1)
    else:
        by_source = got1.reshape(levels, mem_size, 2 * rows, nlon)
        total1_rows = by_source[:, 0, :rows]
        image_rows = jnp.sum(by_source[:, :, rows:], axis=1)

    residual_next = residual - step1 * image
    weight_rows = observed_count.astype(jnp.float32)[None] * obs_precision[:, None, None]
    moved_rows = total1_rows - step1 * image_rows
    sums, _ = exchange(
        [
            squares(residual_next),
            jnp.sum(jnp.where(own[None], residual_next * residual, 0.0), axis=(0, 1)),
            jnp.where(first, jnp.sum(weight_rows * moved_rows * moved_rows, axis=(0, 1)), 0.0),
            jnp.where(first, jnp.sum(weight_rows * moved_rows * total1_rows, axis=(0, 1)), 0.0),
        ],
        jnp.zeros((grid_size * mem_size, 0, nlon), jnp.float32),
        width=32,
    )
    norm_next = sums[0]
    beta = norm_next / norm_now
    direction_sq = norm_next + 2.0 * beta * sums[1] + beta * beta * norm_now
    curvature2 = sums[2] + 2.0 * beta * sums[3] + beta * beta * curvature1
    step2 = norm_next / (direction_sq + curvature2)
    total2_rows = moved_rows + beta * total1_rows
    whole = step1 * total1_rows + step2 * total2_rows

    share = levels // mem_size
    mine_out = lax.dynamic_slice_in_dim(whole, mem_index * share, share, 0)
    recentred = (members.astype(jnp.float32) + whole[None]).astype(jnp.bfloat16)
    return (recentred, mine_out)


def solution(mesh):
    placed = (P("mem", None, "grid", None), P(None, "grid", None), P("grid", None), P())
    grid_size, mem_size = mesh.shape["grid"], mesh.shape["mem"]
    body = local

    def chosen(members, innovation, observed_count, obs_precision):
        levels = members.shape[1]
        fits = grid_size % levels == 0 and grid_size // levels <= 2 and levels % mem_size == 0 and ITERS == 2
        pick = local_by_level if fits else body
        return jax.shard_map(
            pick,
            mesh=mesh,
            in_specs=placed,
            out_specs=(P("mem", None, "grid", None), P("mem", "grid", None)),
            check_vma=False,
        )(members, innovation, observed_count, obs_precision)

    return chosen
```

```python
import jax
import jax.numpy as jnp
from jax import lax
from jax.sharding import PartitionSpec as P

PASSES = 2
ITERS = 2


diffusion = 0.25


def padded(value, sides, width):
    for axis, dim in sides:
        devices, length = (lax.axis_size(axis), value.shape[dim])
        up = [(i, (i + 1) % devices) for i in range(devices - 1)]
        down = [(j, i) for i, j in up]
        last = lax.slice_in_dim(value, length - width, length, axis=dim)
        leading = lax.slice_in_dim(value, 0, width, axis=dim)
        before = lax.ppermute(last, axis, up)
        after = lax.ppermute(leading, axis, down)
        value = jnp.concatenate([before, value, after], axis=dim)
    return value


def smooth(field):
    for sweep_index in range(PASSES):
        extended = padded(field, (("grid", 2),), 1)
        centre = extended[:, :, 1:-1]
        field = centre + diffusion * (extended[:, :, :-2] + extended[:, :, 2:] - 2.0 * centre)
    for sweep_index in range(PASSES):
        field = field + diffusion * (jnp.roll(field, 1, 3) + jnp.roll(field, -1, 3) - 2.0 * field)
    return field


def member_total(product):
    summed = jnp.sum(product, axis=0)
    return summed


def norm_of(residual):
    return lax.psum(jnp.sum(residual * residual), ("grid", "mem"))


def local(members, innovation, observed_count, obs_precision):
    mem_index = lax.axis_index("mem")
    level_share = members.shape[1] // lax.axis_size("mem")
    perturbed = lax.all_to_all(members, "mem", split_axis=1, concat_axis=0, tiled=True)
    precision = lax.dynamic_slice_in_dim(obs_precision, mem_index * level_share, level_share, 0)
    local_innovation = lax.dynamic_slice_in_dim(innovation, mem_index * level_share, level_share, 0)
    weight = observed_count.astype(jnp.float32)[None] * precision[:, None, None]
    gradient = smooth(perturbed * (weight * local_innovation)[None])
    carried = jnp.zeros_like(gradient)
    residual = gradient
    direction = residual
    norm_now = norm_of(residual)
    for iteration in range(ITERS):
        smoothed = smooth(direction)
        total = member_total(perturbed * smoothed)
        back = smooth(perturbed * (weight * total)[None])
        image, smoothed = (direction + back, smoothed)
        step_size = norm_now / lax.psum(jnp.sum(direction * image), ("grid", "mem"))
        carried = carried + step_size * smoothed
        residual = residual - step_size * image
        if iteration + 1 < ITERS:
            norm_next = norm_of(residual)
            direction = residual + norm_next / norm_now * direction
            norm_now = norm_next
    increment = member_total(perturbed * carried)
    whole = lax.all_gather(increment, "mem", axis=0, tiled=True)
    recentred = (members.astype(jnp.float32) + whole[None]).astype(jnp.bfloat16)
    return (recentred, increment)


def smooth_rows(field):
    nlat = field.shape[-2]
    row = lax.broadcasted_iota(jnp.int32, (nlat, 1), 0)
    centre = jnp.where((row == 0) | (row == nlat - 1), 0.3125, 0.375)
    wide = jnp.pad(field, [(0, 0)] * (field.ndim - 2) + [(2, 2), (0, 0)])
    near = lax.slice_in_dim(wide, 1, nlat + 1, axis=-2) + lax.slice_in_dim(wide, 3, nlat + 3, axis=-2)
    far = lax.slice_in_dim(wide, 0, nlat, axis=-2) + lax.slice_in_dim(wide, 4, nlat + 4, axis=-2)
    field = centre * field + 0.25 * near + 0.0625 * far
    nlon = field.shape[-1]
    wide = jnp.concatenate([field[..., nlon - 2 :], field, field[..., :2]], axis=-1)
    near = wide[..., 1 : nlon + 1] + wide[..., 3 : nlon + 3]
    far = wide[..., :nlon] + wide[..., 4 : nlon + 4]
    return 0.375 * field + 0.25 * near + 0.0625 * far


def exchange(values, rows_for, width=128):
    devices = lax.axis_size("grid") * lax.axis_size("mem")
    nlon = rows_for.shape[-1]
    rows = rows_for.shape[1]
    lanes = [jnp.sum(v.reshape(-1, width), axis=0) for v in values]
    head = jnp.broadcast_to(jnp.concatenate(lanes), (devices, width * len(values)))
    parcel = jnp.concatenate([head, rows_for.reshape(devices, rows * nlon)], axis=1)
    got = lax.all_to_all(parcel, ("grid", "mem"), 0, 0, tiled=True)
    parts = jnp.sum(got[:, : width * len(values)].reshape(devices, len(values), width), axis=0)
    sums = jnp.dot(parts, jnp.ones((width, 128), jnp.float32), precision=lax.Precision.HIGHEST)
    received = got[:, width * len(values) :].reshape(devices, rows, nlon)
    return [jnp.tile(sums[i : i + 1], (1, nlon // 128)) for i in range(len(values))], received


def mem_total(part):
    mem_size = lax.axis_size("mem")
    got = lax.all_to_all(jnp.broadcast_to(part, (mem_size,) + part.shape), "mem", 0, 0, tiled=True)
    return jnp.sum(got, axis=0)


def local_by_level(members, innovation, observed_count, obs_precision):
    grid_size = lax.axis_size("grid")
    mem_size = lax.axis_size("mem")
    count, levels, rows, nlon = members.shape
    copies = grid_size // levels
    nlat = rows * grid_size
    grid_index = lax.axis_index("grid")
    mem_index = lax.axis_index("mem")
    level = grid_index // copies

    counts = jnp.broadcast_to(observed_count.astype(jnp.bfloat16), (1, levels, rows, nlon))
    high = lax.reduce_precision(innovation, exponent_bits=8, mantissa_bits=7)
    rest = innovation - high
    middle = lax.reduce_precision(rest, exponent_bits=8, mantissa_bits=7)
    low = rest - middle
    parts = jnp.stack([high, middle, low]).astype(jnp.bfloat16)
    packed = jnp.repeat(jnp.concatenate([members, counts, parts], axis=0), copies, axis=1)
    got = lax.all_to_all(packed, "grid", 1, 2, tiled=True)[:, 0]
    split = got[count + 1 :].astype(jnp.float32)
    innov = (split[0] + split[1]) + split[2]
    precision = lax.dynamic_index_in_dim(obs_precision, level, 0, keepdims=False)
    weight = got[count].astype(jnp.float32) * precision
    widened = got[:count].astype(jnp.float32)

    span = nlat // copies
    own = (lax.broadcasted_iota(jnp.int32, (nlat, nlon), 0) // span) == grid_index % copies
    first = mem_index == 0

    def squares(field):
        return jnp.sum(jnp.where(own[None], field * field, 0.0), axis=(0, 1))

    def weighted(total):
        return jnp.where(first, jnp.sum(jnp.where(own, weight * total * total, 0.0), axis=0), 0.0)

    def by_target(field):
        return jnp.repeat(field.reshape(grid_size, rows, nlon), mem_size, axis=0)

    residual = smooth_rows(widened * (weight * innov)[None])
    total1 = mem_total(jnp.sum(widened * smooth_rows(residual), axis=0))
    image = residual + smooth_rows(widened * (weight * total1)[None])
    image_part = jnp.sum(widened * smooth_rows(image), axis=0)

    if copies > 1:
        rows_for = jnp.where(grid_index % copies == 0, by_target(total1), by_target(image_part))
    else:
        rows_for = jnp.concatenate([by_target(total1), by_target(image_part)], axis=1)
    sums1, got1 = exchange([squares(residual), weighted(total1)], rows_for)
    norm_now = sums1[0]
    curvature1 = sums1[1]
    step1 = norm_now / (norm_now + curvature1)
    if copies > 1:
        by_source = got1.reshape(levels, copies, mem_size, rows, nlon)
        total1_rows = by_source[:, 0, 0]
        image_rows = jnp.sum(by_source[:, 1], axis=1)
    else:
        by_source = got1.reshape(levels, mem_size, 2 * rows, nlon)
        total1_rows = by_source[:, 0, :rows]
        image_rows = jnp.sum(by_source[:, :, rows:], axis=1)

    residual_next = residual - step1 * image
    weight_rows = observed_count.astype(jnp.float32)[None] * obs_precision[:, None, None]
    moved_rows = total1_rows - step1 * image_rows
    sums, _ = exchange(
        [
            squares(residual_next),
            jnp.sum(jnp.where(own[None], residual_next * residual, 0.0), axis=(0, 1)),
            jnp.where(first, jnp.sum(weight_rows * moved_rows * moved_rows, axis=(0, 1)), 0.0),
            jnp.where(first, jnp.sum(weight_rows * moved_rows * total1_rows, axis=(0, 1)), 0.0),
        ],
        jnp.zeros((grid_size * mem_size, 0, nlon), jnp.float32),
        width=128,
    )
    norm_next = sums[0]
    beta = norm_next / norm_now
    direction_sq = norm_next + 2.0 * beta * sums[1] + beta * beta * norm_now
    curvature2 = sums[2] + 2.0 * beta * sums[3] + beta * beta * curvature1
    step2 = norm_next / (direction_sq + curvature2)
    total2_rows = moved_rows + beta * total1_rows
    whole = step1 * total1_rows + step2 * total2_rows

    share = levels // mem_size
    mine_out = lax.dynamic_slice_in_dim(whole, mem_index * share, share, 0)
    recentred = (members.astype(jnp.float32) + whole[None]).astype(jnp.bfloat16)
    return (recentred, mine_out)


def solution(mesh):
    placed = (P("mem", None, "grid", None), P(None, "grid", None), P("grid", None), P())
    grid_size, mem_size = mesh.shape["grid"], mesh.shape["mem"]
    body = local

    def chosen(members, innovation, observed_count, obs_precision):
        levels = members.shape[1]
        fits = grid_size % levels == 0 and grid_size // levels <= 2 and levels % mem_size == 0 and ITERS == 2
        pick = local_by_level if fits else body
        return jax.shard_map(
            pick,
            mesh=mesh,
            in_specs=placed,
            out_specs=(P("mem", None, "grid", None), P("mem", "grid", None)),
            check_vma=False,
        )(members, innovation, observed_count, obs_precision)

    return chosen
```

```python
import jax
import jax.numpy as jnp
from jax import lax
from jax.sharding import PartitionSpec as P


PASSES = 2
ITERS = 2


diffusion = 0.25


def padded(value, sides, width):
    for axis, dim in sides:
        devices, length = (lax.axis_size(axis), value.shape[dim])
        up = [(i, (i + 1) % devices) for i in range(devices - 1)]
        down = [(j, i) for i, j in up]
        last = lax.slice_in_dim(value, length - width, length, axis=dim)
        leading = lax.slice_in_dim(value, 0, width, axis=dim)
        before = lax.ppermute(last, axis, up)
        after = lax.ppermute(leading, axis, down)
        value = jnp.concatenate([before, value, after], axis=dim)
    return value


def smooth(field):
    for _ in range(PASSES):
        extended = padded(field, (("grid", 2),), 1)
        centre = extended[:, :, 1:-1]
        field = centre + diffusion * (extended[:, :, :-2] + extended[:, :, 2:] - 2.0 * centre)
    for _ in range(PASSES):
        field = field + diffusion * (jnp.roll(field, 1, 3) + jnp.roll(field, -1, 3) - 2.0 * field)
    return field


def member_total(product):
    summed = jnp.sum(product, axis=0)
    return summed


def norm_of(residual):
    return lax.psum(jnp.sum(residual * residual), ("grid", "mem"))


def local(members, innovation, observed_count, obs_precision):
    mem_index = lax.axis_index("mem")
    level_share = members.shape[1] // lax.axis_size("mem")
    perturbed = lax.all_to_all(members, "mem", split_axis=1, concat_axis=0, tiled=True)
    precision = lax.dynamic_slice_in_dim(obs_precision, mem_index * level_share, level_share, 0)
    local_innovation = lax.dynamic_slice_in_dim(innovation, mem_index * level_share, level_share, 0)
    weight = observed_count.astype(jnp.float32)[None] * precision[:, None, None]
    gradient = smooth(perturbed * (weight * local_innovation)[None])
    carried = jnp.zeros_like(gradient)
    residual = gradient
    direction = residual
    norm_now = norm_of(residual)
    for iteration in range(ITERS):
        smoothed = smooth(direction)
        total = member_total(perturbed * smoothed)
        back = smooth(perturbed * (weight * total)[None])
        image, smoothed = (direction + back, smoothed)
        step_size = norm_now / lax.psum(jnp.sum(direction * image), ("grid", "mem"))
        carried = carried + step_size * smoothed
        residual = residual - step_size * image
        if iteration + 1 < ITERS:
            norm_next = norm_of(residual)
            direction = residual + norm_next / norm_now * direction
            norm_now = norm_next
    increment = member_total(perturbed * carried)
    whole = lax.all_gather(increment, "mem", axis=0, tiled=True)
    recentred = (members.astype(jnp.float32) + whole[None]).astype(jnp.bfloat16)
    return (recentred, increment)


def smooth_rows(field):
    nlat = field.shape[-2]
    row = lax.broadcasted_iota(jnp.int32, (nlat, 1), 0)
    centre = jnp.where((row == 0) | (row == nlat - 1), 0.3125, 0.375)
    wide = jnp.pad(field, [(0, 0)] * (field.ndim - 2) + [(2, 2), (0, 0)])
    near = lax.slice_in_dim(wide, 1, nlat + 1, axis=-2) + lax.slice_in_dim(wide, 3, nlat + 3, axis=-2)
    far = lax.slice_in_dim(wide, 0, nlat, axis=-2) + lax.slice_in_dim(wide, 4, nlat + 4, axis=-2)
    field = centre * field + 0.25 * near + 0.0625 * far
    nlon = field.shape[-1]
    wide = jnp.concatenate([field[..., nlon - 2 :], field, field[..., :2]], axis=-1)
    near = wide[..., 1 : nlon + 1] + wide[..., 3 : nlon + 3]
    far = wide[..., :nlon] + wide[..., 4 : nlon + 4]
    return 0.375 * field + 0.25 * near + 0.0625 * far


def exchange(values, rows_for, width=128):
    devices = lax.axis_size("grid") * lax.axis_size("mem")
    nlon = rows_for.shape[-1]
    rows = rows_for.shape[1]
    lanes = [jnp.sum(v.reshape(-1, width), axis=0) for v in values]
    head = jnp.broadcast_to(jnp.concatenate(lanes), (devices, width * len(values)))
    parcel = jnp.concatenate([head, rows_for.reshape(devices, rows * nlon)], axis=1)
    got = lax.all_to_all(parcel, ("grid", "mem"), 0, 0, tiled=True)
    parts = jnp.sum(got[:, : width * len(values)].reshape(devices, len(values), width), axis=0)
    sums = jnp.dot(parts, jnp.ones((width, 128), jnp.float32), precision=lax.Precision.HIGHEST)
    received = got[:, width * len(values) :].reshape(devices, rows, nlon)
    return [jnp.tile(sums[i : i + 1], (1, nlon // 128)) for i in range(len(values))], received


def mem_total(part):
    mem_size = lax.axis_size("mem")
    got = lax.all_to_all(jnp.broadcast_to(part, (mem_size,) + part.shape), "mem", 0, 0, tiled=True)
    return jnp.sum(got, axis=0)


def local_by_level(*args):
    return level_body(*args)


def level_body(members, innovation, observed_count, obs_precision):
    grid_size = lax.axis_size("grid")
    mem_size = lax.axis_size("mem")
    count, levels, rows, nlon = members.shape
    copies = grid_size // levels
    nlat = rows * grid_size
    grid_index = lax.axis_index("grid")
    mem_index = lax.axis_index("mem")
    level = grid_index // copies

    counts = jnp.broadcast_to(observed_count.astype(jnp.bfloat16), (1, levels, rows, nlon))
    high = lax.reduce_precision(innovation, exponent_bits=8, mantissa_bits=7)
    rest = innovation - high
    middle = lax.reduce_precision(rest, exponent_bits=8, mantissa_bits=7)
    low = rest - middle
    parts = jnp.stack([high, middle, low]).astype(jnp.bfloat16)
    packed = jnp.repeat(jnp.concatenate([members, counts, parts], axis=0), copies, axis=1)
    got = lax.all_to_all(packed, "grid", 1, 2, tiled=True)[:, 0]
    split = got[count + 1 :].astype(jnp.float32)
    innov = (split[0] + split[1]) + split[2]
    precision = lax.dynamic_index_in_dim(obs_precision, level, 0, keepdims=False)
    weight = got[count].astype(jnp.float32) * precision
    widened = got[:count].astype(jnp.float32)

    span = nlat // copies
    own = (lax.broadcasted_iota(jnp.int32, (nlat, nlon), 0) // span) == grid_index % copies
    first = mem_index == 0

    def squares(field):
        return jnp.sum(jnp.where(own[None], field * field, 0.0), axis=(0, 1))

    def weighted(total):
        return jnp.where(first, jnp.sum(jnp.where(own, weight * total * total, 0.0), axis=0), 0.0)

    def by_target(field):
        return jnp.repeat(field.reshape(grid_size, rows, nlon), mem_size, axis=0)

    residual = smooth_rows(widened * (weight * innov)[None])
    total1 = mem_total(jnp.sum(widened * smooth_rows(residual), axis=0))
    image = residual + smooth_rows(widened * (weight * total1)[None])
    image_part = jnp.sum(widened * smooth_rows(image), axis=0)

    if copies > 1:
        rows_for = jnp.where(grid_index % copies == 0, by_target(total1), by_target(image_part))
    else:
        rows_for = jnp.concatenate([by_target(total1), by_target(image_part)], axis=1)
    norm_part = squares(lax.optimization_barrier(residual))
    sums1, got1 = exchange([norm_part, weighted(total1)], rows_for)
    norm_now = sums1[0]
    curvature1 = sums1[1]
    step1 = norm_now / (norm_now + curvature1)
    if copies > 1:
        by_source = got1.reshape(levels, copies, mem_size, rows, nlon)
        total1_rows = by_source[:, 0, 0]
        image_rows = jnp.sum(by_source[:, 1], axis=1)
    else:
        by_source = got1.reshape(levels, mem_size, 2 * rows, nlon)
        total1_rows = by_source[:, 0, :rows]
        image_rows = jnp.sum(by_source[:, :, rows:], axis=1)

    residual_next = residual - step1 * image
    weight_rows = observed_count.astype(jnp.float32)[None] * obs_precision[:, None, None]
    moved_rows = total1_rows - step1 * image_rows
    sums, _ = exchange(
        [
            squares(residual_next),
            jnp.sum(jnp.where(own[None], residual_next * residual, 0.0), axis=(0, 1)),
            jnp.where(first, jnp.sum(weight_rows * moved_rows * moved_rows, axis=(0, 1)), 0.0),
            jnp.where(first, jnp.sum(weight_rows * moved_rows * total1_rows, axis=(0, 1)), 0.0),
        ],
        jnp.zeros((grid_size * mem_size, 0, nlon), jnp.float32),
        width=128,
    )
    norm_next = sums[0]
    beta = norm_next / norm_now
    direction_sq = norm_next + 2.0 * beta * sums[1] + beta * beta * norm_now
    curvature2 = sums[2] + 2.0 * beta * sums[3] + beta * beta * curvature1
    step2 = norm_next / (direction_sq + curvature2)
    total2_rows = moved_rows + beta * total1_rows
    whole = step1 * total1_rows + step2 * total2_rows

    share = levels // mem_size
    if share == 1:
        pick = lax.broadcasted_iota(jnp.int32, (levels, 1, 1), 0) == mem_index
        mine_out = jnp.sum(jnp.where(pick, whole, 0.0), axis=0, keepdims=True)
    else:
        mine_out = lax.dynamic_slice_in_dim(whole, mem_index * share, share, 0)
    recentred = (members.astype(jnp.float32) + whole[None]).astype(jnp.bfloat16)
    return (recentred, mine_out)


def solution(mesh):
    placed = (P("mem", None, "grid", None), P(None, "grid", None), P("grid", None), P())
    grid_size, mem_size = mesh.shape["grid"], mesh.shape["mem"]
    body = local

    def chosen(members, innovation, observed_count, obs_precision):
        levels = members.shape[1]
        fits = grid_size % levels == 0 and grid_size // levels <= 2 and levels % mem_size == 0 and ITERS == 2
        pick = local_by_level if fits else body
        return jax.shard_map(
            pick,
            mesh=mesh,
            in_specs=placed,
            out_specs=(P("mem", None, "grid", None), P("mem", "grid", None)),
            check_vma=False,
        )(members, innovation, observed_count, obs_precision)

    return chosen
```

```python
import jax
import jax.numpy as jnp
from jax import lax
from jax.sharding import PartitionSpec as P

PASSES = 2
ITERS = 2


diffusion = 0.25


def padded(value, sides, width):
    for axis, dim in sides:
        devices, length = (lax.axis_size(axis), value.shape[dim])
        up = [(i, (i + 1) % devices) for i in range(devices - 1)]
        down = [(j, i) for i, j in up]
        last = lax.slice_in_dim(value, length - width, length, axis=dim)
        leading = lax.slice_in_dim(value, 0, width, axis=dim)
        before = lax.ppermute(last, axis, up)
        after = lax.ppermute(leading, axis, down)
        value = jnp.concatenate([before, value, after], axis=dim)
    return value


def smooth(field):
    for sweep_index in range(PASSES):
        extended = padded(field, (("grid", 2),), 1)
        centre = extended[:, :, 1:-1]
        field = centre + diffusion * (extended[:, :, :-2] + extended[:, :, 2:] - 2.0 * centre)
    for sweep_index in range(PASSES):
        field = field + diffusion * (jnp.roll(field, 1, 3) + jnp.roll(field, -1, 3) - 2.0 * field)
    return field


def member_total(product):
    summed = jnp.sum(product, axis=0)
    return summed


def norm_of(residual):
    return lax.psum(jnp.sum(residual * residual), ("grid", "mem"))


def local(members, innovation, observed_count, obs_precision):
    mem_index = lax.axis_index("mem")
    level_share = members.shape[1] // lax.axis_size("mem")
    perturbed = lax.all_to_all(members, "mem", split_axis=1, concat_axis=0, tiled=True)
    precision = lax.dynamic_slice_in_dim(obs_precision, mem_index * level_share, level_share, 0)
    local_innovation = lax.dynamic_slice_in_dim(innovation, mem_index * level_share, level_share, 0)
    weight = observed_count.astype(jnp.float32)[None] * precision[:, None, None]
    gradient = smooth(perturbed * (weight * local_innovation)[None])
    carried = jnp.zeros_like(gradient)
    residual = gradient
    direction = residual
    norm_now = norm_of(residual)
    for iteration in range(ITERS):
        smoothed = smooth(direction)
        total = member_total(perturbed * smoothed)
        back = smooth(perturbed * (weight * total)[None])
        image, smoothed = (direction + back, smoothed)
        step_size = norm_now / lax.psum(jnp.sum(direction * image), ("grid", "mem"))
        carried = carried + step_size * smoothed
        residual = residual - step_size * image
        if iteration + 1 < ITERS:
            norm_next = norm_of(residual)
            direction = residual + norm_next / norm_now * direction
            norm_now = norm_next
    increment = member_total(perturbed * carried)
    whole = lax.all_gather(increment, "mem", axis=0, tiled=True)
    recentred = (members.astype(jnp.float32) + whole[None]).astype(jnp.bfloat16)
    return (recentred, increment)


def smooth_rows(field):
    nlat = field.shape[-2]
    row = lax.broadcasted_iota(jnp.int32, (nlat, 1), 0)
    centre = jnp.where((row == 0) | (row == nlat - 1), 0.3125, 0.375)
    wide = jnp.pad(field, [(0, 0)] * (field.ndim - 2) + [(2, 2), (0, 0)])
    near = lax.slice_in_dim(wide, 1, nlat + 1, axis=-2) + lax.slice_in_dim(wide, 3, nlat + 3, axis=-2)
    far = lax.slice_in_dim(wide, 0, nlat, axis=-2) + lax.slice_in_dim(wide, 4, nlat + 4, axis=-2)
    field = centre * field + 0.25 * near + 0.0625 * far
    nlon = field.shape[-1]
    wide = jnp.concatenate([field[..., nlon - 2 :], field, field[..., :2]], axis=-1)
    near = wide[..., 1 : nlon + 1] + wide[..., 3 : nlon + 3]
    far = wide[..., :nlon] + wide[..., 4 : nlon + 4]
    return 0.375 * field + 0.25 * near + 0.0625 * far


def exchange(values, rows_for, width=128):
    devices = lax.axis_size("grid") * lax.axis_size("mem")
    nlon = rows_for.shape[-1]
    rows = rows_for.shape[1]
    lanes = [jnp.sum(v.reshape(-1, width), axis=0) for v in values]
    head = jnp.broadcast_to(jnp.concatenate(lanes), (devices, width * len(values)))
    parcel = jnp.concatenate([head, rows_for.reshape(devices, rows * nlon)], axis=1)
    got = lax.all_to_all(parcel, ("grid", "mem"), 0, 0, tiled=True)
    parts = jnp.sum(got[:, : width * len(values)].reshape(devices, len(values), width), axis=0)
    sums = jnp.dot(parts, jnp.ones((width, 128), jnp.float32), precision=lax.Precision.HIGHEST)
    received = got[:, width * len(values) :].reshape(devices, rows, nlon)
    return [jnp.tile(sums[i : i + 1], (1, nlon // 128)) for i in range(len(values))], received


def mem_total(part):
    mem_size = lax.axis_size("mem")
    got = lax.all_to_all(jnp.broadcast_to(part, (mem_size,) + part.shape), "mem", 0, 0, tiled=True)
    return jnp.sum(got, axis=0)


def local_by_level(members, innovation, observed_count, obs_precision):
    grid_size = lax.axis_size("grid")
    mem_size = lax.axis_size("mem")
    count, levels, rows, nlon = members.shape
    copies = grid_size // levels
    nlat = rows * grid_size
    grid_index = lax.axis_index("grid")
    mem_index = lax.axis_index("mem")
    level = grid_index // copies

    counts = jnp.broadcast_to(observed_count.astype(jnp.bfloat16), (1, levels, rows, nlon))
    high = lax.reduce_precision(innovation, exponent_bits=8, mantissa_bits=7)
    rest = innovation - high
    middle = lax.reduce_precision(rest, exponent_bits=8, mantissa_bits=7)
    low = rest - middle
    parts = jnp.stack([high, middle, low]).astype(jnp.bfloat16)
    packed = jnp.repeat(jnp.concatenate([members, counts, parts], axis=0), copies, axis=1)
    got = lax.all_to_all(packed, "grid", 1, 2, tiled=True)[:, 0]
    split = got[count + 1 :].astype(jnp.float32)
    innov = (split[0] + split[1]) + split[2]
    precision = lax.dynamic_index_in_dim(obs_precision, level, 0, keepdims=False)
    weight = got[count].astype(jnp.float32) * precision
    widened = lax.optimization_barrier(got[:count]).astype(jnp.float32)

    span = nlat // copies
    own = (lax.broadcasted_iota(jnp.int32, (nlat, nlon), 0) // span) == grid_index % copies
    first = mem_index == 0

    def squares(field):
        return jnp.sum(jnp.where(own[None], field * field, 0.0), axis=(0, 1))

    def weighted(total):
        return jnp.where(first, jnp.sum(jnp.where(own, weight * total * total, 0.0), axis=0), 0.0)

    def by_target(field):
        return jnp.repeat(field.reshape(grid_size, rows, nlon), mem_size, axis=0)

    residual = smooth_rows(widened * (weight * innov)[None])
    total1 = mem_total(jnp.sum(widened * smooth_rows(residual), axis=0))
    image = residual + smooth_rows(widened * (weight * total1)[None])
    image_part = jnp.sum(widened * smooth_rows(image), axis=0)

    if copies > 1:
        rows_for = jnp.where(grid_index % copies == 0, by_target(total1), by_target(image_part))
    else:
        rows_for = jnp.concatenate([by_target(total1), by_target(image_part)], axis=1)
    sums1, got1 = exchange([squares(residual), weighted(total1)], rows_for)
    norm_now = sums1[0]
    curvature1 = sums1[1]
    step1 = norm_now / (norm_now + curvature1)
    if copies > 1:
        by_source = got1.reshape(levels, copies, mem_size, rows, nlon)
        total1_rows = by_source[:, 0, 0]
        image_rows = jnp.sum(by_source[:, 1], axis=1)
    else:
        by_source = got1.reshape(levels, mem_size, 2 * rows, nlon)
        total1_rows = by_source[:, 0, :rows]
        image_rows = jnp.sum(by_source[:, :, rows:], axis=1)

    residual_next = residual - step1 * image
    weight_rows = observed_count.astype(jnp.float32)[None] * obs_precision[:, None, None]
    moved_rows = total1_rows - step1 * image_rows
    sums, _ = exchange(
        [
            squares(residual_next),
            jnp.sum(jnp.where(own[None], residual_next * residual, 0.0), axis=(0, 1)),
            jnp.where(first, jnp.sum(weight_rows * moved_rows * moved_rows, axis=(0, 1)), 0.0),
            jnp.where(first, jnp.sum(weight_rows * moved_rows * total1_rows, axis=(0, 1)), 0.0),
        ],
        jnp.zeros((grid_size * mem_size, 0, nlon), jnp.float32),
        width=128,
    )
    norm_next = sums[0]
    beta = norm_next / norm_now
    direction_sq = norm_next + 2.0 * beta * sums[1] + beta * beta * norm_now
    curvature2 = sums[2] + 2.0 * beta * sums[3] + beta * beta * curvature1
    step2 = norm_next / (direction_sq + curvature2)
    total2_rows = moved_rows + beta * total1_rows
    whole = step1 * total1_rows + step2 * total2_rows

    share = levels // mem_size
    mine_out = lax.dynamic_slice_in_dim(whole, mem_index * share, share, 0)
    recentred = (members.astype(jnp.float32) + whole[None]).astype(jnp.bfloat16)
    return (recentred, mine_out)


def solution(mesh):
    placed = (P("mem", None, "grid", None), P(None, "grid", None), P("grid", None), P())
    grid_size, mem_size = mesh.shape["grid"], mesh.shape["mem"]
    body = local

    def chosen(members, innovation, observed_count, obs_precision):
        levels = members.shape[1]
        fits = grid_size % levels == 0 and grid_size // levels <= 2 and levels % mem_size == 0 and ITERS == 2
        pick = local_by_level if fits else body
        return jax.shard_map(
            pick,
            mesh=mesh,
            in_specs=placed,
            out_specs=(P("mem", None, "grid", None), P("mem", "grid", None)),
            check_vma=False,
        )(members, innovation, observed_count, obs_precision)

    return chosen
```

```python
import jax
import jax.numpy as jnp
from jax import lax
from jax.sharding import PartitionSpec as P

PASSES = 2
ITERS = 2


diffusion = 0.25


def padded(value, sides, width):
    for axis, dim in sides:
        devices, length = (lax.axis_size(axis), value.shape[dim])
        up = [(i, (i + 1) % devices) for i in range(devices - 1)]
        down = [(j, i) for i, j in up]
        last = lax.slice_in_dim(value, length - width, length, axis=dim)
        leading = lax.slice_in_dim(value, 0, width, axis=dim)
        before = lax.ppermute(last, axis, up)
        after = lax.ppermute(leading, axis, down)
        value = jnp.concatenate([before, value, after], axis=dim)
    return value


def smooth(field):
    for sweep_index in range(PASSES):
        extended = padded(field, (("grid", 2),), 1)
        centre = extended[:, :, 1:-1]
        field = centre + diffusion * (extended[:, :, :-2] + extended[:, :, 2:] - 2.0 * centre)
    for sweep_index in range(PASSES):
        field = field + diffusion * (jnp.roll(field, 1, 3) + jnp.roll(field, -1, 3) - 2.0 * field)
    return field


def member_total(product):
    summed = jnp.sum(product, axis=0)
    return summed


def norm_of(residual):
    return lax.psum(jnp.sum(residual * residual), ("grid", "mem"))


def local(members, innovation, observed_count, obs_precision):
    mem_index = lax.axis_index("mem")
    level_share = members.shape[1] // lax.axis_size("mem")
    perturbed = lax.all_to_all(members, "mem", split_axis=1, concat_axis=0, tiled=True)
    precision = lax.dynamic_slice_in_dim(obs_precision, mem_index * level_share, level_share, 0)
    local_innovation = lax.dynamic_slice_in_dim(innovation, mem_index * level_share, level_share, 0)
    weight = observed_count.astype(jnp.float32)[None] * precision[:, None, None]
    gradient = smooth(perturbed * (weight * local_innovation)[None])
    carried = jnp.zeros_like(gradient)
    residual = gradient
    direction = residual
    norm_now = norm_of(residual)
    for iteration in range(ITERS):
        smoothed = smooth(direction)
        total = member_total(perturbed * smoothed)
        back = smooth(perturbed * (weight * total)[None])
        image, smoothed = (direction + back, smoothed)
        step_size = norm_now / lax.psum(jnp.sum(direction * image), ("grid", "mem"))
        carried = carried + step_size * smoothed
        residual = residual - step_size * image
        if iteration + 1 < ITERS:
            norm_next = norm_of(residual)
            direction = residual + norm_next / norm_now * direction
            norm_now = norm_next
    increment = member_total(perturbed * carried)
    whole = lax.all_gather(increment, "mem", axis=0, tiled=True)
    recentred = (members.astype(jnp.float32) + whole[None]).astype(jnp.bfloat16)
    return (recentred, increment)


def smooth_rows(field):
    nlat = field.shape[-2]
    row = lax.broadcasted_iota(jnp.int32, (nlat, 1), 0)
    centre = jnp.where((row == 0) | (row == nlat - 1), 0.3125, 0.375)
    wide = jnp.pad(field, [(0, 0)] * (field.ndim - 2) + [(2, 2), (0, 0)])
    near = lax.slice_in_dim(wide, 1, nlat + 1, axis=-2) + lax.slice_in_dim(wide, 3, nlat + 3, axis=-2)
    far = lax.slice_in_dim(wide, 0, nlat, axis=-2) + lax.slice_in_dim(wide, 4, nlat + 4, axis=-2)
    field = centre * field + 0.25 * near + 0.0625 * far
    nlon = field.shape[-1]
    wide = jnp.concatenate([field[..., nlon - 2 :], field, field[..., :2]], axis=-1)
    near = wide[..., 1 : nlon + 1] + wide[..., 3 : nlon + 3]
    far = wide[..., :nlon] + wide[..., 4 : nlon + 4]
    return 0.375 * field + 0.25 * near + 0.0625 * far


def exchange(values, rows_for, width=128):
    devices = lax.axis_size("grid") * lax.axis_size("mem")
    nlon = rows_for.shape[-1]
    rows = rows_for.shape[1]
    lanes = [jnp.sum(v.reshape(-1, width), axis=0) for v in values]
    head = jnp.broadcast_to(jnp.concatenate(lanes), (devices, width * len(values)))
    parcel = jnp.concatenate([head, rows_for.reshape(devices, rows * nlon)], axis=1)
    got = lax.all_to_all(parcel, ("grid", "mem"), 0, 0, tiled=True)
    parts = jnp.sum(got[:, : width * len(values)].reshape(devices, len(values), width), axis=0)
    sums = jnp.dot(parts, jnp.ones((width, 128), jnp.float32), precision=lax.Precision.HIGHEST)
    received = got[:, width * len(values) :].reshape(devices, rows, nlon)
    return [jnp.tile(sums[i : i + 1], (1, nlon // 128)) for i in range(len(values))], received


def mem_total(part):
    mem_size = lax.axis_size("mem")
    got = lax.all_to_all(jnp.broadcast_to(part, (mem_size,) + part.shape), "mem", 0, 0, tiled=True)
    return jnp.sum(got, axis=0)


def local_by_level(members, innovation, observed_count, obs_precision):
    grid_size = lax.axis_size("grid")
    mem_size = lax.axis_size("mem")
    count, levels, rows, nlon = members.shape
    copies = grid_size // levels
    nlat = rows * grid_size
    grid_index = lax.axis_index("grid")
    mem_index = lax.axis_index("mem")
    level = grid_index // copies

    counts = jnp.broadcast_to(observed_count.astype(jnp.bfloat16), (1, levels, rows, nlon))
    high = lax.reduce_precision(innovation, exponent_bits=8, mantissa_bits=7)
    rest = innovation - high
    middle = lax.reduce_precision(rest, exponent_bits=8, mantissa_bits=7)
    low = rest - middle
    parts = jnp.stack([high, middle, low]).astype(jnp.bfloat16)
    packed = jnp.repeat(jnp.concatenate([members, counts, parts], axis=0), copies, axis=1)
    got = lax.all_to_all(packed, "grid", 1, 2, tiled=True)[:, 0]
    extra = lax.optimization_barrier(got[count:]).astype(jnp.float32)
    innov = (extra[1] + extra[2]) + extra[3]
    precision = lax.dynamic_index_in_dim(obs_precision, level, 0, keepdims=False)
    weight = extra[0] * precision
    widened = lax.optimization_barrier(got[:count]).astype(jnp.float32)

    span = nlat // copies
    own = (lax.broadcasted_iota(jnp.int32, (nlat, nlon), 0) // span) == grid_index % copies
    first = mem_index == 0

    def squares(field):
        return jnp.sum(jnp.where(own[None], field * field, 0.0), axis=(0, 1))

    def weighted(total):
        return jnp.where(first, jnp.sum(jnp.where(own, weight * total * total, 0.0), axis=0), 0.0)

    def by_target(field):
        return jnp.repeat(field.reshape(grid_size, rows, nlon), mem_size, axis=0)

    residual = smooth_rows(widened * (weight * innov)[None])
    total1 = mem_total(jnp.sum(widened * smooth_rows(residual), axis=0))
    image = residual + smooth_rows(widened * (weight * total1)[None])
    image_part = jnp.sum(widened * smooth_rows(image), axis=0)

    if copies > 1:
        rows_for = jnp.where(grid_index % copies == 0, by_target(total1), by_target(image_part))
    else:
        rows_for = jnp.concatenate([by_target(total1), by_target(image_part)], axis=1)
    sums1, got1 = exchange([squares(residual), weighted(total1)], rows_for)
    norm_now = sums1[0]
    curvature1 = sums1[1]
    step1 = norm_now / (norm_now + curvature1)
    if copies > 1:
        by_source = got1.reshape(levels, copies, mem_size, rows, nlon)
        total1_rows = by_source[:, 0, 0]
        image_rows = jnp.sum(by_source[:, 1], axis=1)
    else:
        by_source = got1.reshape(levels, mem_size, 2 * rows, nlon)
        total1_rows = by_source[:, 0, :rows]
        image_rows = jnp.sum(by_source[:, :, rows:], axis=1)

    residual_next = residual - step1 * image
    weight_rows = observed_count.astype(jnp.float32)[None] * obs_precision[:, None, None]
    moved_rows = total1_rows - step1 * image_rows
    sums, _ = exchange(
        [
            squares(residual_next),
            jnp.sum(jnp.where(own[None], residual_next * residual, 0.0), axis=(0, 1)),
            jnp.where(first, jnp.sum(weight_rows * moved_rows * moved_rows, axis=(0, 1)), 0.0),
            jnp.where(first, jnp.sum(weight_rows * moved_rows * total1_rows, axis=(0, 1)), 0.0),
        ],
        jnp.zeros((grid_size * mem_size, 0, nlon), jnp.float32),
        width=128,
    )
    norm_next = sums[0]
    beta = norm_next / norm_now
    direction_sq = norm_next + 2.0 * beta * sums[1] + beta * beta * norm_now
    curvature2 = sums[2] + 2.0 * beta * sums[3] + beta * beta * curvature1
    step2 = norm_next / (direction_sq + curvature2)
    total2_rows = moved_rows + beta * total1_rows
    whole = step1 * total1_rows + step2 * total2_rows

    share = levels // mem_size
    mine_out = lax.dynamic_slice_in_dim(whole, mem_index * share, share, 0)
    recentred = (members.astype(jnp.float32) + whole[None]).astype(jnp.bfloat16)
    return (recentred, mine_out)


def solution(mesh):
    placed = (P("mem", None, "grid", None), P(None, "grid", None), P("grid", None), P())
    grid_size, mem_size = mesh.shape["grid"], mesh.shape["mem"]
    body = local

    def chosen(members, innovation, observed_count, obs_precision):
        levels = members.shape[1]
        fits = grid_size % levels == 0 and grid_size // levels <= 2 and levels % mem_size == 0 and ITERS == 2
        pick = local_by_level if fits else body
        return jax.shard_map(
            pick,
            mesh=mesh,
            in_specs=placed,
            out_specs=(P("mem", None, "grid", None), P("mem", "grid", None)),
            check_vma=False,
        )(members, innovation, observed_count, obs_precision)

    return chosen
```

```python
import jax
import jax.numpy as jnp
from jax import lax
from jax.sharding import PartitionSpec as P

PASSES = 2
ITERS = 2


diffusion = 0.25


def padded(value, sides, width):
    for axis, dim in sides:
        devices, length = (lax.axis_size(axis), value.shape[dim])
        up = [(i, (i + 1) % devices) for i in range(devices - 1)]
        down = [(j, i) for i, j in up]
        last = lax.slice_in_dim(value, length - width, length, axis=dim)
        leading = lax.slice_in_dim(value, 0, width, axis=dim)
        before = lax.ppermute(last, axis, up)
        after = lax.ppermute(leading, axis, down)
        value = jnp.concatenate([before, value, after], axis=dim)
    return value


def smooth(field):
    for sweep_index in range(PASSES):
        extended = padded(field, (("grid", 2),), 1)
        centre = extended[:, :, 1:-1]
        field = centre + diffusion * (extended[:, :, :-2] + extended[:, :, 2:] - 2.0 * centre)
    for sweep_index in range(PASSES):
        field = field + diffusion * (jnp.roll(field, 1, 3) + jnp.roll(field, -1, 3) - 2.0 * field)
    return field


def member_total(product):
    summed = jnp.sum(product, axis=0)
    return summed


def norm_of(residual):
    return lax.psum(jnp.sum(residual * residual), ("grid", "mem"))


def local(members, innovation, observed_count, obs_precision):
    mem_index = lax.axis_index("mem")
    level_share = members.shape[1] // lax.axis_size("mem")
    perturbed = lax.all_to_all(members, "mem", split_axis=1, concat_axis=0, tiled=True)
    precision = lax.dynamic_slice_in_dim(obs_precision, mem_index * level_share, level_share, 0)
    local_innovation = lax.dynamic_slice_in_dim(innovation, mem_index * level_share, level_share, 0)
    weight = observed_count.astype(jnp.float32)[None] * precision[:, None, None]
    gradient = smooth(perturbed * (weight * local_innovation)[None])
    carried = jnp.zeros_like(gradient)
    residual = gradient
    direction = residual
    norm_now = norm_of(residual)
    for iteration in range(ITERS):
        smoothed = smooth(direction)
        total = member_total(perturbed * smoothed)
        back = smooth(perturbed * (weight * total)[None])
        image, smoothed = (direction + back, smoothed)
        step_size = norm_now / lax.psum(jnp.sum(direction * image), ("grid", "mem"))
        carried = carried + step_size * smoothed
        residual = residual - step_size * image
        if iteration + 1 < ITERS:
            norm_next = norm_of(residual)
            direction = residual + norm_next / norm_now * direction
            norm_now = norm_next
    increment = member_total(perturbed * carried)
    whole = lax.all_gather(increment, "mem", axis=0, tiled=True)
    recentred = (members.astype(jnp.float32) + whole[None]).astype(jnp.bfloat16)
    return (recentred, increment)


def smooth_rows(field):
    nlat = field.shape[-2]
    row = lax.broadcasted_iota(jnp.int32, (nlat, 1), 0)
    centre = jnp.where((row == 0) | (row == nlat - 1), 0.3125, 0.375)
    wide = jnp.pad(field, [(0, 0)] * (field.ndim - 2) + [(2, 2), (0, 0)])
    near = lax.slice_in_dim(wide, 1, nlat + 1, axis=-2) + lax.slice_in_dim(wide, 3, nlat + 3, axis=-2)
    far = lax.slice_in_dim(wide, 0, nlat, axis=-2) + lax.slice_in_dim(wide, 4, nlat + 4, axis=-2)
    field = centre * field + 0.25 * near + 0.0625 * far
    nlon = field.shape[-1]
    wide = jnp.concatenate([field[..., nlon - 2 :], field, field[..., :2]], axis=-1)
    near = wide[..., 1 : nlon + 1] + wide[..., 3 : nlon + 3]
    far = wide[..., :nlon] + wide[..., 4 : nlon + 4]
    return 0.375 * field + 0.25 * near + 0.0625 * far


def exchange(values, rows_for, width=128):
    devices = lax.axis_size("grid") * lax.axis_size("mem")
    nlon = rows_for.shape[-1]
    rows = rows_for.shape[1]
    lanes = [jnp.sum(v.reshape(-1, width), axis=0) for v in values]
    head = jnp.broadcast_to(jnp.concatenate(lanes), (devices, width * len(values)))
    parcel = jnp.concatenate([head, rows_for.reshape(devices, rows * nlon)], axis=1)
    got = lax.all_to_all(parcel, ("grid", "mem"), 0, 0, tiled=True)
    parts = jnp.sum(got[:, : width * len(values)].reshape(devices, len(values), width), axis=0)
    sums = jnp.dot(parts, jnp.ones((width, 128), jnp.float32), precision=lax.Precision.HIGHEST)
    received = got[:, width * len(values) :].reshape(devices, rows, nlon)
    return [jnp.tile(sums[i : i + 1], (1, nlon // 128)) for i in range(len(values))], received


def mem_total(part):
    mem_size = lax.axis_size("mem")
    got = lax.all_to_all(jnp.broadcast_to(part, (mem_size,) + part.shape), "mem", 0, 0, tiled=True)
    return jnp.sum(got, axis=0)


def local_by_level(members, innovation, observed_count, obs_precision):
    grid_size = lax.axis_size("grid")
    mem_size = lax.axis_size("mem")
    count, levels, rows, nlon = members.shape
    copies = grid_size // levels
    nlat = rows * grid_size
    grid_index = lax.axis_index("grid")
    mem_index = lax.axis_index("mem")
    level = grid_index // copies

    counts = jnp.broadcast_to(observed_count.astype(jnp.bfloat16), (1, levels, rows, nlon))
    high = lax.reduce_precision(innovation, exponent_bits=8, mantissa_bits=7)
    rest = innovation - high
    middle = lax.reduce_precision(rest, exponent_bits=8, mantissa_bits=7)
    low = rest - middle
    parts = jnp.stack([high, middle, low]).astype(jnp.bfloat16)
    packed = jnp.repeat(jnp.concatenate([members, counts, parts], axis=0), copies, axis=1)
    got = lax.all_to_all(packed, "grid", 1, 2, tiled=True)[:, 0]
    split = got[count + 1 :].astype(jnp.float32)
    innov = (split[0] + split[1]) + split[2]
    precision = lax.dynamic_index_in_dim(obs_precision, level, 0, keepdims=False)
    weight = got[count].astype(jnp.float32) * precision
    widened = lax.optimization_barrier(got[:count]).astype(jnp.float32)

    span = nlat // copies
    own = (lax.broadcasted_iota(jnp.int32, (nlat, nlon), 0) // span) == grid_index % copies
    first = mem_index == 0

    half = grid_index % copies

    def own_rows(field):
        return lax.dynamic_slice_in_dim(field, half * span, span, axis=1)

    def squares(field):
        mine = own_rows(field)
        return jnp.sum(mine * mine, axis=(0, 1))

    def weighted(total):
        return jnp.where(first, jnp.sum(jnp.where(own, weight * total * total, 0.0), axis=0), 0.0)

    def by_target(field):
        return jnp.repeat(field.reshape(grid_size, rows, nlon), mem_size, axis=0)

    residual = smooth_rows(widened * (weight * innov)[None])
    total1 = mem_total(jnp.sum(widened * smooth_rows(residual), axis=0))
    image = residual + smooth_rows(widened * (weight * total1)[None])
    image_part = jnp.sum(widened * smooth_rows(image), axis=0)

    if copies > 1:
        rows_for = jnp.where(grid_index % copies == 0, by_target(total1), by_target(image_part))
    else:
        rows_for = jnp.concatenate([by_target(total1), by_target(image_part)], axis=1)
    sums1, got1 = exchange([squares(residual), weighted(total1)], rows_for)
    norm_now = sums1[0]
    curvature1 = sums1[1]
    step1 = norm_now / (norm_now + curvature1)
    if copies > 1:
        by_source = got1.reshape(levels, copies, mem_size, rows, nlon)
        total1_rows = by_source[:, 0, 0]
        image_rows = jnp.sum(by_source[:, 1], axis=1)
    else:
        by_source = got1.reshape(levels, mem_size, 2 * rows, nlon)
        total1_rows = by_source[:, 0, :rows]
        image_rows = jnp.sum(by_source[:, :, rows:], axis=1)

    residual_next = residual - step1 * image
    weight_rows = observed_count.astype(jnp.float32)[None] * obs_precision[:, None, None]
    moved_rows = total1_rows - step1 * image_rows
    sums, _ = exchange(
        [
            squares(residual_next),
            jnp.sum(own_rows(residual_next) * own_rows(residual), axis=(0, 1)),
            jnp.where(first, jnp.sum(weight_rows * moved_rows * moved_rows, axis=(0, 1)), 0.0),
            jnp.where(first, jnp.sum(weight_rows * moved_rows * total1_rows, axis=(0, 1)), 0.0),
        ],
        jnp.zeros((grid_size * mem_size, 0, nlon), jnp.float32),
        width=128,
    )
    norm_next = sums[0]
    beta = norm_next / norm_now
    direction_sq = norm_next + 2.0 * beta * sums[1] + beta * beta * norm_now
    curvature2 = sums[2] + 2.0 * beta * sums[3] + beta * beta * curvature1
    step2 = norm_next / (direction_sq + curvature2)
    total2_rows = moved_rows + beta * total1_rows
    whole = step1 * total1_rows + step2 * total2_rows

    share = levels // mem_size
    mine_out = lax.dynamic_slice_in_dim(whole, mem_index * share, share, 0)
    recentred = (members.astype(jnp.float32) + whole[None]).astype(jnp.bfloat16)
    return (recentred, mine_out)


def solution(mesh):
    placed = (P("mem", None, "grid", None), P(None, "grid", None), P("grid", None), P())
    grid_size, mem_size = mesh.shape["grid"], mesh.shape["mem"]
    body = local

    def chosen(members, innovation, observed_count, obs_precision):
        levels = members.shape[1]
        fits = grid_size % levels == 0 and grid_size // levels <= 2 and levels % mem_size == 0 and ITERS == 2
        pick = local_by_level if fits else body
        return jax.shard_map(
            pick,
            mesh=mesh,
            in_specs=placed,
            out_specs=(P("mem", None, "grid", None), P("mem", "grid", None)),
            check_vma=False,
        )(members, innovation, observed_count, obs_precision)

    return chosen
```

```python
import jax
import jax.numpy as jnp
from jax import lax
from jax.sharding import PartitionSpec as P

PASSES = 2
ITERS = 2


diffusion = 0.25


def padded(value, sides, width):
    for axis, dim in sides:
        devices, length = (lax.axis_size(axis), value.shape[dim])
        up = [(i, (i + 1) % devices) for i in range(devices - 1)]
        down = [(j, i) for i, j in up]
        last = lax.slice_in_dim(value, length - width, length, axis=dim)
        leading = lax.slice_in_dim(value, 0, width, axis=dim)
        before = lax.ppermute(last, axis, up)
        after = lax.ppermute(leading, axis, down)
        value = jnp.concatenate([before, value, after], axis=dim)
    return value


def smooth(field):
    for sweep_index in range(PASSES):
        extended = padded(field, (("grid", 2),), 1)
        centre = extended[:, :, 1:-1]
        field = centre + diffusion * (extended[:, :, :-2] + extended[:, :, 2:] - 2.0 * centre)
    for sweep_index in range(PASSES):
        field = field + diffusion * (jnp.roll(field, 1, 3) + jnp.roll(field, -1, 3) - 2.0 * field)
    return field


def member_total(product):
    summed = jnp.sum(product, axis=0)
    return summed


def norm_of(residual):
    return lax.psum(jnp.sum(residual * residual), ("grid", "mem"))


def local(members, innovation, observed_count, obs_precision):
    mem_index = lax.axis_index("mem")
    level_share = members.shape[1] // lax.axis_size("mem")
    perturbed = lax.all_to_all(members, "mem", split_axis=1, concat_axis=0, tiled=True)
    precision = lax.dynamic_slice_in_dim(obs_precision, mem_index * level_share, level_share, 0)
    local_innovation = lax.dynamic_slice_in_dim(innovation, mem_index * level_share, level_share, 0)
    weight = observed_count.astype(jnp.float32)[None] * precision[:, None, None]
    gradient = smooth(perturbed * (weight * local_innovation)[None])
    carried = jnp.zeros_like(gradient)
    residual = gradient
    direction = residual
    norm_now = norm_of(residual)
    for iteration in range(ITERS):
        smoothed = smooth(direction)
        total = member_total(perturbed * smoothed)
        back = smooth(perturbed * (weight * total)[None])
        image, smoothed = (direction + back, smoothed)
        step_size = norm_now / lax.psum(jnp.sum(direction * image), ("grid", "mem"))
        carried = carried + step_size * smoothed
        residual = residual - step_size * image
        if iteration + 1 < ITERS:
            norm_next = norm_of(residual)
            direction = residual + norm_next / norm_now * direction
            norm_now = norm_next
    increment = member_total(perturbed * carried)
    whole = lax.all_gather(increment, "mem", axis=0, tiled=True)
    recentred = (members.astype(jnp.float32) + whole[None]).astype(jnp.bfloat16)
    return (recentred, increment)


def smooth_rows(field):
    nlat = field.shape[-2]
    row = lax.broadcasted_iota(jnp.int32, (nlat, 1), 0)
    centre = jnp.where((row == 0) | (row == nlat - 1), 0.3125, 0.375)
    wide = jnp.pad(field, [(0, 0)] * (field.ndim - 2) + [(2, 2), (0, 0)])
    near = lax.slice_in_dim(wide, 1, nlat + 1, axis=-2) + lax.slice_in_dim(wide, 3, nlat + 3, axis=-2)
    far = lax.slice_in_dim(wide, 0, nlat, axis=-2) + lax.slice_in_dim(wide, 4, nlat + 4, axis=-2)
    field = centre * field + 0.25 * near + 0.0625 * far
    nlon = field.shape[-1]
    wide = jnp.concatenate([field[..., nlon - 2 :], field, field[..., :2]], axis=-1)
    near = wide[..., 1 : nlon + 1] + wide[..., 3 : nlon + 3]
    far = wide[..., :nlon] + wide[..., 4 : nlon + 4]
    return 0.375 * field + 0.25 * near + 0.0625 * far


def exchange(values, rows_for, width=128):
    devices = lax.axis_size("grid") * lax.axis_size("mem")
    nlon = rows_for.shape[-1]
    rows = rows_for.shape[1]
    lanes = [jnp.sum(v.reshape(-1, width), axis=0) for v in values]
    head = jnp.broadcast_to(jnp.concatenate(lanes), (devices, width * len(values)))
    parcel = jnp.concatenate([head, rows_for.reshape(devices, rows * nlon)], axis=1)
    got = lax.all_to_all(parcel, ("grid", "mem"), 0, 0, tiled=True)
    parts = jnp.sum(got[:, : width * len(values)].reshape(devices, len(values), width), axis=0)
    sums = jnp.dot(parts, jnp.ones((width, 128), jnp.float32), precision=lax.Precision.HIGHEST)
    received = got[:, width * len(values) :].reshape(devices, rows, nlon)
    return [jnp.tile(sums[i : i + 1], (1, nlon // 128)) for i in range(len(values))], received


def mem_total(part):
    mem_size = lax.axis_size("mem")
    got = lax.all_to_all(jnp.broadcast_to(part, (mem_size,) + part.shape), "mem", 0, 0, tiled=True)
    return jnp.sum(got, axis=0)


def local_by_level(members, innovation, observed_count, obs_precision):
    grid_size = lax.axis_size("grid")
    mem_size = lax.axis_size("mem")
    count, levels, rows, nlon = members.shape
    copies = grid_size // levels
    nlat = rows * grid_size
    grid_index = lax.axis_index("grid")
    mem_index = lax.axis_index("mem")
    level = grid_index // copies

    counts = jnp.broadcast_to(observed_count.astype(jnp.bfloat16), (1, levels, rows, nlon))
    high = lax.reduce_precision(innovation, exponent_bits=8, mantissa_bits=7)
    rest = innovation - high
    middle = lax.reduce_precision(rest, exponent_bits=8, mantissa_bits=7)
    low = rest - middle
    parts = jnp.stack([high, middle, low]).astype(jnp.bfloat16)
    packed = jnp.repeat(jnp.concatenate([members, counts, parts], axis=0), copies, axis=1)
    got = lax.all_to_all(packed, "grid", 1, 2, tiled=True)[:, 0]
    split = got[count + 1 :].astype(jnp.float32)
    innov = (split[0] + split[1]) + split[2]
    precision = lax.dynamic_index_in_dim(obs_precision, level, 0, keepdims=False)
    weight = got[count].astype(jnp.float32) * precision
    widened = lax.optimization_barrier(got[:count]).astype(jnp.float32)

    span = nlat // copies
    own = (lax.broadcasted_iota(jnp.int32, (nlat, nlon), 0) // span) == grid_index % copies
    first = mem_index == 0
    half = grid_index % copies

    def own_rows(field):
        return lax.dynamic_slice_in_dim(field, half * span, span, axis=1)

    def squares(field):
        mine = own_rows(field)
        return jnp.sum(mine * mine, axis=(0, 1))

    def weighted(total):
        mine = lax.dynamic_slice_in_dim(total, half * span, span, axis=0)
        scale = lax.dynamic_slice_in_dim(weight, half * span, span, axis=0)
        return jnp.where(first, jnp.sum(scale * mine * mine, axis=0), 0.0)

    def by_target(field):
        return jnp.repeat(field.reshape(grid_size, rows, nlon), mem_size, axis=0)

    residual = smooth_rows(widened * (weight * innov)[None])
    total1 = mem_total(jnp.sum(widened * smooth_rows(residual), axis=0))
    image = residual + smooth_rows(widened * (weight * total1)[None])
    image_part = jnp.sum(widened * smooth_rows(image), axis=0)

    if copies > 1:
        rows_for = jnp.where(grid_index % copies == 0, by_target(total1), by_target(image_part))
    else:
        rows_for = jnp.concatenate([by_target(total1), by_target(image_part)], axis=1)
    sums1, got1 = exchange([squares(residual), weighted(total1)], rows_for)
    norm_now = sums1[0]
    curvature1 = sums1[1]
    step1 = norm_now / (norm_now + curvature1)
    if copies > 1:
        by_source = got1.reshape(levels, copies, mem_size, rows, nlon)
        total1_rows = by_source[:, 0, 0]
        image_rows = jnp.sum(by_source[:, 1], axis=1)
    else:
        by_source = got1.reshape(levels, mem_size, 2 * rows, nlon)
        total1_rows = by_source[:, 0, :rows]
        image_rows = jnp.sum(by_source[:, :, rows:], axis=1)

    residual_next = residual - step1 * image
    weight_rows = observed_count.astype(jnp.float32)[None] * obs_precision[:, None, None]
    moved_rows = total1_rows - step1 * image_rows
    sums, _ = exchange(
        [
            squares(residual_next),
            jnp.sum(own_rows(residual_next) * own_rows(residual), axis=(0, 1)),
            jnp.where(first, jnp.sum(weight_rows * moved_rows * moved_rows, axis=(0, 1)), 0.0),
            jnp.where(first, jnp.sum(weight_rows * moved_rows * total1_rows, axis=(0, 1)), 0.0),
        ],
        jnp.zeros((grid_size * mem_size, 0, nlon), jnp.float32),
        width=128,
    )
    norm_next = sums[0]
    beta = norm_next / norm_now
    direction_sq = norm_next + 2.0 * beta * sums[1] + beta * beta * norm_now
    curvature2 = sums[2] + 2.0 * beta * sums[3] + beta * beta * curvature1
    step2 = norm_next / (direction_sq + curvature2)
    total2_rows = moved_rows + beta * total1_rows
    whole = step1 * total1_rows + step2 * total2_rows

    share = levels // mem_size
    mine_out = lax.dynamic_slice_in_dim(whole, mem_index * share, share, 0)
    recentred = (members.astype(jnp.float32) + whole[None]).astype(jnp.bfloat16)
    return (recentred, mine_out)


def solution(mesh):
    placed = (P("mem", None, "grid", None), P(None, "grid", None), P("grid", None), P())
    grid_size, mem_size = mesh.shape["grid"], mesh.shape["mem"]
    body = local

    def chosen(members, innovation, observed_count, obs_precision):
        levels = members.shape[1]
        fits = grid_size % levels == 0 and grid_size // levels <= 2 and levels % mem_size == 0 and ITERS == 2
        pick = local_by_level if fits else body
        return jax.shard_map(
            pick,
            mesh=mesh,
            in_specs=placed,
            out_specs=(P("mem", None, "grid", None), P("mem", "grid", None)),
            check_vma=False,
        )(members, innovation, observed_count, obs_precision)

    return chosen
```
